256 devices in a mesh: guide: 2 (over x_hi), req: 128 (over x_lo, y, z, core).
Axes of the slice: x: 4 (x_hi: 2, x_lo: 2; x = x_hi * 2 + x_lo), y: 4, z: 8, core: 2. Of those that a mesh axis runs over, the one named last changes fastest.
Arguments:
- hidden_in: bfloat16 [2, 3072, 2048], P('guide', 'req'), may hold values from -24 to 24
- attn_gain: float32 [2048], replicated, may hold values from 0.25 to 1.75
- w_qkv: bfloat16 [2048, 1920], P('guide'), may hold values from -0.125 to 0.125
- w_out: bfloat16 [1280, 2048], P('guide'), may hold values from -0.3125 to 0.3125
- final_gain: float32 [2048], replicated, may hold values from 0.25 to 1.75
- w_vocab: bfloat16 [2048, 32000], P(None, 'req'), may hold values from -0.125 to 0.125
- kv_pool: bfloat16 [2, 5888, 64, 640], P('guide', 'req'), may hold values from -1400 to 1400
- cache_len: int32 [2, 3072], P('guide'), may hold values from 1 to 512, as said below
- page_table: int32 [2, 3072, 8], P('guide'), may hold values from 0 to 45, as said below
- migrations: int32 [2, 128, 3], P('guide'), may hold values from 0 to 3071, as said below
Outputs:
- guided: float32 [3072, 32000], P('guide', 'req')
The draws below stay inside these ranges and needn't reach their ends.
Inputs may be any that keep to these rules, and one draw needn't show every extreme that they name: `cache_len`: cached tokens of a request of group 0 number at most 512, of group 1 at most 256; both bounds are reached in each group. `page_table`: row i lists request i's pages in order as numbers within the pool of its owner (old owner if listed, else req index i // 24); entries past its last page are 0; pages of different requests on one device differ. `migrations`: 128 rows per group, distinct requests; the new owner is request // 24; the old owner differs from it by 1 to 2 modulo 128; at most one row per pair of owners; a listed request has at most 2 pages; in each group some new owner receives, from each of its 4 nearest old owners, a request of 2 pages.
All inputs are finite; a program needn't handle non-finite values.
Results may differ from the reference program's by a relative error of at most 0.011.
The reference program's roundings to bfloat16 on the way (of `normed`, `joined`, `rounded`, `attended` and `final`) count: a program that leaves them out, or rounds other values in their place, can miss the bound.
Values may be sent and summed in bfloat16 or wider, within the bound.
No kernel may reach another device: no remote copies, remote signals or barrier semaphores. Data moves between devices by JAX's collectives and lax.ppermute only.
A program may use at most 128 MiB of HBM per device.

```python
import math
import jax
import jax.numpy as jnp
from jax import lax

D = 2048
QH = 20
KVH = 5
HD = 64
VOCAB = 32000
REQ_DEV = 24
PAGE = 64
MAXP = 8
MAXP_U = 4
MIGP = 2
HOP = 2
REQS = 3072
POOL = 46
MIGS = 128
N_REQ = 128


def draw_hidden_in(key, part):
    key_rows, key_cols, key_main = jax.random.split(key, 3)
    row_scale = jnp.exp(jax.random.uniform(key_rows, (2, REQS, 1), jnp.float32, math.log(0.3), math.log(3.0)))
    col_scale = jnp.exp(jax.random.uniform(key_cols, (1, 1, D), jnp.float32, math.log(0.5), math.log(2.0)))
    values = jax.random.truncated_normal(key_main, -4.0, 4.0, (2, REQS, D), jnp.float32) * row_scale * col_scale
    return values.astype(jnp.bfloat16)


def draw_kv_pool(key, part):
    page_total = 2 * N_REQ * POOL
    half_width = KVH * HD
    full_width = 2 * half_width
    col_scale = jnp.where(jnp.arange(full_width) < half_width, 2.0, 1.0).astype(jnp.float32)

    def one_page(number):
        page_key = jax.random.fold_in(key, number)
        key_base = jax.random.fold_in(page_key, 0)
        base = jax.random.truncated_normal(key_base, -4.0, 4.0, (PAGE, full_width), jnp.float32) * col_scale
        return base.astype(jnp.bfloat16)
    pages_all = lax.map(one_page, jnp.arange(page_total, dtype=jnp.int32))
    return pages_all.reshape(2, N_REQ * POOL, PAGE, full_width)


def group_layout(key, most_pages):
    owners = N_REQ
    per_owner = REQ_DEV
    slots = 2 * HOP
    filler = per_owner - 2 - slots
    pieces = jax.random.split(key, 9)
    orders = jax.vmap(lambda sub_key: jax.random.permutation(sub_key, per_owner))(jax.random.split(pieces[0], owners)).astype(jnp.int32)
    home = jnp.arange(owners, dtype=jnp.int32)
    busiest = jax.random.randint(pieces[1], (), 0, owners)
    long_count = jnp.where(home == busiest, 2, jax.random.randint(pieces[2], (owners,), 0, 3))
    long_pages = jax.random.randint(pieces[3], (owners, 2), max(most_pages // 4, 1), most_pages + 1)
    long_pages = long_pages.at[busiest, 0].set(most_pages)
    receiver = jax.random.randint(pieces[4], (), 0, owners)
    pair_count = owners * slots
    pair_ids = jnp.arange(pair_count, dtype=jnp.int32)
    ranking = jax.random.randint(pieces[5], (pair_count,), 0, 1 << 20) * pair_count + pair_ids
    ranking = jnp.where(pair_ids // slots == receiver, pair_ids - 2 * pair_count, ranking)
    chosen = jnp.argsort(ranking)[:MIGS].astype(jnp.int32)
    flags = jnp.zeros((pair_count,), jnp.int32).at[chosen].set(1).reshape(owners, slots)
    moved_pages = jax.random.randint(pieces[6], (owners, slots), 1, MIGP + 1)
    moved_pages = jnp.where(home[:, None] == receiver, MIGP, moved_pages).astype(jnp.int32)
    place = jnp.arange(per_owner, dtype=jnp.int32)[None, :]
    long_fill = jnp.concatenate([long_pages, jnp.ones((owners, per_owner - 2), jnp.int32)], axis=1)
    moved_fill = jnp.concatenate([jnp.ones((owners, 2), jnp.int32), moved_pages, jnp.ones((owners, filler), jnp.int32)], axis=1)
    flag_fill = jnp.concatenate([jnp.zeros((owners, 2), jnp.int32), flags, jnp.zeros((owners, filler), jnp.int32)], axis=1)
    slot_fill = jnp.concatenate([jnp.zeros((owners, 2), jnp.int32), jnp.broadcast_to(jnp.arange(slots, dtype=jnp.int32)[None, :], (owners, slots)), jnp.zeros((owners, filler), jnp.int32)], axis=1)
    is_long = place < long_count[:, None]
    pages_at = jnp.where(is_long, long_fill, jnp.where(flag_fill == 1, moved_fill, 1))
    full_at = is_long & (place == 0) & (home[:, None] == busiest) | (flag_fill == 1) & (home[:, None] == receiver)
    tails = jax.random.randint(pieces[7], (owners, per_owner), 1, PAGE + 1)
    length_at = (pages_at - 1) * PAGE + jnp.where(full_at, PAGE, tails)
    inverse = jnp.argsort(orders, axis=1).astype(jnp.int32)
    pages_req = jnp.take_along_axis(pages_at, inverse, axis=1)
    length_req = jnp.take_along_axis(length_at, inverse, axis=1)
    moved_req = jnp.take_along_axis(flag_fill, inverse, axis=1)
    slot_req = jnp.take_along_axis(slot_fill, inverse, axis=1)
    offsets = jnp.array([number - HOP if number < HOP else number - HOP + 1 for number in range(slots)], jnp.int32)
    own_count = jnp.where(moved_req == 1, 0, pages_req)
    own_base = jnp.cumsum(own_count, axis=1) - own_count
    own_total = jnp.sum(own_count, axis=1)
    carried = flags * moved_pages
    held_count = jnp.stack([carried[jnp.remainder(home + offsets[number], owners), number] for number in range(slots)], axis=1)
    held_base = own_total[:, None] + jnp.cumsum(held_count, axis=1) - held_count
    shuffles = jax.vmap(lambda sub_key: jax.random.permutation(sub_key, POOL))(jax.random.split(pieces[8], owners)).astype(jnp.int32)
    old_req = jnp.remainder(home[:, None] - offsets[slot_req], owners)
    base_page = jnp.where(moved_req == 1, held_base[old_req, slot_req], own_base)
    holder = jnp.where(moved_req == 1, old_req, home[:, None])
    column = jnp.arange(MAXP, dtype=jnp.int32)
    entry = jnp.minimum(base_page[..., None] + column, POOL - 1)
    table = shuffles[holder[..., None], entry]
    table = jnp.where(column < pages_req[..., None], table, 0).astype(jnp.int32)
    chosen_home = chosen // slots
    chosen_slot = chosen % slots
    request = chosen_home * per_owner + orders[chosen_home, 2 + chosen_slot]
    old_owner = jnp.remainder(chosen_home - offsets[chosen_slot], owners)
    listing = jnp.stack([request, old_owner, chosen_home], axis=1).astype(jnp.int32)
    return (length_req.reshape(owners * per_owner).astype(jnp.int32), table.reshape(owners * per_owner, MAXP), listing)


def both_layouts(key):
    first = group_layout(jax.random.fold_in(key, 101), MAXP)
    second = group_layout(jax.random.fold_in(key, 202), MAXP_U)
    return (first, second)


def draw_cache_len(key, part):
    first, second = both_layouts(key)
    return jnp.stack([first[0], second[0]])


def draw_page_table(key, part):
    first, second = both_layouts(key)
    return jnp.stack([first[1], second[1]])


def draw_migrations(key, part):
    first, second = both_layouts(key)
    return jnp.stack([first[2], second[2]])


def level_of(rng, extent, cuts, low, high):
    loudness, own = 1.0, jax.random.fold_in(rng, 6)
    for dim, blocks in cuts:
        draws = jnp.exp(jax.random.uniform(jax.random.fold_in(own, dim), (blocks,), jnp.float32, low / len(cuts), high / len(cuts)))
        loudness = loudness * jnp.repeat(draws, extent[dim] // blocks).reshape([-1 if axis == dim else 1 for axis in range(len(extent))])
    return loudness


def centred(own_key, shape, scale, most, cuts=(), held_as=jnp.bfloat16):
    values = jax.random.normal(own_key, shape, jnp.float32) * scale
    if len(cuts) > 0:
        values = level_of(own_key, shape, cuts, -0.22, 0.18) * values
    return jnp.clip(values, min=-most, max=most).astype(held_as)


def setup_inputs(seed: int = 0) -> dict:
    splits = jax.random.split(jax.random.key(seed), 11)
    return {
        "hidden_in": draw_hidden_in(jax.random.fold_in(splits[10], 71), 0),
        "attn_gain": jnp.clip(1.0 + 0.15 * jax.random.normal(splits[1], (D,), jnp.float32), 0.25, 1.75),
        "w_qkv": centred(splits[2], (D, (QH + 2 * KVH) * HD), D ** -0.5, 0.125, ((0, 2),)),
        "w_out": centred(splits[3], (QH * HD, D), (QH * HD // 4) ** -0.5, 0.3125, ((0, 2),)),
        "final_gain": jnp.clip(1.0 + 0.15 * jax.random.normal(splits[4], (D,), jnp.float32), 0.25, 1.75),
        "w_vocab": centred(splits[5], (D, VOCAB), D ** -0.5, 0.125, ((1, 128),)),
        "kv_pool": draw_kv_pool(jax.random.fold_in(splits[10], 71), 0),
        "cache_len": draw_cache_len(jax.random.fold_in(splits[10], 71), 0),
        "page_table": draw_page_table(jax.random.fold_in(splits[10], 71), 0),
        "migrations": draw_migrations(jax.random.fold_in(splits[10], 71), 0),
    }


epsilon = 1e-06
guidance = 3.0

def rms_scale(values, gain):
    return values * lax.rsqrt(lax.optimization_barrier(jnp.mean(values * values, axis=-1, keepdims=True)) + epsilon) * gain

def reference(hidden_in, attn_gain, w_qkv, w_out, final_gain, w_vocab, kv_pool, cache_len, page_table, migrations):
    group = QH // KVH
    query_width = QH * HD
    key_width = KVH * HD
    scaling = 1.0 / math.sqrt(HD)
    request_ids = jnp.arange(REQS, dtype=jnp.int32)
    token_ids = jnp.arange(MAXP * PAGE, dtype=jnp.int32)
    results = []
    for side in range(2):
        states_in = hidden_in[side].astype(jnp.float32)
        normed = rms_scale(states_in, attn_gain).astype(jnp.bfloat16)
        joined = jnp.dot(normed, w_qkv, preferred_element_type=jnp.float32).astype(jnp.bfloat16)
        queries = joined[:, :query_width].reshape(REQS, KVH, group, HD)
        new_keys = joined[:, query_width:query_width + key_width].reshape(REQS, KVH, HD)
        new_values = joined[:, query_width + key_width:].reshape(REQS, KVH, HD)
        moved = jnp.full((REQS,), -1, jnp.int32).at[migrations[side, :, 0]].set(migrations[side, :, 1])
        owner = jnp.where(moved >= 0, moved, request_ids // REQ_DEV).astype(jnp.int32)
        global_pages = (owner[:, None] * POOL + page_table[side]).astype(jnp.int32)
        pool = kv_pool[side]

        def one_request(items):
            query, key_new, value_new, pages, length = items
            rows_all = pool[pages].reshape(MAXP * PAGE, 2 * key_width)
            cached_keys = rows_all[:, :key_width].reshape(-1, KVH, HD).astype(jnp.float32)
            cached_values = rows_all[:, key_width:].reshape(-1, KVH, HD).astype(jnp.float32)
            query_f = query.astype(jnp.float32)
            scores = jnp.einsum('kgd,tkd->kgt', query_f, cached_keys, precision=lax.Precision.HIGHEST) * scaling
            scores = jnp.where(token_ids < length, scores, -jnp.inf)
            own_score = jnp.einsum('kgd,kd->kg', query_f, key_new.astype(jnp.float32), precision=lax.Precision.HIGHEST) * scaling
            highest = jnp.maximum(lax.optimization_barrier(jnp.max(scores, axis=-1)), own_score)
            weights = jnp.exp(scores - highest[..., None])
            own_weight = jnp.exp(own_score - highest)
            denominator = lax.optimization_barrier(jnp.sum(weights, axis=-1)) + own_weight
            rounded = lax.optimization_barrier(weights.astype(jnp.bfloat16)).astype(jnp.float32)
            own_rounded = lax.optimization_barrier(own_weight.astype(jnp.bfloat16)).astype(jnp.float32)
            summed = jnp.einsum('kgt,tkd->kgd', rounded, cached_values, precision=lax.Precision.HIGHEST)
            summed = summed + own_rounded[..., None] * value_new.astype(jnp.float32)[:, None, :]
            return (summed / denominator[..., None]).reshape(query_width)
        attended = lax.map(one_request, (queries, new_keys, new_values, global_pages, cache_len[side]))
        attended = attended.astype(jnp.bfloat16)
        state_after = states_in + jnp.dot(attended, w_out, preferred_element_type=jnp.float32)
        final = rms_scale(state_after, final_gain).astype(jnp.bfloat16)
        results.append(jnp.dot(final, w_vocab, preferred_element_type=jnp.float32))
    return results[1] + guidance * (results[0] - results[1])
```

```python
import math

import jax
import jax.numpy as jnp
from jax import lax
from jax.sharding import PartitionSpec as P

QH = 20
KVH = 5
HD = 64
MAXP = 8
MIGP = 2
HOP = 2


epsilon = 1e-06
guidance = 3.0


def from_partner(block, axis, bit):
    count = lax.axis_size(axis)
    route = []
    for low in range(count):
        high = low | 1 << bit
        if high != low and high < count:
            route += [(low, high), (high, low)]
    return lax.ppermute(block, axis, route)


def shifted(value, axis, steps):
    count = lax.axis_size(axis)
    pairs = [(source, (source + steps) % count) for source in range(count)]
    return lax.ppermute(value, axis, pairs)


def rms_scale(values, gain):
    return values * lax.rsqrt(jnp.mean(values * values, axis=-1, keepdims=True) + epsilon) * gain


def masked_scores(queries, page_rows, lengths):
    count = page_rows.shape[0]
    span = page_rows.shape[1]
    half_width = page_rows.shape[2] // 2
    key_rows = page_rows[:, :, :half_width].reshape(count, span, KVH, HD)
    value_rows = page_rows[:, :, half_width:].reshape(count, span, KVH, HD)
    scores = jnp.einsum(
        "rkgd,rskd->rkgs", queries, key_rows, preferred_element_type=jnp.float32
    ) * (1.0 / math.sqrt(HD))
    living = jnp.arange(span, dtype=jnp.int32)[None, :] < lengths[:, None]
    scores = jnp.where(living[:, None, None, :], scores, -jnp.inf)
    return (scores, value_rows)


def attend_all(queries, page_rows, lengths, own_score, value_new):
    scores, value_rows = masked_scores(queries, page_rows, lengths)
    highest = jnp.maximum(jnp.max(scores, axis=-1), own_score)
    weights = jnp.exp(scores - highest[..., None])
    own_weight = jnp.exp(own_score - highest)
    denominator = jnp.sum(weights, axis=-1) + own_weight
    weighted = jnp.einsum(
        "rkgs,rskd->rkgd",
        weights.astype(jnp.bfloat16),
        value_rows,
        preferred_element_type=jnp.float32,
    )
    own_rounded = own_weight.astype(jnp.bfloat16).astype(jnp.float32)
    weighted = weighted + own_rounded[..., None] * value_new.astype(jnp.float32)[:, :, None, :]
    return (highest, denominator, weighted)


def gather_pages(pool, tables):
    picked = pool[tables]
    return picked.reshape(tables.shape[0], tables.shape[1] * pool.shape[1], pool.shape[2])


def body(
    hidden_in,
    attn_gain,
    w_qkv,
    w_out,
    final_gain,
    w_vocab,
    kv_pool,
    cache_len,
    page_table,
    migrations,
):
    device = lax.axis_index("req")
    devices = lax.axis_size("req")
    side = lax.axis_index("guide")
    local_rows = hidden_in.shape[1]
    group = QH // KVH
    query_width = QH * HD
    key_width = KVH * HD
    scaling = 1.0 / math.sqrt(HD)
    slots = 2 * HOP
    offsets = [number - HOP if number < HOP else number - HOP + 1 for number in range(slots)]
    states_in = hidden_in[0].astype(jnp.float32)
    normed = rms_scale(states_in, attn_gain).astype(jnp.bfloat16)
    partner_normed = from_partner(normed, "guide", 0)
    both_normed = jnp.where(
        side == 0, jnp.stack([normed, partner_normed]), jnp.stack([partner_normed, normed])
    )
    inner_half = w_qkv.shape[0]
    normed_part = lax.dynamic_slice_in_dim(both_normed, side * inner_half, inner_half, 2)
    selected = normed_part
    joined = lax.psum_scatter(
        jnp.einsum("grd,df->grf", selected, w_qkv, preferred_element_type=jnp.float32),
        "guide",
        scatter_dimension=0,
        tiled=True,
    )[0].astype(jnp.bfloat16)
    queries = joined[:, :query_width].reshape(local_rows, KVH, group, HD)
    new_keys = joined[:, query_width : query_width + key_width].reshape(local_rows, KVH, HD)
    new_values = joined[:, query_width + key_width :].reshape(local_rows, KVH, HD)
    own_score = (
        jnp.einsum("rkgd,rkd->rkg", queries, new_keys, preferred_element_type=jnp.float32) * scaling
    )
    tables = page_table[0]
    lengths_all = cache_len[0]
    listing = migrations[0]
    pool = kv_pool[0]
    pool_pages = pool.shape[0]
    first_row = device * local_rows
    own_table = lax.dynamic_slice_in_dim(tables, first_row, local_rows, 0)
    own_lengths = lax.dynamic_slice_in_dim(lengths_all, first_row, local_rows, 0)
    global_ids = first_row + jnp.arange(local_rows, dtype=jnp.int32)
    matches = listing[None, :, 0] == global_ids[:, None]
    is_moved = jnp.any(matches, axis=1)
    old_owner = jnp.sum(jnp.where(matches, listing[None, :, 1], 0), axis=1)
    distance = jnp.remainder(device - old_owner, devices)
    slot_of = jnp.where(distance <= HOP, HOP + distance - 1, HOP - (devices - distance))
    arrivals = []
    for number in range(slots):
        offset = offsets[number]
        holding = (listing[:, 1] == device) & (
            listing[:, 2] == jnp.remainder(device + offset, devices)
        )
        held_request = listing[jnp.argmax(holding), 0]
        pages_sent = pool[tables[held_request, :MIGP]]
        arrivals.append(shifted(pages_sent, "req", offset))
    extended = jnp.concatenate([pool] + arrivals, axis=0)
    page_column = jnp.minimum(jnp.arange(MAXP, dtype=jnp.int32), MIGP - 1)
    moved_pages = pool_pages + slot_of[:, None] * MIGP + page_column[None, :]
    used_table = jnp.where(is_moved[:, None], moved_pages, own_table)
    tops, sums, accs = attend_all(
        queries, gather_pages(extended, used_table), own_lengths, own_score, new_values
    )
    attended = (accs / sums[..., None]).reshape(local_rows, query_width).astype(jnp.bfloat16)
    partner_attended = from_partner(attended, "guide", 0)
    both_attended = jnp.where(
        side == 0, jnp.stack([attended, partner_attended]), jnp.stack([partner_attended, attended])
    )
    head_half = w_out.shape[0]
    attended_part = lax.dynamic_slice_in_dim(both_attended, side * head_half, head_half, 2)
    selected = attended_part
    state_after = (
        states_in
        + lax.psum_scatter(
            jnp.einsum("grc,cd->grd", selected, w_out, preferred_element_type=jnp.float32).astype(
                jnp.bfloat16
            ),
            "guide",
            scatter_dimension=0,
            tiled=True,
        ).astype(jnp.float32)[0]
    )
    final = rms_scale(state_after, final_gain).astype(jnp.bfloat16)
    partner_final = from_partner(final, "guide", 0)
    cond = jnp.where(side == 0, final, partner_final).astype(jnp.float32)
    uncond = jnp.where(side == 0, partner_final, final).astype(jnp.float32)
    combined = (uncond + guidance * (cond - uncond)).astype(jnp.bfloat16)
    half_devices = devices // 2
    half_rows = local_rows // 2
    upper = device // half_devices
    kept = lax.dynamic_slice_in_dim(combined, upper * half_rows, half_rows, 0)
    sent = lax.dynamic_slice_in_dim(combined, (1 - upper) * half_rows, half_rows, 0)
    swapped = shifted(sent, "req", half_devices)
    mine = jnp.where(upper == side, kept, swapped)
    gathered = lax.all_gather(mine, "req", axis=0, tiled=False)
    gathered = gathered.reshape(2, half_devices, half_rows, gathered.shape[-1])
    logits = jnp.einsum(
        "xjkd,dv->jxkv", gathered, w_vocab, preferred_element_type=jnp.float32
    )
    return logits.reshape(half_devices * local_rows, logits.shape[-1])


def solution(mesh):
    in_specs = (
        P("guide", "req", None),
        P(),
        P("guide", None),
        P("guide", None),
        P(),
        P(None, "req"),
        P("guide", "req", None, None),
        P("guide", None),
        P("guide", None, None),
        P("guide", None, None),
    )
    out_specs = P("guide", "req")
    return jax.shard_map(body, mesh=mesh, in_specs=in_specs, out_specs=out_specs, check_vma=False)
```

```python
import math

import jax
import jax.numpy as jnp
from jax import lax
from jax.sharding import Mesh
from jax.sharding import PartitionSpec as P

QH = 20
KVH = 5
HD = 64
MAXP = 8
MIGP = 2
HOP = 2
REQ = ("x_lo", "y", "z", "core")
REQ_SPLIT = (2, 4, 8, 2)


epsilon = 1e-06
guidance = 3.0


def from_partner(block, axis, bit):
    count = lax.axis_size(axis)
    route = []
    for low in range(count):
        high = low | 1 << bit
        if high != low and high < count:
            route += [(low, high), (high, low)]
    return lax.ppermute(block, axis, route)


def shifted(value, axis, steps):
    count = lax.axis_size(axis)
    pairs = [(source, (source + steps) % count) for source in range(count)]
    return lax.ppermute(value, axis, pairs)


def rms_scale(values, gain):
    return values * lax.rsqrt(jnp.mean(values * values, axis=-1, keepdims=True) + epsilon) * gain


def masked_scores(queries, page_rows, lengths):
    count = page_rows.shape[0]
    span = page_rows.shape[1]
    half_width = page_rows.shape[2] // 2
    key_rows = page_rows[:, :, :half_width].reshape(count, span, KVH, HD)
    value_rows = page_rows[:, :, half_width:].reshape(count, span, KVH, HD)
    scores = jnp.einsum(
        "rkgd,rskd->rkgs", queries, key_rows, preferred_element_type=jnp.float32
    ) * (1.0 / math.sqrt(HD))
    living = jnp.arange(span, dtype=jnp.int32)[None, :] < lengths[:, None]
    scores = jnp.where(living[:, None, None, :], scores, -jnp.inf)
    return (scores, value_rows)


def attend_all(queries, page_rows, lengths, own_score, value_new):
    scores, value_rows = masked_scores(queries, page_rows, lengths)
    highest = jnp.maximum(jnp.max(scores, axis=-1), own_score)
    weights = jnp.exp(scores - highest[..., None])
    own_weight = jnp.exp(own_score - highest)
    denominator = jnp.sum(weights, axis=-1) + own_weight
    weighted = jnp.einsum(
        "rkgs,rskd->rkgd",
        weights.astype(jnp.bfloat16),
        value_rows,
        preferred_element_type=jnp.float32,
    )
    own_rounded = own_weight.astype(jnp.bfloat16).astype(jnp.float32)
    weighted = weighted + own_rounded[..., None] * value_new.astype(jnp.float32)[:, :, None, :]
    return (highest, denominator, weighted)


def gather_pages(pool, tables):
    picked = pool[tables]
    return picked.reshape(tables.shape[0], tables.shape[1] * pool.shape[1], pool.shape[2])


def body(
    hidden_in,
    attn_gain,
    w_qkv,
    w_out,
    final_gain,
    w_vocab,
    kv_pool,
    cache_len,
    page_table,
    migrations,
):
    device = lax.axis_index(REQ)
    devices = lax.axis_size(REQ)
    side = lax.axis_index("guide")
    local_rows = hidden_in.shape[1]
    group = QH // KVH
    query_width = QH * HD
    key_width = KVH * HD
    scaling = 1.0 / math.sqrt(HD)
    slots = 2 * HOP
    offsets = [number - HOP if number < HOP else number - HOP + 1 for number in range(slots)]
    states_in = hidden_in[0].astype(jnp.float32)
    normed = rms_scale(states_in, attn_gain).astype(jnp.bfloat16)
    partner_normed = from_partner(normed, "guide", 0)
    both_normed = jnp.where(
        side == 0, jnp.stack([normed, partner_normed]), jnp.stack([partner_normed, normed])
    )
    inner_half = w_qkv.shape[0]
    normed_part = lax.dynamic_slice_in_dim(both_normed, side * inner_half, inner_half, 2)
    selected = normed_part
    joined = lax.psum_scatter(
        jnp.einsum("grd,df->grf", selected, w_qkv, preferred_element_type=jnp.float32),
        "guide",
        scatter_dimension=0,
        tiled=True,
    )[0].astype(jnp.bfloat16)
    queries = joined[:, :query_width].reshape(local_rows, KVH, group, HD)
    new_keys = joined[:, query_width : query_width + key_width].reshape(local_rows, KVH, HD)
    new_values = joined[:, query_width + key_width :].reshape(local_rows, KVH, HD)
    own_score = (
        jnp.einsum("rkgd,rkd->rkg", queries, new_keys, preferred_element_type=jnp.float32) * scaling
    )
    tables = page_table[0]
    lengths_all = cache_len[0]
    listing = migrations[0]
    pool = kv_pool[0]
    pool_pages = pool.shape[0]
    first_row = device * local_rows
    own_table = lax.dynamic_slice_in_dim(tables, first_row, local_rows, 0)
    own_lengths = lax.dynamic_slice_in_dim(lengths_all, first_row, local_rows, 0)
    global_ids = first_row + jnp.arange(local_rows, dtype=jnp.int32)
    matches = listing[None, :, 0] == global_ids[:, None]
    is_moved = jnp.any(matches, axis=1)
    old_owner = jnp.sum(jnp.where(matches, listing[None, :, 1], 0), axis=1)
    distance = jnp.remainder(device - old_owner, devices)
    slot_of = jnp.where(distance <= HOP, HOP + distance - 1, HOP - (devices - distance))
    arrivals = []
    for number in range(slots):
        offset = offsets[number]
        holding = (listing[:, 1] == device) & (
            listing[:, 2] == jnp.remainder(device + offset, devices)
        )
        held_request = listing[jnp.argmax(holding), 0]
        pages_sent = pool[tables[held_request, :MIGP]]
        arrivals.append(shifted(pages_sent, REQ, offset))
    extended = jnp.concatenate([pool] + arrivals, axis=0)
    page_column = jnp.minimum(jnp.arange(MAXP, dtype=jnp.int32), MIGP - 1)
    moved_pages = pool_pages + slot_of[:, None] * MIGP + page_column[None, :]
    used_table = jnp.where(is_moved[:, None], moved_pages, own_table)
    tops, sums, accs = attend_all(
        queries, gather_pages(extended, used_table), own_lengths, own_score, new_values
    )
    attended = (accs / sums[..., None]).reshape(local_rows, query_width).astype(jnp.bfloat16)
    partner_attended = from_partner(attended, "guide", 0)
    both_attended = jnp.where(
        side == 0, jnp.stack([attended, partner_attended]), jnp.stack([partner_attended, attended])
    )
    head_half = w_out.shape[0]
    attended_part = lax.dynamic_slice_in_dim(both_attended, side * head_half, head_half, 2)
    selected = attended_part
    state_after = (
        states_in
        + lax.psum_scatter(
            jnp.einsum("grc,cd->grd", selected, w_out, preferred_element_type=jnp.float32).astype(
                jnp.bfloat16
            ),
            "guide",
            scatter_dimension=0,
            tiled=True,
        ).astype(jnp.float32)[0]
    )
    final = rms_scale(state_after, final_gain).astype(jnp.bfloat16)
    partner_final = from_partner(final, "guide", 0)
    cond = jnp.where(side == 0, final, partner_final).astype(jnp.float32)
    uncond = jnp.where(side == 0, partner_final, final).astype(jnp.float32)
    combined = (uncond + guidance * (cond - uncond)).astype(jnp.bfloat16)
    half_devices = devices // 2
    half_rows = local_rows // 2
    upper = device // half_devices
    kept = lax.dynamic_slice_in_dim(combined, upper * half_rows, half_rows, 0)
    sent = lax.dynamic_slice_in_dim(combined, (1 - upper) * half_rows, half_rows, 0)
    swapped = shifted(sent, REQ, half_devices)
    mine = jnp.where(upper == side, kept, swapped)
    gathered = lax.all_gather(mine, "x_lo", axis=0, tiled=False)
    gathered = lax.all_gather(gathered, "y", axis=0, tiled=False)
    gathered = lax.all_gather(gathered, "z", axis=1, tiled=False)
    gathered = lax.all_gather(gathered, "core", axis=2, tiled=False)
    logits = jnp.einsum(
        "yzcxkd,dv->yzcxkv", gathered, w_vocab, preferred_element_type=jnp.float32
    )
    return logits.reshape(half_devices * local_rows, logits.shape[-1])


def solution(mesh):
    split = Mesh(mesh.devices.reshape((mesh.devices.shape[0],) + REQ_SPLIT), ("guide",) + REQ)
    in_specs = (
        P("guide", REQ, None),
        P(),
        P("guide", None),
        P("guide", None),
        P(),
        P(None, REQ),
        P("guide", REQ, None, None),
        P("guide", None),
        P("guide", None, None),
        P("guide", None, None),
    )
    out_specs = P("guide", REQ)
    return jax.shard_map(body, mesh=split, in_specs=in_specs, out_specs=out_specs, check_vma=False)
```

```python
import math

import jax
import jax.numpy as jnp
from jax import lax
from jax.sharding import Mesh
from jax.sharding import PartitionSpec as P

QH = 20
KVH = 5
HD = 64
MAXP = 8
MIGP = 2
HOP = 2
REQ = ("x_lo", "y", "z", "core")
REQ_SPLIT = (2, 4, 8, 2)


epsilon = 1e-06
guidance = 3.0


def from_partner(block, axis, bit):
    count = lax.axis_size(axis)
    route = []
    for low in range(count):
        high = low | 1 << bit
        if high != low and high < count:
            route += [(low, high), (high, low)]
    return lax.ppermute(block, axis, route)


def shifted(value, axis, steps):
    count = lax.axis_size(axis)
    pairs = [(source, (source + steps) % count) for source in range(count)]
    return lax.ppermute(value, axis, pairs)


def rms_scale(values, gain):
    return values * lax.rsqrt(jnp.mean(values * values, axis=-1, keepdims=True) + epsilon) * gain


def masked_scores(queries, page_rows, lengths):
    count = page_rows.shape[0]
    span = page_rows.shape[1]
    half_width = page_rows.shape[2] // 2
    key_rows = page_rows[:, :, :half_width].reshape(count, span, KVH, HD)
    value_rows = page_rows[:, :, half_width:].reshape(count, span, KVH, HD)
    scores = jnp.einsum(
        "rkgd,rskd->rkgs", queries, key_rows, preferred_element_type=jnp.float32
    ) * (1.0 / math.sqrt(HD))
    living = jnp.arange(span, dtype=jnp.int32)[None, :] < lengths[:, None]
    scores = jnp.where(living[:, None, None, :], scores, -jnp.inf)
    return (scores, value_rows)


def attend_all(queries, page_rows, lengths, own_score, value_new):
    scores, value_rows = masked_scores(queries, page_rows, lengths)
    highest = jnp.maximum(jnp.max(scores, axis=-1), own_score)
    weights = jnp.exp(scores - highest[..., None])
    own_weight = jnp.exp(own_score - highest)
    denominator = jnp.sum(weights, axis=-1) + own_weight
    weighted = jnp.einsum(
        "rkgs,rskd->rkgd",
        weights.astype(jnp.bfloat16),
        value_rows,
        preferred_element_type=jnp.float32,
    )
    own_rounded = own_weight.astype(jnp.bfloat16).astype(jnp.float32)
    weighted = weighted + own_rounded[..., None] * value_new.astype(jnp.float32)[:, :, None, :]
    return (highest, denominator, weighted)


def gather_pages(pool, tables):
    picked = pool[tables]
    return picked.reshape(tables.shape[0], tables.shape[1] * pool.shape[1], pool.shape[2])


def dense_scores(queries, page_rows, counts):
    count = page_rows.shape[0] * page_rows.shape[1]
    half_width = page_rows.shape[2] // 2
    flat = page_rows.reshape(count, page_rows.shape[2])
    key_rows = flat[:, :half_width].reshape(count, KVH, HD)
    value_rows = flat[:, half_width:].reshape(count, KVH, HD)
    scores = jnp.einsum(
        "rkgd,tkd->rkgt", queries, key_rows, preferred_element_type=jnp.float32
    ) * (1.0 / math.sqrt(HD))
    scores = jnp.where(counts[:, None, None, :] > 0, scores, -jnp.inf)
    return (scores, value_rows)


def body(
    hidden_in,
    attn_gain,
    w_qkv,
    w_out,
    final_gain,
    w_vocab,
    kv_pool,
    cache_len,
    page_table,
    migrations,
):
    device = lax.axis_index(REQ)
    devices = lax.axis_size(REQ)
    side = lax.axis_index("guide")
    local_rows = hidden_in.shape[1]
    group = QH // KVH
    query_width = QH * HD
    key_width = KVH * HD
    scaling = 1.0 / math.sqrt(HD)
    slots = 2 * HOP
    offsets = [number - HOP if number < HOP else number - HOP + 1 for number in range(slots)]
    states_in = hidden_in[0].astype(jnp.float32)
    normed = rms_scale(states_in, attn_gain).astype(jnp.bfloat16)
    partner_normed = from_partner(normed, "guide", 0)
    both_normed = jnp.where(
        side == 0, jnp.stack([normed, partner_normed]), jnp.stack([partner_normed, normed])
    )
    inner_half = w_qkv.shape[0]
    normed_part = lax.dynamic_slice_in_dim(both_normed, side * inner_half, inner_half, 2)
    selected = normed_part
    joined = lax.psum_scatter(
        jnp.einsum("grd,df->grf", selected, w_qkv, preferred_element_type=jnp.float32),
        "guide",
        scatter_dimension=0,
        tiled=True,
    )[0].astype(jnp.bfloat16)
    queries = joined[:, :query_width].reshape(local_rows, KVH, group, HD)
    new_keys = joined[:, query_width : query_width + key_width].reshape(local_rows, KVH, HD)
    new_values = joined[:, query_width + key_width :].reshape(local_rows, KVH, HD)
    own_score = (
        jnp.einsum("rkgd,rkd->rkg", queries, new_keys, preferred_element_type=jnp.float32) * scaling
    )
    tables = page_table[0]
    lengths_all = cache_len[0]
    listing = migrations[0]
    pool = kv_pool[0]
    pool_pages = pool.shape[0]
    first_row = device * local_rows
    own_table = lax.dynamic_slice_in_dim(tables, first_row, local_rows, 0)
    own_lengths = lax.dynamic_slice_in_dim(lengths_all, first_row, local_rows, 0)
    global_ids = first_row + jnp.arange(local_rows, dtype=jnp.int32)
    matches = listing[None, :, 0] == global_ids[:, None]
    is_moved = jnp.any(matches, axis=1)
    old_owner = jnp.sum(jnp.where(matches, listing[None, :, 1], 0), axis=1)
    distance = jnp.remainder(device - old_owner, devices)
    slot_of = jnp.where(distance <= HOP, HOP + distance - 1, HOP - (devices - distance))
    arrivals = []
    for number in range(slots):
        offset = offsets[number]
        holding = (listing[:, 1] == device) & (
            listing[:, 2] == jnp.remainder(device + offset, devices)
        )
        held_request = listing[jnp.argmax(holding), 0]
        pages_sent = pool[tables[held_request, :MIGP]]
        arrivals.append(shifted(pages_sent, REQ, offset))
    arrived = jnp.concatenate(arrivals, axis=0)
    page_column = jnp.minimum(jnp.arange(MAXP, dtype=jnp.int32), MIGP - 1)
    moved_pages = pool_pages + slot_of[:, None] * MIGP + page_column[None, :]
    used_table = jnp.where(is_moved[:, None], moved_pages, own_table)
    page_rows = pool.shape[1]
    living = (
        jnp.arange(MAXP, dtype=jnp.int32)[:, None] * page_rows
        + jnp.arange(page_rows, dtype=jnp.int32)[None, :]
    )[None] < own_lengths[:, None, None]
    living = living.astype(jnp.float32)
    all_pages = jnp.arange(pool_pages + arrived.shape[0], dtype=jnp.int32)
    hits = (used_table[:, :, None] == all_pages[None, None, :]).astype(jnp.float32)
    counts = jnp.einsum("rsp,rsw->rpw", hits, living).reshape(local_rows, -1)
    pool_counts = counts[:, : pool_pages * page_rows]
    arrived_counts = counts[:, pool_pages * page_rows :]
    pool_scores, pool_values = dense_scores(queries, pool, pool_counts)
    arrived_scores, arrived_values = dense_scores(queries, arrived, arrived_counts)
    tops = jnp.maximum(
        jnp.maximum(jnp.max(pool_scores, axis=-1), jnp.max(arrived_scores, axis=-1)), own_score
    )
    own_weight = jnp.exp(own_score - tops)
    sums = own_weight
    accs = own_weight.astype(jnp.bfloat16).astype(jnp.float32)[..., None] * new_values.astype(
        jnp.float32
    )[:, :, None, :]
    for scores, values, count in (
        (pool_scores, pool_values, pool_counts),
        (arrived_scores, arrived_values, arrived_counts),
    ):
        weights = jnp.exp(scores - tops[..., None])
        sums = sums + jnp.sum(weights * count[:, None, None, :], axis=-1)
        rounded = weights.astype(jnp.bfloat16).astype(jnp.float32) * count[:, None, None, :]
        accs = accs + jnp.einsum(
            "rkgt,tkd->rkgd",
            rounded,
            values.astype(jnp.float32),
            precision=lax.Precision.HIGHEST,
            preferred_element_type=jnp.float32,
        )
    attended = (accs / sums[..., None]).reshape(local_rows, query_width).astype(jnp.bfloat16)
    partner_attended = from_partner(attended, "guide", 0)
    both_attended = jnp.where(
        side == 0, jnp.stack([attended, partner_attended]), jnp.stack([partner_attended, attended])
    )
    head_half = w_out.shape[0]
    attended_part = lax.dynamic_slice_in_dim(both_attended, side * head_half, head_half, 2)
    selected = attended_part
    state_after = (
        states_in
        + lax.psum_scatter(
            jnp.einsum("grc,cd->grd", selected, w_out, preferred_element_type=jnp.float32).astype(
                jnp.bfloat16
            ),
            "guide",
            scatter_dimension=0,
            tiled=True,
        ).astype(jnp.float32)[0]
    )
    final = rms_scale(state_after, final_gain).astype(jnp.bfloat16)
    partner_final = from_partner(final, "guide", 0)
    cond = jnp.where(side == 0, final, partner_final).astype(jnp.float32)
    uncond = jnp.where(side == 0, partner_final, final).astype(jnp.float32)
    combined = (uncond + guidance * (cond - uncond)).astype(jnp.bfloat16)
    half_devices = devices // 2
    half_rows = local_rows // 2
    upper = device // half_devices
    kept = lax.dynamic_slice_in_dim(combined, upper * half_rows, half_rows, 0)
    sent = lax.dynamic_slice_in_dim(combined, (1 - upper) * half_rows, half_rows, 0)
    swapped = shifted(sent, REQ, half_devices)
    mine = jnp.where(upper == side, kept, swapped)
    gathered = lax.all_gather(mine, "x_lo", axis=0, tiled=False)
    gathered = lax.all_gather(gathered, "y", axis=0, tiled=False)
    gathered = lax.all_gather(gathered, "z", axis=1, tiled=False)
    gathered = lax.all_gather(gathered, "core", axis=2, tiled=False)
    logits = jnp.einsum(
        "yzcxkd,dv->yzcxkv", gathered, w_vocab, preferred_element_type=jnp.float32
    )
    return logits.reshape(half_devices * local_rows, logits.shape[-1])


def solution(mesh):
    split = Mesh(mesh.devices.reshape((mesh.devices.shape[0],) + REQ_SPLIT), ("guide",) + REQ)
    in_specs = (
        P("guide", REQ, None),
        P(),
        P("guide", None),
        P("guide", None),
        P(),
        P(None, REQ),
        P("guide", REQ, None, None),
        P("guide", None),
        P("guide", None, None),
        P("guide", None, None),
    )
    out_specs = P("guide", REQ)
    return jax.shard_map(body, mesh=split, in_specs=in_specs, out_specs=out_specs, check_vma=False)
```

```python
import math

import jax
import jax.numpy as jnp
from jax import lax
from jax.sharding import Mesh
from jax.sharding import PartitionSpec as P

QH = 20
KVH = 5
HD = 64
MAXP = 8
MIGP = 2
HOP = 2
REQ = ("x_lo", "y", "z", "core")
REQ_SPLIT = (2, 4, 8, 2)


epsilon = 1e-06
guidance = 3.0


def from_partner(block, axis, bit):
    count = lax.axis_size(axis)
    route = []
    for low in range(count):
        high = low | 1 << bit
        if high != low and high < count:
            route += [(low, high), (high, low)]
    return lax.ppermute(block, axis, route)


def shifted(value, axis, steps):
    count = lax.axis_size(axis)
    pairs = [(source, (source + steps) % count) for source in range(count)]
    return lax.ppermute(value, axis, pairs)


def xor_partner(block, axes, offset):
    count = lax.axis_size(axes)
    return lax.ppermute(block, axes, [(source, source ^ offset) for source in range(count)])


def rms_scale(values, gain):
    return values * lax.rsqrt(jnp.mean(values * values, axis=-1, keepdims=True) + epsilon) * gain


def masked_scores(queries, page_rows, lengths):
    count = page_rows.shape[0]
    span = page_rows.shape[1]
    half_width = page_rows.shape[2] // 2
    key_rows = page_rows[:, :, :half_width].reshape(count, span, KVH, HD)
    value_rows = page_rows[:, :, half_width:].reshape(count, span, KVH, HD)
    scores = jnp.einsum(
        "rkgd,rskd->rkgs", queries, key_rows, preferred_element_type=jnp.float32
    ) * (1.0 / math.sqrt(HD))
    living = jnp.arange(span, dtype=jnp.int32)[None, :] < lengths[:, None]
    scores = jnp.where(living[:, None, None, :], scores, -jnp.inf)
    return (scores, value_rows)


def attend_all(queries, page_rows, lengths, own_score, value_new):
    scores, value_rows = masked_scores(queries, page_rows, lengths)
    highest = jnp.maximum(jnp.max(scores, axis=-1), own_score)
    weights = jnp.exp(scores - highest[..., None])
    own_weight = jnp.exp(own_score - highest)
    denominator = jnp.sum(weights, axis=-1) + own_weight
    weighted = jnp.einsum(
        "rkgs,rskd->rkgd",
        weights.astype(jnp.bfloat16),
        value_rows,
        preferred_element_type=jnp.float32,
    )
    own_rounded = own_weight.astype(jnp.bfloat16).astype(jnp.float32)
    weighted = weighted + own_rounded[..., None] * value_new.astype(jnp.float32)[:, :, None, :]
    return (highest, denominator, weighted)


def gather_pages(pool, tables):
    picked = pool[tables]
    return picked.reshape(tables.shape[0], tables.shape[1] * pool.shape[1], pool.shape[2])


def dense_scores(queries, page_rows, counts):
    count = page_rows.shape[0] * page_rows.shape[1]
    half_width = page_rows.shape[2] // 2
    flat = page_rows.reshape(count, page_rows.shape[2])
    key_rows = flat[:, :half_width].reshape(count, KVH, HD)
    value_rows = flat[:, half_width:].reshape(count, KVH, HD)
    scores = jnp.einsum(
        "rkgd,tkd->rkgt", queries, key_rows, preferred_element_type=jnp.float32
    ) * (1.0 / math.sqrt(HD))
    scores = jnp.where(counts[:, None, None, :] > 0, scores, -jnp.inf)
    return (scores, value_rows)


def body(
    hidden_in,
    attn_gain,
    w_qkv,
    w_out,
    final_gain,
    w_vocab,
    kv_pool,
    cache_len,
    page_table,
    migrations,
):
    device = lax.axis_index(REQ)
    devices = lax.axis_size(REQ)
    side = lax.axis_index("guide")
    local_rows = hidden_in.shape[1]
    group = QH // KVH
    query_width = QH * HD
    key_width = KVH * HD
    scaling = 1.0 / math.sqrt(HD)
    slots = 2 * HOP
    offsets = [number - HOP if number < HOP else number - HOP + 1 for number in range(slots)]
    states_in = hidden_in[0].astype(jnp.float32)
    normed = rms_scale(states_in, attn_gain).astype(jnp.bfloat16)
    partner_normed = from_partner(normed, "guide", 0)
    both_normed = jnp.where(
        side == 0, jnp.stack([normed, partner_normed]), jnp.stack([partner_normed, normed])
    )
    inner_half = w_qkv.shape[0]
    normed_part = lax.dynamic_slice_in_dim(both_normed, side * inner_half, inner_half, 2)
    selected = normed_part
    joined = lax.psum_scatter(
        jnp.einsum("grd,df->grf", selected, w_qkv, preferred_element_type=jnp.float32),
        "guide",
        scatter_dimension=0,
        tiled=True,
    )[0].astype(jnp.bfloat16)
    queries = joined[:, :query_width].reshape(local_rows, KVH, group, HD)
    new_keys = joined[:, query_width : query_width + key_width].reshape(local_rows, KVH, HD)
    new_values = joined[:, query_width + key_width :].reshape(local_rows, KVH, HD)
    own_score = (
        jnp.einsum("rkgd,rkd->rkg", queries, new_keys, preferred_element_type=jnp.float32) * scaling
    )
    tables = page_table[0]
    lengths_all = cache_len[0]
    listing = migrations[0]
    pool = kv_pool[0]
    pool_pages = pool.shape[0]
    first_row = device * local_rows
    own_table = lax.dynamic_slice_in_dim(tables, first_row, local_rows, 0)
    own_lengths = lax.dynamic_slice_in_dim(lengths_all, first_row, local_rows, 0)
    global_ids = first_row + jnp.arange(local_rows, dtype=jnp.int32)
    matches = listing[None, :, 0] == global_ids[:, None]
    is_moved = jnp.any(matches, axis=1)
    old_owner = jnp.sum(jnp.where(matches, listing[None, :, 1], 0), axis=1)
    distance = jnp.remainder(device - old_owner, devices)
    slot_of = jnp.where(distance <= HOP, HOP + distance - 1, HOP - (devices - distance))
    arrivals = []
    for number in range(slots):
        offset = offsets[number]
        holding = (listing[:, 1] == device) & (
            listing[:, 2] == jnp.remainder(device + offset, devices)
        )
        held_request = listing[jnp.argmax(holding), 0]
        pages_sent = pool[tables[held_request, :MIGP]]
        arrivals.append(shifted(pages_sent, REQ, offset))
    arrived = jnp.concatenate(arrivals, axis=0)
    page_column = jnp.minimum(jnp.arange(MAXP, dtype=jnp.int32), MIGP - 1)
    moved_pages = pool_pages + slot_of[:, None] * MIGP + page_column[None, :]
    used_table = jnp.where(is_moved[:, None], moved_pages, own_table)
    page_rows = pool.shape[1]
    living = (
        jnp.arange(MAXP, dtype=jnp.int32)[:, None] * page_rows
        + jnp.arange(page_rows, dtype=jnp.int32)[None, :]
    )[None] < own_lengths[:, None, None]
    living = living.astype(jnp.float32)
    all_pages = jnp.arange(pool_pages + arrived.shape[0], dtype=jnp.int32)
    hits = (used_table[:, :, None] == all_pages[None, None, :]).astype(jnp.float32)
    counts = jnp.einsum("rsp,rsw->rpw", hits, living).reshape(local_rows, -1)
    pool_counts = counts[:, : pool_pages * page_rows]
    arrived_counts = counts[:, pool_pages * page_rows :]
    pool_scores, pool_values = dense_scores(queries, pool, pool_counts)
    arrived_scores, arrived_values = dense_scores(queries, arrived, arrived_counts)
    tops = jnp.maximum(
        jnp.maximum(jnp.max(pool_scores, axis=-1), jnp.max(arrived_scores, axis=-1)), own_score
    )
    own_weight = jnp.exp(own_score - tops)
    sums = own_weight
    accs = own_weight.astype(jnp.bfloat16).astype(jnp.float32)[..., None] * new_values.astype(
        jnp.float32
    )[:, :, None, :]
    for scores, values, count in (
        (pool_scores, pool_values, pool_counts),
        (arrived_scores, arrived_values, arrived_counts),
    ):
        weights = jnp.exp(scores - tops[..., None])
        sums = sums + jnp.sum(weights * count[:, None, None, :], axis=-1)
        rounded = weights.astype(jnp.bfloat16).astype(jnp.float32) * count[:, None, None, :]
        accs = accs + jnp.einsum(
            "rkgt,tkd->rkgd",
            rounded,
            values.astype(jnp.float32),
            precision=lax.Precision.HIGHEST,
            preferred_element_type=jnp.float32,
        )
    attended = (accs / sums[..., None]).reshape(local_rows, query_width).astype(jnp.bfloat16)
    near = ("x_lo", "core")
    members = lax.axis_size(near)
    blocks = [w_vocab] + [xor_partner(w_vocab, near, offset) for offset in range(1, members)]
    blocks, attended = lax.optimization_barrier((blocks, attended))
    partner_attended = from_partner(attended, "guide", 0)
    both_attended = jnp.where(
        side == 0, jnp.stack([attended, partner_attended]), jnp.stack([partner_attended, attended])
    )
    head_half = w_out.shape[0]
    attended_part = lax.dynamic_slice_in_dim(both_attended, side * head_half, head_half, 2)
    selected = attended_part
    state_after = (
        states_in
        + lax.psum_scatter(
            jnp.einsum("grc,cd->grd", selected, w_out, preferred_element_type=jnp.float32).astype(
                jnp.bfloat16
            ),
            "guide",
            scatter_dimension=0,
            tiled=True,
        ).astype(jnp.float32)[0]
    )
    final = rms_scale(state_after, final_gain).astype(jnp.bfloat16)
    partner_final = from_partner(final, "guide", 0)
    cond = jnp.where(side == 0, final, partner_final).astype(jnp.float32)
    uncond = jnp.where(side == 0, partner_final, final).astype(jnp.float32)
    combined = (uncond + guidance * (cond - uncond)).astype(jnp.bfloat16)
    half_devices = devices // 2
    half_rows = local_rows // 2
    upper = device // half_devices
    kept = lax.dynamic_slice_in_dim(combined, upper * half_rows, half_rows, 0)
    sent = lax.dynamic_slice_in_dim(combined, (1 - upper) * half_rows, half_rows, 0)
    swapped = shifted(sent, REQ, half_devices)
    mine = jnp.where(upper == side, kept, swapped)
    gathered = lax.all_gather(mine, "y", axis=0, tiled=False)
    gathered = lax.all_gather(gathered, "z", axis=1, tiled=False)
    logits = jnp.einsum(
        "yzkd,mdv->myzkv",
        gathered,
        jnp.stack(blocks),
        preferred_element_type=jnp.float32,
    )
    parts = [logits[0]] + [
        xor_partner(logits[offset], near, offset) for offset in range(1, members)
    ]
    core = lax.axis_index("core")
    cores = lax.axis_size("core")
    x_low = lax.axis_index("x_lo")
    ordered = []
    for source_core in range(cores):
        for source_x in range(members // cores):
            wanted = (source_x ^ x_low) * cores + (source_core ^ core)
            pick = parts[0]
            for offset in range(1, members):
                pick = jnp.where(wanted == offset, parts[offset], pick)
            ordered.append(pick)
    placed = jnp.stack(ordered).reshape((cores, members // cores) + parts[0].shape)
    placed = jnp.transpose(placed, (2, 3, 0, 1, 4, 5))
    return placed.reshape(half_devices * local_rows, placed.shape[-1])


def solution(mesh):
    split = Mesh(mesh.devices.reshape((mesh.devices.shape[0],) + REQ_SPLIT), ("guide",) + REQ)
    in_specs = (
        P("guide", REQ, None),
        P(),
        P("guide", None),
        P("guide", None),
        P(),
        P(None, REQ),
        P("guide", REQ, None, None),
        P("guide", None),
        P("guide", None, None),
        P("guide", None, None),
    )
    out_specs = P("guide", REQ)
    return jax.shard_map(body, mesh=split, in_specs=in_specs, out_specs=out_specs, check_vma=False)
```

```python
import math

import jax
import jax.numpy as jnp
from jax import lax
from jax.sharding import Mesh
from jax.sharding import PartitionSpec as P

QH = 20
KVH = 5
HD = 64
MAXP = 8
MIGP = 2
HOP = 2
REQ = ("x_lo", "y", "z", "core")
REQ_SPLIT = (2, 4, 8, 2)


epsilon = 1e-06
guidance = 3.0


def from_partner(block, axis, bit):
    count = lax.axis_size(axis)
    route = []
    for low in range(count):
        high = low | 1 << bit
        if high != low and high < count:
            route += [(low, high), (high, low)]
    return lax.ppermute(block, axis, route)


def shifted(value, axis, steps):
    count = lax.axis_size(axis)
    pairs = [(source, (source + steps) % count) for source in range(count)]
    return lax.ppermute(value, axis, pairs)


def rms_scale(values, gain):
    return values * lax.rsqrt(jnp.mean(values * values, axis=-1, keepdims=True) + epsilon) * gain


def masked_scores(queries, page_rows, lengths):
    count = page_rows.shape[0]
    span = page_rows.shape[1]
    half_width = page_rows.shape[2] // 2
    key_rows = page_rows[:, :, :half_width].reshape(count, span, KVH, HD)
    value_rows = page_rows[:, :, half_width:].reshape(count, span, KVH, HD)
    scores = jnp.einsum(
        "rkgd,rskd->rkgs", queries, key_rows, preferred_element_type=jnp.float32
    ) * (1.0 / math.sqrt(HD))
    living = jnp.arange(span, dtype=jnp.int32)[None, :] < lengths[:, None]
    scores = jnp.where(living[:, None, None, :], scores, -jnp.inf)
    return (scores, value_rows)


def attend_all(queries, page_rows, lengths, own_score, value_new):
    scores, value_rows = masked_scores(queries, page_rows, lengths)
    highest = jnp.maximum(jnp.max(scores, axis=-1), own_score)
    weights = jnp.exp(scores - highest[..., None])
    own_weight = jnp.exp(own_score - highest)
    denominator = jnp.sum(weights, axis=-1) + own_weight
    weighted = jnp.einsum(
        "rkgs,rskd->rkgd",
        weights.astype(jnp.bfloat16),
        value_rows,
        preferred_element_type=jnp.float32,
    )
    own_rounded = own_weight.astype(jnp.bfloat16).astype(jnp.float32)
    weighted = weighted + own_rounded[..., None] * value_new.astype(jnp.float32)[:, :, None, :]
    return (highest, denominator, weighted)


def gather_pages(pool, tables):
    picked = pool[tables]
    return picked.reshape(tables.shape[0], tables.shape[1] * pool.shape[1], pool.shape[2])


def dense_scores(queries, page_rows, counts):
    count = page_rows.shape[0] * page_rows.shape[1]
    half_width = page_rows.shape[2] // 2
    flat = page_rows.reshape(count, page_rows.shape[2])
    key_rows = flat[:, :half_width].reshape(count, KVH, HD)
    value_rows = flat[:, half_width:].reshape(count, KVH, HD)
    scores = jnp.einsum(
        "rkgd,tkd->rkgt", queries, key_rows, preferred_element_type=jnp.float32
    ) * (1.0 / math.sqrt(HD))
    scores = jnp.where(counts[:, None, None, :] > 0, scores, -jnp.inf)
    return (scores, value_rows)


def body(
    hidden_in,
    attn_gain,
    w_qkv,
    w_out,
    final_gain,
    w_vocab,
    kv_pool,
    cache_len,
    page_table,
    migrations,
):
    device = lax.axis_index(REQ)
    devices = lax.axis_size(REQ)
    side = lax.axis_index("guide")
    local_rows = hidden_in.shape[1]
    group = QH // KVH
    query_width = QH * HD
    key_width = KVH * HD
    scaling = 1.0 / math.sqrt(HD)
    slots = 2 * HOP
    offsets = [number - HOP if number < HOP else number - HOP + 1 for number in range(slots)]
    states_in = hidden_in[0].astype(jnp.float32)
    normed = rms_scale(states_in, attn_gain).astype(jnp.bfloat16)
    partner_normed = from_partner(normed, "guide", 0)
    both_normed = jnp.where(
        side == 0, jnp.stack([normed, partner_normed]), jnp.stack([partner_normed, normed])
    )
    inner_half = w_qkv.shape[0]
    normed_part = lax.dynamic_slice_in_dim(both_normed, side * inner_half, inner_half, 2)
    selected = normed_part
    qkv_parts = jnp.einsum("grd,df->grf", selected, w_qkv, preferred_element_type=jnp.float32)
    own_qkv = jnp.where(side == 0, qkv_parts[0], qkv_parts[1])
    other_qkv = jnp.where(side == 0, qkv_parts[1], qkv_parts[0])
    joined = (own_qkv + from_partner(other_qkv, "guide", 0)).astype(jnp.bfloat16)
    queries = joined[:, :query_width].reshape(local_rows, KVH, group, HD)
    new_keys = joined[:, query_width : query_width + key_width].reshape(local_rows, KVH, HD)
    new_values = joined[:, query_width + key_width :].reshape(local_rows, KVH, HD)
    own_score = (
        jnp.einsum("rkgd,rkd->rkg", queries, new_keys, preferred_element_type=jnp.float32) * scaling
    )
    tables = page_table[0]
    lengths_all = cache_len[0]
    listing = migrations[0]
    pool = kv_pool[0]
    pool_pages = pool.shape[0]
    first_row = device * local_rows
    own_table = lax.dynamic_slice_in_dim(tables, first_row, local_rows, 0)
    own_lengths = lax.dynamic_slice_in_dim(lengths_all, first_row, local_rows, 0)
    global_ids = first_row + jnp.arange(local_rows, dtype=jnp.int32)
    matches = listing[None, :, 0] == global_ids[:, None]
    is_moved = jnp.any(matches, axis=1)
    old_owner = jnp.sum(jnp.where(matches, listing[None, :, 1], 0), axis=1)
    distance = jnp.remainder(device - old_owner, devices)
    slot_of = jnp.where(distance <= HOP, HOP + distance - 1, HOP - (devices - distance))
    arrivals = []
    for number in range(slots):
        offset = offsets[number]
        holding = (listing[:, 1] == device) & (
            listing[:, 2] == jnp.remainder(device + offset, devices)
        )
        held_request = listing[jnp.argmax(holding), 0]
        pages_sent = pool[tables[held_request, :MIGP]]
        arrivals.append(shifted(pages_sent, REQ, offset))
    arrived = jnp.concatenate(arrivals, axis=0)
    page_column = jnp.minimum(jnp.arange(MAXP, dtype=jnp.int32), MIGP - 1)
    moved_pages = pool_pages + slot_of[:, None] * MIGP + page_column[None, :]
    used_table = jnp.where(is_moved[:, None], moved_pages, own_table)
    page_rows = pool.shape[1]
    living = (
        jnp.arange(MAXP, dtype=jnp.int32)[:, None] * page_rows
        + jnp.arange(page_rows, dtype=jnp.int32)[None, :]
    )[None] < own_lengths[:, None, None]
    living = living.astype(jnp.float32)
    all_pages = jnp.arange(pool_pages + arrived.shape[0], dtype=jnp.int32)
    hits = (used_table[:, :, None] == all_pages[None, None, :]).astype(jnp.float32)
    counts = jnp.einsum("rsp,rsw->rpw", hits, living).reshape(local_rows, -1)
    pool_counts = counts[:, : pool_pages * page_rows]
    arrived_counts = counts[:, pool_pages * page_rows :]
    pool_scores, pool_values = dense_scores(queries, pool, pool_counts)
    arrived_scores, arrived_values = dense_scores(queries, arrived, arrived_counts)
    tops = jnp.maximum(
        jnp.maximum(jnp.max(pool_scores, axis=-1), jnp.max(arrived_scores, axis=-1)), own_score
    )
    own_weight = jnp.exp(own_score - tops)
    sums = own_weight
    accs = own_weight.astype(jnp.bfloat16).astype(jnp.float32)[..., None] * new_values.astype(
        jnp.float32
    )[:, :, None, :]
    for scores, values, count in (
        (pool_scores, pool_values, pool_counts),
        (arrived_scores, arrived_values, arrived_counts),
    ):
        weights = jnp.exp(scores - tops[..., None])
        sums = sums + jnp.sum(weights * count[:, None, None, :], axis=-1)
        rounded = weights.astype(jnp.bfloat16).astype(jnp.float32) * count[:, None, None, :]
        accs = accs + jnp.einsum(
            "rkgt,tkd->rkgd",
            rounded,
            values.astype(jnp.float32),
            precision=lax.Precision.HIGHEST,
            preferred_element_type=jnp.float32,
        )
    attended = (accs / sums[..., None]).reshape(local_rows, query_width).astype(jnp.bfloat16)
    partner_attended = from_partner(attended, "guide", 0)
    both_attended = jnp.where(
        side == 0, jnp.stack([attended, partner_attended]), jnp.stack([partner_attended, attended])
    )
    head_half = w_out.shape[0]
    attended_part = lax.dynamic_slice_in_dim(both_attended, side * head_half, head_half, 2)
    selected = attended_part
    out_parts = jnp.einsum("grc,cd->grd", selected, w_out, preferred_element_type=jnp.float32)
    own_out = jnp.where(side == 0, out_parts[0], out_parts[1])
    other_out = jnp.where(side == 0, out_parts[1], out_parts[0]).astype(jnp.bfloat16)
    state_after = states_in + (
        own_out + from_partner(other_out, "guide", 0).astype(jnp.float32)
    )
    final = rms_scale(state_after, final_gain).astype(jnp.bfloat16)
    pair = ("guide", "x_lo")
    from_side = lax.ppermute(final, pair, [(0, 1), (3, 2)])
    from_diagonal = lax.ppermute(final, pair, [(2, 1), (1, 2)])
    from_guide = lax.ppermute(final, pair, [(2, 0), (1, 3)])
    home = lax.axis_index("x_lo") == side
    same_group = jnp.where(home, final, from_side)
    other_group = jnp.where(home, from_guide, from_diagonal)
    cond = jnp.where(side == 0, same_group, other_group).astype(jnp.float32)
    uncond = jnp.where(side == 0, other_group, same_group).astype(jnp.float32)
    combined = (uncond + guidance * (cond - uncond)).astype(jnp.bfloat16)
    gathered = lax.all_gather(combined, "y", axis=0, tiled=False)
    gathered = lax.all_gather(gathered, "z", axis=1, tiled=False)
    gathered = lax.all_gather(gathered, "core", axis=2, tiled=False)
    logits = jnp.einsum(
        "yzcrd,dv->yzcrv", gathered, w_vocab, preferred_element_type=jnp.float32
    )
    return logits.reshape(-1, logits.shape[-1])


def solution(mesh):
    split = Mesh(mesh.devices.reshape((mesh.devices.shape[0],) + REQ_SPLIT), ("guide",) + REQ)
    in_specs = (
        P("guide", REQ, None),
        P(),
        P("guide", None),
        P("guide", None),
        P(),
        P(None, REQ),
        P("guide", REQ, None, None),
        P("guide", None),
        P("guide", None, None),
        P("guide", None, None),
    )
    out_specs = P("guide", REQ)
    return jax.shard_map(body, mesh=split, in_specs=in_specs, out_specs=out_specs, check_vma=False)
```

```python
import math

import jax
import jax.numpy as jnp
from jax import lax
from jax.sharding import Mesh
from jax.sharding import PartitionSpec as P

QH = 20
KVH = 5
HD = 64
MAXP = 8
MIGP = 2
HOP = 2
REQ = ("x_lo", "y", "z", "core")
REQ_SPLIT = (2, 4, 8, 2)


epsilon = 1e-06
guidance = 3.0


def from_partner(block, axis, bit):
    count = lax.axis_size(axis)
    route = []
    for low in range(count):
        high = low | 1 << bit
        if high != low and high < count:
            route += [(low, high), (high, low)]
    return lax.ppermute(block, axis, route)


def shifted(value, axis, steps):
    count = lax.axis_size(axis)
    pairs = [(source, (source + steps) % count) for source in range(count)]
    return lax.ppermute(value, axis, pairs)


def rms_scale(values, gain):
    return values * lax.rsqrt(jnp.mean(values * values, axis=-1, keepdims=True) + epsilon) * gain


def masked_scores(queries, page_rows, lengths):
    count = page_rows.shape[0]
    span = page_rows.shape[1]
    half_width = page_rows.shape[2] // 2
    key_rows = page_rows[:, :, :half_width].reshape(count, span, KVH, HD)
    value_rows = page_rows[:, :, half_width:].reshape(count, span, KVH, HD)
    scores = jnp.einsum(
        "rkgd,rskd->rkgs", queries, key_rows, preferred_element_type=jnp.float32
    ) * (1.0 / math.sqrt(HD))
    living = jnp.arange(span, dtype=jnp.int32)[None, :] < lengths[:, None]
    scores = jnp.where(living[:, None, None, :], scores, -jnp.inf)
    return (scores, value_rows)


def attend_all(queries, page_rows, lengths, own_score, value_new):
    scores, value_rows = masked_scores(queries, page_rows, lengths)
    highest = jnp.maximum(jnp.max(scores, axis=-1), own_score)
    weights = jnp.exp(scores - highest[..., None])
    own_weight = jnp.exp(own_score - highest)
    denominator = jnp.sum(weights, axis=-1) + own_weight
    weighted = jnp.einsum(
        "rkgs,rskd->rkgd",
        weights.astype(jnp.bfloat16),
        value_rows,
        preferred_element_type=jnp.float32,
    )
    own_rounded = own_weight.astype(jnp.bfloat16).astype(jnp.float32)
    weighted = weighted + own_rounded[..., None] * value_new.astype(jnp.float32)[:, :, None, :]
    return (highest, denominator, weighted)


def gather_pages(pool, tables):
    picked = pool[tables]
    return picked.reshape(tables.shape[0], tables.shape[1] * pool.shape[1], pool.shape[2])


def dense_scores(queries, page_rows, counts):
    count = page_rows.shape[0] * page_rows.shape[1]
    half_width = page_rows.shape[2] // 2
    flat = page_rows.reshape(count, page_rows.shape[2])
    key_rows = flat[:, :half_width].reshape(count, KVH, HD)
    value_rows = flat[:, half_width:].reshape(count, KVH, HD)
    scores = jnp.einsum(
        "rkgd,tkd->rkgt", queries, key_rows, preferred_element_type=jnp.float32
    ) * (1.0 / math.sqrt(HD))
    scores = jnp.where(counts[:, None, None, :] > 0, scores, -jnp.inf)
    return (scores, value_rows)


def body(
    hidden_in,
    attn_gain,
    w_qkv,
    w_out,
    final_gain,
    w_vocab,
    kv_pool,
    cache_len,
    page_table,
    migrations,
):
    device = lax.axis_index(REQ)
    devices = lax.axis_size(REQ)
    side = lax.axis_index("guide")
    local_rows = hidden_in.shape[1]
    group = QH // KVH
    query_width = QH * HD
    key_width = KVH * HD
    scaling = 1.0 / math.sqrt(HD)
    slots = 2 * HOP
    offsets = [number - HOP if number < HOP else number - HOP + 1 for number in range(slots)]
    states_in = hidden_in[0].astype(jnp.float32)
    normed = rms_scale(states_in, attn_gain).astype(jnp.bfloat16)
    partner_normed = from_partner(normed, "guide", 0)
    both_normed = jnp.where(
        side == 0, jnp.stack([normed, partner_normed]), jnp.stack([partner_normed, normed])
    )
    inner_half = w_qkv.shape[0]
    normed_part = lax.dynamic_slice_in_dim(both_normed, side * inner_half, inner_half, 2)
    selected = normed_part
    qkv_parts = jnp.einsum("grd,df->grf", selected, w_qkv, preferred_element_type=jnp.float32)
    own_qkv = jnp.where(side == 0, qkv_parts[0], qkv_parts[1])
    other_qkv = jnp.where(side == 0, qkv_parts[1], qkv_parts[0])
    joined = (own_qkv + from_partner(other_qkv, "guide", 0)).astype(jnp.bfloat16)
    queries = joined[:, :query_width].reshape(local_rows, KVH, group, HD)
    new_keys = joined[:, query_width : query_width + key_width].reshape(local_rows, KVH, HD)
    new_values = joined[:, query_width + key_width :].reshape(local_rows, KVH, HD)
    own_score = (
        jnp.einsum("rkgd,rkd->rkg", queries, new_keys, preferred_element_type=jnp.float32) * scaling
    )
    tables = page_table[0]
    lengths_all = cache_len[0]
    listing = migrations[0]
    pool = kv_pool[0]
    pool_pages = pool.shape[0]
    first_row = device * local_rows
    own_table = lax.dynamic_slice_in_dim(tables, first_row, local_rows, 0)
    own_lengths = lax.dynamic_slice_in_dim(lengths_all, first_row, local_rows, 0)
    global_ids = first_row + jnp.arange(local_rows, dtype=jnp.int32)
    matches = listing[None, :, 0] == global_ids[:, None]
    is_moved = jnp.any(matches, axis=1)
    old_owner = jnp.sum(jnp.where(matches, listing[None, :, 1], 0), axis=1)
    distance = jnp.remainder(device - old_owner, devices)
    slot_of = jnp.where(distance <= HOP, HOP + distance - 1, HOP - (devices - distance))
    targets = jnp.remainder(device + jnp.array(offsets, jnp.int32), devices)
    holding = (listing[None, :, 1] == device) & (listing[None, :, 2] == targets[:, None])
    held_request = jnp.sum(jnp.where(holding, listing[None, :, 0], 0), axis=1)
    request_hit = jnp.arange(tables.shape[0], dtype=jnp.int32)[None, :] == held_request[:, None]
    sent_ids = jnp.sum(jnp.where(request_hit[:, :, None], tables[None, :, :MIGP], 0), axis=1)
    page_hit = (
        sent_ids[:, :, None] == jnp.arange(pool_pages, dtype=jnp.int32)[None, None, :]
    ).astype(jnp.bfloat16)
    pages_sent = jnp.einsum(
        "smp,pwc->smwc", page_hit, pool, preferred_element_type=jnp.float32
    ).astype(jnp.bfloat16)
    arrivals = [shifted(pages_sent[number], REQ, offsets[number]) for number in range(slots)]
    arrived = jnp.concatenate(arrivals, axis=0)
    page_column = jnp.minimum(jnp.arange(MAXP, dtype=jnp.int32), MIGP - 1)
    moved_pages = pool_pages + slot_of[:, None] * MIGP + page_column[None, :]
    used_table = jnp.where(is_moved[:, None], moved_pages, own_table)
    page_rows = pool.shape[1]
    living = (
        jnp.arange(MAXP, dtype=jnp.int32)[:, None] * page_rows
        + jnp.arange(page_rows, dtype=jnp.int32)[None, :]
    )[None] < own_lengths[:, None, None]
    living = living.astype(jnp.float32)
    all_pages = jnp.arange(pool_pages + arrived.shape[0], dtype=jnp.int32)
    hits = (used_table[:, :, None] == all_pages[None, None, :]).astype(jnp.float32)
    counts = jnp.einsum("rsp,rsw->rpw", hits, living).reshape(local_rows, -1)
    pool_counts = counts[:, : pool_pages * page_rows]
    arrived_counts = counts[:, pool_pages * page_rows :]
    pool_scores, pool_values = dense_scores(queries, pool, pool_counts)
    arrived_scores, arrived_values = dense_scores(queries, arrived, arrived_counts)
    tops = jnp.maximum(
        jnp.maximum(jnp.max(pool_scores, axis=-1), jnp.max(arrived_scores, axis=-1)), own_score
    )
    own_weight = jnp.exp(own_score - tops)
    sums = own_weight
    accs = own_weight.astype(jnp.bfloat16).astype(jnp.float32)[..., None] * new_values.astype(
        jnp.float32
    )[:, :, None, :]
    for scores, values, count in (
        (pool_scores, pool_values, pool_counts),
        (arrived_scores, arrived_values, arrived_counts),
    ):
        weights = jnp.exp(scores - tops[..., None])
        sums = sums + jnp.sum(weights * count[:, None, None, :], axis=-1)
        rounded = weights.astype(jnp.bfloat16).astype(jnp.float32) * count[:, None, None, :]
        accs = accs + jnp.einsum(
            "rkgt,tkd->rkgd",
            rounded,
            values.astype(jnp.float32),
            precision=lax.Precision.HIGHEST,
            preferred_element_type=jnp.float32,
        )
    attended = (accs / sums[..., None]).reshape(local_rows, query_width).astype(jnp.bfloat16)
    partner_attended = from_partner(attended, "guide", 0)
    both_attended = jnp.where(
        side == 0, jnp.stack([attended, partner_attended]), jnp.stack([partner_attended, attended])
    )
    head_half = w_out.shape[0]
    attended_part = lax.dynamic_slice_in_dim(both_attended, side * head_half, head_half, 2)
    selected = attended_part
    out_parts = jnp.einsum("grc,cd->grd", selected, w_out, preferred_element_type=jnp.float32)
    own_out = jnp.where(side == 0, out_parts[0], out_parts[1])
    other_out = jnp.where(side == 0, out_parts[1], out_parts[0]).astype(jnp.bfloat16)
    state_after = states_in + (
        own_out + from_partner(other_out, "guide", 0).astype(jnp.float32)
    )
    final = rms_scale(state_after, final_gain).astype(jnp.bfloat16)
    pair = ("guide", "x_lo")
    from_side = lax.ppermute(final, pair, [(0, 1), (3, 2)])
    from_diagonal = lax.ppermute(final, pair, [(2, 1), (1, 2)])
    from_guide = lax.ppermute(final, pair, [(2, 0), (1, 3)])
    home = lax.axis_index("x_lo") == side
    same_group = jnp.where(home, final, from_side)
    other_group = jnp.where(home, from_guide, from_diagonal)
    cond = jnp.where(side == 0, same_group, other_group).astype(jnp.float32)
    uncond = jnp.where(side == 0, other_group, same_group).astype(jnp.float32)
    combined = (uncond + guidance * (cond - uncond)).astype(jnp.bfloat16)
    gathered = lax.all_gather(combined, "y", axis=0, tiled=False)
    gathered = lax.all_gather(gathered, "z", axis=1, tiled=False)
    gathered = lax.all_gather(gathered, "core", axis=2, tiled=False)
    logits = jnp.einsum(
        "yzcrd,dv->yzcrv", gathered, w_vocab, preferred_element_type=jnp.float32
    )
    return logits.reshape(-1, logits.shape[-1])


def solution(mesh):
    split = Mesh(mesh.devices.reshape((mesh.devices.shape[0],) + REQ_SPLIT), ("guide",) + REQ)
    in_specs = (
        P("guide", REQ, None),
        P(),
        P("guide", None),
        P("guide", None),
        P(),
        P(None, REQ),
        P("guide", REQ, None, None),
        P("guide", None),
        P("guide", None, None),
        P("guide", None, None),
    )
    out_specs = P("guide", REQ)
    return jax.shard_map(body, mesh=split, in_specs=in_specs, out_specs=out_specs, check_vma=False)
```

```python
import math

import jax
import jax.numpy as jnp
from jax import lax
from jax.sharding import Mesh
from jax.sharding import PartitionSpec as P

QH = 20
KVH = 5
HD = 64
MAXP = 8
MIGP = 2
HOP = 2
REQ = ("x_lo", "y", "z", "core")
REQ_SPLIT = (2, 4, 8, 2)


epsilon = 1e-06
guidance = 3.0


def from_partner(block, axis, bit):
    count = lax.axis_size(axis)
    route = []
    for low in range(count):
        high = low | 1 << bit
        if high != low and high < count:
            route += [(low, high), (high, low)]
    return lax.ppermute(block, axis, route)


def shifted(value, axis, steps):
    count = lax.axis_size(axis)
    pairs = [(source, (source + steps) % count) for source in range(count)]
    return lax.ppermute(value, axis, pairs)


def rms_scale(values, gain):
    return values * lax.rsqrt(jnp.mean(values * values, axis=-1, keepdims=True) + epsilon) * gain


def masked_scores(queries, page_rows, lengths):
    count = page_rows.shape[0]
    span = page_rows.shape[1]
    half_width = page_rows.shape[2] // 2
    key_rows = page_rows[:, :, :half_width].reshape(count, span, KVH, HD)
    value_rows = page_rows[:, :, half_width:].reshape(count, span, KVH, HD)
    scores = jnp.einsum(
        "rkgd,rskd->rkgs", queries, key_rows, preferred_element_type=jnp.float32
    ) * (1.0 / math.sqrt(HD))
    living = jnp.arange(span, dtype=jnp.int32)[None, :] < lengths[:, None]
    scores = jnp.where(living[:, None, None, :], scores, -jnp.inf)
    return (scores, value_rows)


def attend_all(queries, page_rows, lengths, own_score, value_new):
    scores, value_rows = masked_scores(queries, page_rows, lengths)
    highest = jnp.maximum(jnp.max(scores, axis=-1), own_score)
    weights = jnp.exp(scores - highest[..., None])
    own_weight = jnp.exp(own_score - highest)
    denominator = jnp.sum(weights, axis=-1) + own_weight
    weighted = jnp.einsum(
        "rkgs,rskd->rkgd",
        weights.astype(jnp.bfloat16),
        value_rows,
        preferred_element_type=jnp.float32,
    )
    own_rounded = own_weight.astype(jnp.bfloat16).astype(jnp.float32)
    weighted = weighted + own_rounded[..., None] * value_new.astype(jnp.float32)[:, :, None, :]
    return (highest, denominator, weighted)


def gather_pages(pool, tables):
    picked = pool[tables]
    return picked.reshape(tables.shape[0], tables.shape[1] * pool.shape[1], pool.shape[2])


def dense_scores(queries, page_rows, counts):
    count = page_rows.shape[0] * page_rows.shape[1]
    half_width = page_rows.shape[2] // 2
    flat = page_rows.reshape(count, page_rows.shape[2])
    key_rows = flat[:, :half_width].reshape(count, KVH, HD)
    value_rows = flat[:, half_width:].reshape(count, KVH, HD)
    scores = jnp.einsum(
        "rkgd,tkd->rkgt", queries, key_rows, preferred_element_type=jnp.float32
    ) * (1.0 / math.sqrt(HD))
    scores = jnp.where(counts[:, None, None, :] > 0, scores, -jnp.inf)
    return (scores, value_rows)


def body(
    hidden_in,
    attn_gain,
    w_qkv,
    w_out,
    final_gain,
    w_vocab,
    kv_pool,
    cache_len,
    page_table,
    migrations,
):
    device = lax.axis_index(REQ)
    devices = lax.axis_size(REQ)
    side = lax.axis_index("guide")
    local_rows = hidden_in.shape[1]
    group = QH // KVH
    query_width = QH * HD
    key_width = KVH * HD
    scaling = 1.0 / math.sqrt(HD)
    slots = 2 * HOP
    offsets = [number - HOP if number < HOP else number - HOP + 1 for number in range(slots)]
    states_in = hidden_in[0].astype(jnp.float32)
    normed = rms_scale(states_in, attn_gain).astype(jnp.bfloat16)
    partner_normed = from_partner(normed, "guide", 0)
    both_normed = jnp.where(
        side == 0, jnp.stack([normed, partner_normed]), jnp.stack([partner_normed, normed])
    )
    inner_half = w_qkv.shape[0]
    normed_part = lax.dynamic_slice_in_dim(both_normed, side * inner_half, inner_half, 2)
    selected = normed_part
    qkv_parts = jnp.einsum("grd,df->grf", selected, w_qkv, preferred_element_type=jnp.float32)
    own_qkv = jnp.where(side == 0, qkv_parts[0], qkv_parts[1])
    other_qkv = jnp.where(side == 0, qkv_parts[1], qkv_parts[0])
    joined = (own_qkv + from_partner(other_qkv, "guide", 0)).astype(jnp.bfloat16)
    queries = joined[:, :query_width].reshape(local_rows, KVH, group, HD)
    new_keys = joined[:, query_width : query_width + key_width].reshape(local_rows, KVH, HD)
    new_values = joined[:, query_width + key_width :].reshape(local_rows, KVH, HD)
    own_score = (
        jnp.einsum("rkgd,rkd->rkg", queries, new_keys, preferred_element_type=jnp.float32) * scaling
    )
    tables = page_table[0]
    lengths_all = cache_len[0]
    listing = migrations[0]
    pool = kv_pool[0]
    pool_pages = pool.shape[0]
    first_row = device * local_rows
    own_table = lax.dynamic_slice_in_dim(tables, first_row, local_rows, 0)
    own_lengths = lax.dynamic_slice_in_dim(lengths_all, first_row, local_rows, 0)
    global_ids = first_row + jnp.arange(local_rows, dtype=jnp.int32)
    matches = listing[None, :, 0] == global_ids[:, None]
    is_moved = jnp.any(matches, axis=1)
    old_owner = jnp.sum(jnp.where(matches, listing[None, :, 1], 0), axis=1)
    distance = jnp.remainder(device - old_owner, devices)
    slot_of = jnp.where(distance <= HOP, HOP + distance - 1, HOP - (devices - distance))
    targets = jnp.remainder(device + jnp.array(offsets, jnp.int32), devices)
    holding = (listing[None, :, 1] == device) & (listing[None, :, 2] == targets[:, None])
    held_request = jnp.sum(jnp.where(holding, listing[None, :, 0], 0), axis=1)
    request_hit = jnp.arange(tables.shape[0], dtype=jnp.int32)[None, :] == held_request[:, None]
    sent_ids = jnp.sum(jnp.where(request_hit[:, :, None], tables[None, :, :MIGP], 0), axis=1)
    page_hit = (
        sent_ids[:, :, None] == jnp.arange(pool_pages, dtype=jnp.int32)[None, None, :]
    ).astype(jnp.bfloat16)
    pages_sent = jnp.einsum(
        "smp,pwc->smwc", page_hit, pool, preferred_element_type=jnp.float32
    ).astype(jnp.bfloat16)
    arrivals = [shifted(pages_sent[number], REQ, offsets[number]) for number in range(slots)]
    arrived = jnp.concatenate(arrivals, axis=0)
    page_column = jnp.minimum(jnp.arange(MAXP, dtype=jnp.int32), MIGP - 1)
    moved_pages = pool_pages + slot_of[:, None] * MIGP + page_column[None, :]
    used_table = jnp.where(is_moved[:, None], moved_pages, own_table)
    page_rows = pool.shape[1]
    living = (
        jnp.arange(MAXP, dtype=jnp.int32)[:, None] * page_rows
        + jnp.arange(page_rows, dtype=jnp.int32)[None, :]
    )[None] < own_lengths[:, None, None]
    living = living.astype(jnp.float32)
    all_pages = jnp.arange(pool_pages + arrived.shape[0], dtype=jnp.int32)
    hits = (used_table[:, :, None] == all_pages[None, None, :]).astype(jnp.float32)
    counts = jnp.einsum("rsp,rsw->rpw", hits, living).reshape(local_rows, -1)
    pool_counts = counts[:, : pool_pages * page_rows]
    arrived_counts = counts[:, pool_pages * page_rows :]
    pool_scores, pool_values = dense_scores(queries, pool, pool_counts)
    arrived_scores, arrived_values = dense_scores(queries, arrived, arrived_counts)
    tops = jnp.maximum(
        jnp.maximum(jnp.max(pool_scores, axis=-1), jnp.max(arrived_scores, axis=-1)), own_score
    )
    own_weight = jnp.exp(own_score - tops)
    sums = own_weight
    accs = own_weight.astype(jnp.bfloat16).astype(jnp.float32)[..., None] * new_values.astype(
        jnp.float32
    )[:, :, None, :]
    for scores, values, count in (
        (pool_scores, pool_values, pool_counts),
        (arrived_scores, arrived_values, arrived_counts),
    ):
        weights = jnp.exp(scores - tops[..., None])
        sums = sums + jnp.sum(weights * count[:, None, None, :], axis=-1)
        rounded = weights.astype(jnp.bfloat16).astype(jnp.float32) * count[:, None, None, :]
        accs = accs + jnp.einsum(
            "rkgt,tkd->rkgd",
            rounded,
            values.astype(jnp.float32),
            precision=lax.Precision.HIGHEST,
            preferred_element_type=jnp.float32,
        )
    attended = (accs / sums[..., None]).reshape(local_rows, query_width).astype(jnp.bfloat16)
    partner_attended = from_partner(attended, "guide", 0)
    both_attended = jnp.where(
        side == 0, jnp.stack([attended, partner_attended]), jnp.stack([partner_attended, attended])
    )
    head_half = w_out.shape[0]
    attended_part = lax.dynamic_slice_in_dim(both_attended, side * head_half, head_half, 2)
    selected = attended_part
    out_parts = jnp.einsum("grc,cd->grd", selected, w_out, preferred_element_type=jnp.float32)
    own_out = jnp.where(side == 0, out_parts[0], out_parts[1])
    other_out = jnp.where(side == 0, out_parts[1], out_parts[0]).astype(jnp.bfloat16)
    state_after = states_in + (
        own_out + from_partner(other_out, "guide", 0).astype(jnp.float32)
    )
    final = rms_scale(state_after, final_gain).astype(jnp.bfloat16)
    pair = ("guide", "x_lo")
    from_side = lax.ppermute(final, pair, [(0, 1), (3, 2)])
    from_diagonal = lax.ppermute(final, pair, [(2, 1), (1, 2)])
    from_guide = lax.ppermute(final, pair, [(2, 0), (1, 3)])
    home = lax.axis_index("x_lo") == side
    same_group = jnp.where(home, final, from_side)
    other_group = jnp.where(home, from_guide, from_diagonal)
    cond = jnp.where(side == 0, same_group, other_group).astype(jnp.float32)
    uncond = jnp.where(side == 0, other_group, same_group).astype(jnp.float32)
    combined = (uncond + guidance * (cond - uncond)).astype(jnp.bfloat16)
    gathered = lax.all_gather(combined, "y", axis=0, tiled=False)
    gathered = lax.all_gather(gathered, "z", axis=1, tiled=False)
    core = lax.axis_index("core")
    twin = lax.ppermute(gathered, "core", [(0, 1), (1, 0)])
    mine_logits = jnp.einsum("yzrd,dv->yzrv", gathered, w_vocab, preferred_element_type=jnp.float32)
    twin_logits = jnp.einsum("yzrd,dv->yzrv", twin, w_vocab, preferred_element_type=jnp.float32)
    logits = jnp.stack(
        [
            jnp.where(core == 0, mine_logits, twin_logits),
            jnp.where(core == 0, twin_logits, mine_logits),
        ],
        axis=2,
    )
    return logits.reshape(-1, logits.shape[-1])


def solution(mesh):
    split = Mesh(mesh.devices.reshape((mesh.devices.shape[0],) + REQ_SPLIT), ("guide",) + REQ)
    in_specs = (
        P("guide", REQ, None),
        P(),
        P("guide", None),
        P("guide", None),
        P(),
        P(None, REQ),
        P("guide", REQ, None, None),
        P("guide", None),
        P("guide", None, None),
        P("guide", None, None),
    )
    out_specs = P("guide", REQ)
    return jax.shard_map(body, mesh=split, in_specs=in_specs, out_specs=out_specs, check_vma=False)
```

```python
import math

import jax
import jax.numpy as jnp
from jax import lax
from jax.sharding import Mesh
from jax.sharding import PartitionSpec as P

QH = 20
KVH = 5
HD = 64
MAXP = 8
MIGP = 2
HOP = 2
REQ = ("x_lo", "y", "z", "core")
REQ_SPLIT = (2, 4, 8, 2)


epsilon = 1e-06
guidance = 3.0


def from_partner(block, axis, bit):
    count = lax.axis_size(axis)
    route = []
    for low in range(count):
        high = low | 1 << bit
        if high != low and high < count:
            route += [(low, high), (high, low)]
    return lax.ppermute(block, axis, route)


def shifted(value, axis, steps):
    count = lax.axis_size(axis)
    pairs = [(source, (source + steps) % count) for source in range(count)]
    return lax.ppermute(value, axis, pairs)


def rms_scale(values, gain):
    return values * lax.rsqrt(jnp.mean(values * values, axis=-1, keepdims=True) + epsilon) * gain


def masked_scores(queries, page_rows, lengths):
    count = page_rows.shape[0]
    span = page_rows.shape[1]
    half_width = page_rows.shape[2] // 2
    key_rows = page_rows[:, :, :half_width].reshape(count, span, KVH, HD)
    value_rows = page_rows[:, :, half_width:].reshape(count, span, KVH, HD)
    scores = jnp.einsum(
        "rkgd,rskd->rkgs", queries, key_rows, preferred_element_type=jnp.float32
    ) * (1.0 / math.sqrt(HD))
    living = jnp.arange(span, dtype=jnp.int32)[None, :] < lengths[:, None]
    scores = jnp.where(living[:, None, None, :], scores, -jnp.inf)
    return (scores, value_rows)


def attend_all(queries, page_rows, lengths, own_score, value_new):
    scores, value_rows = masked_scores(queries, page_rows, lengths)
    highest = jnp.maximum(jnp.max(scores, axis=-1), own_score)
    weights = jnp.exp(scores - highest[..., None])
    own_weight = jnp.exp(own_score - highest)
    denominator = jnp.sum(weights, axis=-1) + own_weight
    weighted = jnp.einsum(
        "rkgs,rskd->rkgd",
        weights.astype(jnp.bfloat16),
        value_rows,
        preferred_element_type=jnp.float32,
    )
    own_rounded = own_weight.astype(jnp.bfloat16).astype(jnp.float32)
    weighted = weighted + own_rounded[..., None] * value_new.astype(jnp.float32)[:, :, None, :]
    return (highest, denominator, weighted)


def gather_pages(pool, tables):
    picked = pool[tables]
    return picked.reshape(tables.shape[0], tables.shape[1] * pool.shape[1], pool.shape[2])


def dense_scores(queries, page_rows, counts):
    count = page_rows.shape[0] * page_rows.shape[1]
    half_width = page_rows.shape[2] // 2
    flat = page_rows.reshape(count, page_rows.shape[2])
    key_rows = flat[:, :half_width].reshape(count, KVH, HD)
    value_rows = flat[:, half_width:].reshape(count, KVH, HD)
    scores = jnp.einsum(
        "rkgd,tkd->rkgt", queries, key_rows, preferred_element_type=jnp.float32
    ) * (1.0 / math.sqrt(HD))
    scores = jnp.where(counts[:, None, None, :] > 0, scores, -jnp.inf)
    return (scores, value_rows)


def body(
    hidden_in,
    attn_gain,
    w_qkv,
    w_out,
    final_gain,
    w_vocab,
    kv_pool,
    cache_len,
    page_table,
    migrations,
):
    device = lax.axis_index(REQ)
    devices = lax.axis_size(REQ)
    side = lax.axis_index("guide")
    local_rows = hidden_in.shape[1]
    group = QH // KVH
    query_width = QH * HD
    key_width = KVH * HD
    scaling = 1.0 / math.sqrt(HD)
    slots = 2 * HOP
    offsets = [number - HOP if number < HOP else number - HOP + 1 for number in range(slots)]
    states_in = hidden_in[0].astype(jnp.float32)
    normed = rms_scale(states_in, attn_gain).astype(jnp.bfloat16)
    partner_normed = from_partner(normed, "guide", 0)
    both_normed = jnp.where(
        side == 0, jnp.stack([normed, partner_normed]), jnp.stack([partner_normed, normed])
    )
    inner_half = w_qkv.shape[0]
    normed_part = lax.dynamic_slice_in_dim(both_normed, side * inner_half, inner_half, 2)
    selected = normed_part
    qkv_parts = jnp.einsum("grd,df->grf", selected, w_qkv, preferred_element_type=jnp.float32)
    own_qkv = jnp.where(side == 0, qkv_parts[0], qkv_parts[1])
    other_qkv = jnp.where(side == 0, qkv_parts[1], qkv_parts[0])
    joined = (own_qkv + from_partner(other_qkv, "guide", 0)).astype(jnp.bfloat16)
    queries = joined[:, :query_width].reshape(local_rows, KVH, group, HD)
    new_keys = joined[:, query_width : query_width + key_width].reshape(local_rows, KVH, HD)
    new_values = joined[:, query_width + key_width :].reshape(local_rows, KVH, HD)
    own_score = (
        jnp.einsum("rkgd,rkd->rkg", queries, new_keys, preferred_element_type=jnp.float32) * scaling
    )
    tables = page_table[0]
    lengths_all = cache_len[0]
    listing = migrations[0]
    pool = kv_pool[0]
    pool_pages = pool.shape[0]
    first_row = device * local_rows
    own_table = lax.dynamic_slice_in_dim(tables, first_row, local_rows, 0)
    own_lengths = lax.dynamic_slice_in_dim(lengths_all, first_row, local_rows, 0)
    global_ids = first_row + jnp.arange(local_rows, dtype=jnp.int32)
    matches = listing[None, :, 0] == global_ids[:, None]
    is_moved = jnp.any(matches, axis=1)
    old_owner = jnp.sum(jnp.where(matches, listing[None, :, 1], 0), axis=1)
    distance = jnp.remainder(device - old_owner, devices)
    slot_of = jnp.where(distance <= HOP, HOP + distance - 1, HOP - (devices - distance))
    targets = jnp.remainder(device + jnp.array(offsets, jnp.int32), devices)
    holding = (listing[None, :, 1] == device) & (listing[None, :, 2] == targets[:, None])
    held_request = jnp.sum(jnp.where(holding, listing[None, :, 0], 0), axis=1)
    request_hit = jnp.arange(tables.shape[0], dtype=jnp.int32)[None, :] == held_request[:, None]
    sent_ids = jnp.sum(jnp.where(request_hit[:, :, None], tables[None, :, :MIGP], 0), axis=1)
    page_hit = (
        sent_ids[:, :, None] == jnp.arange(pool_pages, dtype=jnp.int32)[None, None, :]
    ).astype(jnp.bfloat16)
    pages_sent = jnp.einsum(
        "smp,pwc->smwc", page_hit, pool, preferred_element_type=jnp.float32
    ).astype(jnp.bfloat16)
    arrivals = [shifted(pages_sent[number], REQ, offsets[number]) for number in range(slots)]
    arrived = jnp.concatenate(arrivals, axis=0)
    page_column = jnp.minimum(jnp.arange(MAXP, dtype=jnp.int32), MIGP - 1)
    moved_pages = pool_pages + slot_of[:, None] * MIGP + page_column[None, :]
    used_table = jnp.where(is_moved[:, None], moved_pages, own_table)
    page_rows = pool.shape[1]
    living = (
        jnp.arange(MAXP, dtype=jnp.int32)[:, None] * page_rows
        + jnp.arange(page_rows, dtype=jnp.int32)[None, :]
    )[None] < own_lengths[:, None, None]
    living = living.astype(jnp.float32)
    all_pages = jnp.arange(pool_pages + arrived.shape[0], dtype=jnp.int32)
    hits = (used_table[:, :, None] == all_pages[None, None, :]).astype(jnp.float32)
    counts = jnp.einsum("rsp,rsw->rpw", hits, living).reshape(local_rows, -1)
    pool_counts = counts[:, : pool_pages * page_rows]
    arrived_counts = counts[:, pool_pages * page_rows :]
    pool_scores, pool_values = dense_scores(queries, pool, pool_counts)
    arrived_scores, arrived_values = dense_scores(queries, arrived, arrived_counts)
    tops = jnp.maximum(
        jnp.maximum(jnp.max(pool_scores, axis=-1), jnp.max(arrived_scores, axis=-1)), own_score
    )
    own_weight = jnp.exp(own_score - tops)
    sums = own_weight
    accs = own_weight.astype(jnp.bfloat16).astype(jnp.float32)[..., None] * new_values.astype(
        jnp.float32
    )[:, :, None, :]
    for scores, values, count in (
        (pool_scores, pool_values, pool_counts),
        (arrived_scores, arrived_values, arrived_counts),
    ):
        weights = jnp.exp(scores - tops[..., None])
        sums = sums + jnp.sum(weights * count[:, None, None, :], axis=-1)
        rounded = weights.astype(jnp.bfloat16).astype(jnp.float32) * count[:, None, None, :]
        accs = accs + jnp.einsum(
            "rkgt,tkd->rkgd",
            rounded,
            values.astype(jnp.float32),
            precision=lax.Precision.HIGHEST,
            preferred_element_type=jnp.float32,
        )
    attended = (accs / sums[..., None]).reshape(local_rows, query_width).astype(jnp.bfloat16)
    partner_attended = from_partner(attended, "guide", 0)
    both_attended = jnp.where(
        side == 0, jnp.stack([attended, partner_attended]), jnp.stack([partner_attended, attended])
    )
    head_half = w_out.shape[0]
    attended_part = lax.dynamic_slice_in_dim(both_attended, side * head_half, head_half, 2)
    selected = attended_part
    out_parts = jnp.einsum("grc,cd->grd", selected, w_out, preferred_element_type=jnp.float32)
    own_out = jnp.where(side == 0, out_parts[0], out_parts[1])
    other_out = jnp.where(side == 0, out_parts[1], out_parts[0]).astype(jnp.bfloat16)
    state_after = states_in + (
        own_out + from_partner(other_out, "guide", 0).astype(jnp.float32)
    )
    final = rms_scale(state_after, final_gain).astype(jnp.bfloat16)
    pair = ("guide", "x_lo")
    from_side = lax.ppermute(final, pair, [(0, 1), (3, 2)])
    from_diagonal = lax.ppermute(final, pair, [(2, 1), (1, 2)])
    from_guide = lax.ppermute(final, pair, [(2, 0), (1, 3)])
    home = lax.axis_index("x_lo") == side
    same_group = jnp.where(home, final, from_side)
    other_group = jnp.where(home, from_guide, from_diagonal)
    cond = jnp.where(side == 0, same_group, other_group).astype(jnp.float32)
    uncond = jnp.where(side == 0, other_group, same_group).astype(jnp.float32)
    combined = (uncond + guidance * (cond - uncond)).astype(jnp.bfloat16)
    gathered = lax.all_gather(combined, ("y", "z"), axis=0, tiled=False)
    gathered = gathered.reshape(
        (lax.axis_size("y"), lax.axis_size("z")) + combined.shape
    )
    core = lax.axis_index("core")
    twin = lax.ppermute(gathered, "core", [(0, 1), (1, 0)])
    mine_logits = jnp.einsum("yzrd,dv->yzrv", gathered, w_vocab, preferred_element_type=jnp.float32)
    twin_logits = jnp.einsum("yzrd,dv->yzrv", twin, w_vocab, preferred_element_type=jnp.float32)
    logits = jnp.stack(
        [
            jnp.where(core == 0, mine_logits, twin_logits),
            jnp.where(core == 0, twin_logits, mine_logits),
        ],
        axis=2,
    )
    return logits.reshape(-1, logits.shape[-1])


def solution(mesh):
    split = Mesh(mesh.devices.reshape((mesh.devices.shape[0],) + REQ_SPLIT), ("guide",) + REQ)
    in_specs = (
        P("guide", REQ, None),
        P(),
        P("guide", None),
        P("guide", None),
        P(),
        P(None, REQ),
        P("guide", REQ, None, None),
        P("guide", None),
        P("guide", None, None),
        P("guide", None, None),
    )
    out_specs = P("guide", REQ)
    return jax.shard_map(body, mesh=split, in_specs=in_specs, out_specs=out_specs, check_vma=False)
```

```python
import math

import jax
import jax.numpy as jnp
from jax import lax
from jax.sharding import Mesh
from jax.sharding import PartitionSpec as P

QH = 20
KVH = 5
HD = 64
MAXP = 8
MIGP = 2
HOP = 2
REQ = ("x_lo", "y", "z", "core")
REQ_SPLIT = (2, 4, 8, 2)


epsilon = 1e-06
guidance = 3.0


def from_partner(block, axis, bit):
    count = lax.axis_size(axis)
    route = []
    for low in range(count):
        high = low | 1 << bit
        if high != low and high < count:
            route += [(low, high), (high, low)]
    return lax.ppermute(block, axis, route)


def shifted(value, axis, steps):
    count = lax.axis_size(axis)
    pairs = [(source, (source + steps) % count) for source in range(count)]
    return lax.ppermute(value, axis, pairs)


def rms_scale(values, gain):
    return values * lax.rsqrt(jnp.mean(values * values, axis=-1, keepdims=True) + epsilon) * gain


def masked_scores(queries, page_rows, lengths):
    count = page_rows.shape[0]
    span = page_rows.shape[1]
    half_width = page_rows.shape[2] // 2
    key_rows = page_rows[:, :, :half_width].reshape(count, span, KVH, HD)
    value_rows = page_rows[:, :, half_width:].reshape(count, span, KVH, HD)
    scores = jnp.einsum(
        "rkgd,rskd->rkgs", queries, key_rows, preferred_element_type=jnp.float32
    ) * (1.0 / math.sqrt(HD))
    living = jnp.arange(span, dtype=jnp.int32)[None, :] < lengths[:, None]
    scores = jnp.where(living[:, None, None, :], scores, -jnp.inf)
    return (scores, value_rows)


def attend_all(queries, page_rows, lengths, own_score, value_new):
    scores, value_rows = masked_scores(queries, page_rows, lengths)
    highest = jnp.maximum(jnp.max(scores, axis=-1), own_score)
    weights = jnp.exp(scores - highest[..., None])
    own_weight = jnp.exp(own_score - highest)
    denominator = jnp.sum(weights, axis=-1) + own_weight
    weighted = jnp.einsum(
        "rkgs,rskd->rkgd",
        weights.astype(jnp.bfloat16),
        value_rows,
        preferred_element_type=jnp.float32,
    )
    own_rounded = own_weight.astype(jnp.bfloat16).astype(jnp.float32)
    weighted = weighted + own_rounded[..., None] * value_new.astype(jnp.float32)[:, :, None, :]
    return (highest, denominator, weighted)


def gather_pages(pool, tables):
    picked = pool[tables]
    return picked.reshape(tables.shape[0], tables.shape[1] * pool.shape[1], pool.shape[2])


def dense_scores(queries, page_rows, counts):
    count = page_rows.shape[0] * page_rows.shape[1]
    half_width = page_rows.shape[2] // 2
    flat = page_rows.reshape(count, page_rows.shape[2])
    key_rows = flat[:, :half_width].reshape(count, KVH, HD)
    value_rows = flat[:, half_width:].reshape(count, KVH, HD)
    scores = jnp.einsum(
        "rkgd,tkd->rkgt", queries, key_rows, preferred_element_type=jnp.float32
    ) * (1.0 / math.sqrt(HD))
    scores = jnp.where(counts[:, None, None, :] > 0, scores, -jnp.inf)
    return (scores, value_rows)


def body(
    hidden_in,
    attn_gain,
    w_qkv,
    w_out,
    final_gain,
    w_vocab,
    kv_pool,
    cache_len,
    page_table,
    migrations,
):
    device = lax.axis_index(REQ)
    devices = lax.axis_size(REQ)
    side = lax.axis_index("guide")
    local_rows = hidden_in.shape[1]
    group = QH // KVH
    query_width = QH * HD
    key_width = KVH * HD
    scaling = 1.0 / math.sqrt(HD)
    slots = 2 * HOP
    offsets = [number - HOP if number < HOP else number - HOP + 1 for number in range(slots)]
    states_in = hidden_in[0].astype(jnp.float32)
    normed = rms_scale(states_in, attn_gain).astype(jnp.bfloat16)
    partner_normed = from_partner(normed, "guide", 0)
    both_normed = jnp.where(
        side == 0, jnp.stack([normed, partner_normed]), jnp.stack([partner_normed, normed])
    )
    inner_half = w_qkv.shape[0]
    normed_part = lax.dynamic_slice_in_dim(both_normed, side * inner_half, inner_half, 2)
    selected = normed_part
    qkv_parts = jnp.einsum("grd,df->grf", selected, w_qkv, preferred_element_type=jnp.float32)
    own_qkv = jnp.where(side == 0, qkv_parts[0], qkv_parts[1])
    other_qkv = jnp.where(side == 0, qkv_parts[1], qkv_parts[0])
    joined = (own_qkv + from_partner(other_qkv, "guide", 0)).astype(jnp.bfloat16)
    queries = joined[:, :query_width].reshape(local_rows, KVH, group, HD)
    new_keys = joined[:, query_width : query_width + key_width].reshape(local_rows, KVH, HD)
    new_values = joined[:, query_width + key_width :].reshape(local_rows, KVH, HD)
    own_score = (
        jnp.einsum("rkgd,rkd->rkg", queries, new_keys, preferred_element_type=jnp.float32) * scaling
    )
    tables = page_table[0]
    lengths_all = cache_len[0]
    listing = migrations[0]
    pool = kv_pool[0]
    pool_pages = pool.shape[0]
    first_row = device * local_rows
    own_table = lax.dynamic_slice_in_dim(tables, first_row, local_rows, 0)
    own_lengths = lax.dynamic_slice_in_dim(lengths_all, first_row, local_rows, 0)
    global_ids = first_row + jnp.arange(local_rows, dtype=jnp.int32)
    matches = listing[None, :, 0] == global_ids[:, None]
    is_moved = jnp.any(matches, axis=1)
    old_owner = jnp.sum(jnp.where(matches, listing[None, :, 1], 0), axis=1)
    distance = jnp.remainder(device - old_owner, devices)
    slot_of = jnp.where(distance <= HOP, HOP + distance - 1, HOP - (devices - distance))
    targets = jnp.remainder(device + jnp.array(offsets, jnp.int32), devices)
    holding = (listing[None, :, 1] == device) & (listing[None, :, 2] == targets[:, None])
    held_request = jnp.sum(jnp.where(holding, listing[None, :, 0], 0), axis=1)
    request_hit = jnp.arange(tables.shape[0], dtype=jnp.int32)[None, :] == held_request[:, None]
    sent_ids = jnp.sum(jnp.where(request_hit[:, :, None], tables[None, :, :MIGP], 0), axis=1)
    page_hit = (
        sent_ids[:, :, None] == jnp.arange(pool_pages, dtype=jnp.int32)[None, None, :]
    ).astype(jnp.bfloat16)
    pages_sent = jnp.einsum(
        "smp,pwc->smwc", page_hit, pool, preferred_element_type=jnp.float32
    ).astype(jnp.bfloat16)
    arrivals = [shifted(pages_sent[number], REQ, offsets[number]) for number in range(slots)]
    arrived = jnp.concatenate(arrivals, axis=0)
    page_column = jnp.minimum(jnp.arange(MAXP, dtype=jnp.int32), MIGP - 1)
    moved_pages = pool_pages + slot_of[:, None] * MIGP + page_column[None, :]
    used_table = jnp.where(is_moved[:, None], moved_pages, own_table)
    page_rows = pool.shape[1]
    living = (
        jnp.arange(MAXP, dtype=jnp.int32)[:, None] * page_rows
        + jnp.arange(page_rows, dtype=jnp.int32)[None, :]
    )[None] < own_lengths[:, None, None]
    living = living.astype(jnp.float32)
    all_pages = jnp.arange(pool_pages + arrived.shape[0], dtype=jnp.int32)
    hits = (used_table[:, :, None] == all_pages[None, None, :]).astype(jnp.float32)
    counts = jnp.einsum("rsp,rsw->rpw", hits, living).reshape(local_rows, -1)
    pool_counts = counts[:, : pool_pages * page_rows]
    arrived_counts = counts[:, pool_pages * page_rows :]
    pool_scores, pool_values = dense_scores(queries, pool, pool_counts)
    arrived_scores, arrived_values = dense_scores(queries, arrived, arrived_counts)
    tops = jnp.maximum(
        jnp.maximum(jnp.max(pool_scores, axis=-1), jnp.max(arrived_scores, axis=-1)), own_score
    )
    own_weight = jnp.exp(own_score - tops)
    sums = own_weight
    accs = own_weight.astype(jnp.bfloat16).astype(jnp.float32)[..., None] * new_values.astype(
        jnp.float32
    )[:, :, None, :]
    for scores, values, count in (
        (pool_scores, pool_values, pool_counts),
        (arrived_scores, arrived_values, arrived_counts),
    ):
        weights = jnp.exp(scores - tops[..., None])
        sums = sums + jnp.sum(weights * count[:, None, None, :], axis=-1)
        rounded = weights.astype(jnp.bfloat16).astype(jnp.float32) * count[:, None, None, :]
        accs = accs + jnp.einsum(
            "rkgt,tkd->rkgd",
            rounded,
            values.astype(jnp.float32),
            precision=lax.Precision.HIGHEST,
            preferred_element_type=jnp.float32,
        )
    attended = (accs / sums[..., None]).reshape(local_rows, query_width).astype(jnp.bfloat16)
    head_half = w_out.shape[0]
    partner_w_out = from_partner(w_out, "guide", 0)
    partner_w_out, attended = lax.optimization_barrier((partner_w_out, attended))
    own_heads = lax.dynamic_slice_in_dim(attended, side * head_half, head_half, 1)
    other_heads = lax.dynamic_slice_in_dim(attended, (1 - side) * head_half, head_half, 1)
    state_after = states_in + (
        jnp.dot(own_heads, w_out, preferred_element_type=jnp.float32)
        + jnp.dot(other_heads, partner_w_out, preferred_element_type=jnp.float32)
    )
    final = rms_scale(state_after, final_gain).astype(jnp.bfloat16)
    pair = ("guide", "x_lo")
    from_side = lax.ppermute(final, pair, [(0, 1), (3, 2)])
    from_diagonal = lax.ppermute(final, pair, [(2, 1), (1, 2)])
    from_guide = lax.ppermute(final, pair, [(2, 0), (1, 3)])
    home = lax.axis_index("x_lo") == side
    same_group = jnp.where(home, final, from_side)
    other_group = jnp.where(home, from_guide, from_diagonal)
    cond = jnp.where(side == 0, same_group, other_group).astype(jnp.float32)
    uncond = jnp.where(side == 0, other_group, same_group).astype(jnp.float32)
    combined = (uncond + guidance * (cond - uncond)).astype(jnp.bfloat16)
    gathered = lax.all_gather(combined, "y", axis=0, tiled=False)
    gathered = lax.all_gather(gathered, "z", axis=1, tiled=False)
    core = lax.axis_index("core")
    twin = lax.ppermute(gathered, "core", [(0, 1), (1, 0)])
    mine_logits = jnp.einsum("yzrd,dv->yzrv", gathered, w_vocab, preferred_element_type=jnp.float32)
    twin_logits = jnp.einsum("yzrd,dv->yzrv", twin, w_vocab, preferred_element_type=jnp.float32)
    logits = jnp.stack(
        [
            jnp.where(core == 0, mine_logits, twin_logits),
            jnp.where(core == 0, twin_logits, mine_logits),
        ],
        axis=2,
    )
    return logits.reshape(-1, logits.shape[-1])


def solution(mesh):
    split = Mesh(mesh.devices.reshape((mesh.devices.shape[0],) + REQ_SPLIT), ("guide",) + REQ)
    in_specs = (
        P("guide", REQ, None),
        P(),
        P("guide", None),
        P("guide", None),
        P(),
        P(None, REQ),
        P("guide", REQ, None, None),
        P("guide", None),
        P("guide", None, None),
        P("guide", None, None),
    )
    out_specs = P("guide", REQ)
    return jax.shard_map(body, mesh=split, in_specs=in_specs, out_specs=out_specs, check_vma=False)
```

```python
import math

import jax
import jax.numpy as jnp
from jax import lax
from jax.sharding import Mesh
from jax.sharding import PartitionSpec as P

QH = 20
KVH = 5
HD = 64
MAXP = 8
MIGP = 2
HOP = 2
REQ = ("x_lo", "y", "z", "core")
REQ_SPLIT = (2, 4, 8, 2)


epsilon = 1e-06
guidance = 3.0


def from_partner(block, axis, bit):
    count = lax.axis_size(axis)
    route = []
    for low in range(count):
        high = low | 1 << bit
        if high != low and high < count:
            route += [(low, high), (high, low)]
    return lax.ppermute(block, axis, route)


def shifted(value, axis, steps):
    count = lax.axis_size(axis)
    pairs = [(source, (source + steps) % count) for source in range(count)]
    return lax.ppermute(value, axis, pairs)


def rms_scale(values, gain):
    return values * lax.rsqrt(jnp.mean(values * values, axis=-1, keepdims=True) + epsilon) * gain


def masked_scores(queries, page_rows, lengths):
    count = page_rows.shape[0]
    span = page_rows.shape[1]
    half_width = page_rows.shape[2] // 2
    key_rows = page_rows[:, :, :half_width].reshape(count, span, KVH, HD)
    value_rows = page_rows[:, :, half_width:].reshape(count, span, KVH, HD)
    scores = jnp.einsum(
        "rkgd,rskd->rkgs", queries, key_rows, preferred_element_type=jnp.float32
    ) * (1.0 / math.sqrt(HD))
    living = jnp.arange(span, dtype=jnp.int32)[None, :] < lengths[:, None]
    scores = jnp.where(living[:, None, None, :], scores, -jnp.inf)
    return (scores, value_rows)


def attend_all(queries, page_rows, lengths, own_score, value_new):
    scores, value_rows = masked_scores(queries, page_rows, lengths)
    highest = jnp.maximum(jnp.max(scores, axis=-1), own_score)
    weights = jnp.exp(scores - highest[..., None])
    own_weight = jnp.exp(own_score - highest)
    denominator = jnp.sum(weights, axis=-1) + own_weight
    weighted = jnp.einsum(
        "rkgs,rskd->rkgd",
        weights.astype(jnp.bfloat16),
        value_rows,
        preferred_element_type=jnp.float32,
    )
    own_rounded = own_weight.astype(jnp.bfloat16).astype(jnp.float32)
    weighted = weighted + own_rounded[..., None] * value_new.astype(jnp.float32)[:, :, None, :]
    return (highest, denominator, weighted)


def gather_pages(pool, tables):
    picked = pool[tables]
    return picked.reshape(tables.shape[0], tables.shape[1] * pool.shape[1], pool.shape[2])


def dense_scores(blocked, page_rows, counts):
    count = page_rows.shape[0] * page_rows.shape[1]
    half_width = page_rows.shape[2] // 2
    flat = page_rows.reshape(count, page_rows.shape[2])
    key_rows = flat[:, :half_width]
    value_rows = flat[:, half_width:]
    scores = jnp.einsum(
        "rkgc,tc->rkgt", blocked, key_rows, preferred_element_type=jnp.float32
    ) * (1.0 / math.sqrt(HD))
    scores = jnp.where(counts[:, None, None, :] > 0, scores, -jnp.inf)
    return (scores, value_rows)


def body(
    hidden_in,
    attn_gain,
    w_qkv,
    w_out,
    final_gain,
    w_vocab,
    kv_pool,
    cache_len,
    page_table,
    migrations,
):
    device = lax.axis_index(REQ)
    devices = lax.axis_size(REQ)
    side = lax.axis_index("guide")
    local_rows = hidden_in.shape[1]
    group = QH // KVH
    query_width = QH * HD
    key_width = KVH * HD
    scaling = 1.0 / math.sqrt(HD)
    slots = 2 * HOP
    offsets = [number - HOP if number < HOP else number - HOP + 1 for number in range(slots)]
    states_in = hidden_in[0].astype(jnp.float32)
    normed = rms_scale(states_in, attn_gain).astype(jnp.bfloat16)
    partner_normed = from_partner(normed, "guide", 0)
    both_normed = jnp.where(
        side == 0, jnp.stack([normed, partner_normed]), jnp.stack([partner_normed, normed])
    )
    inner_half = w_qkv.shape[0]
    normed_part = lax.dynamic_slice_in_dim(both_normed, side * inner_half, inner_half, 2)
    selected = normed_part
    qkv_parts = jnp.einsum("grd,df->grf", selected, w_qkv, preferred_element_type=jnp.float32)
    own_qkv = jnp.where(side == 0, qkv_parts[0], qkv_parts[1])
    other_qkv = jnp.where(side == 0, qkv_parts[1], qkv_parts[0])
    joined = (own_qkv + from_partner(other_qkv, "guide", 0)).astype(jnp.bfloat16)
    queries = joined[:, :query_width].reshape(local_rows, KVH, group, HD)
    new_keys = joined[:, query_width : query_width + key_width].reshape(local_rows, KVH, HD)
    new_values = joined[:, query_width + key_width :].reshape(local_rows, KVH, HD)
    own_score = (
        jnp.einsum("rkgd,rkd->rkg", queries, new_keys, preferred_element_type=jnp.float32) * scaling
    )
    tables = page_table[0]
    lengths_all = cache_len[0]
    listing = migrations[0]
    pool = kv_pool[0]
    pool_pages = pool.shape[0]
    first_row = device * local_rows
    own_table = lax.dynamic_slice_in_dim(tables, first_row, local_rows, 0)
    own_lengths = lax.dynamic_slice_in_dim(lengths_all, first_row, local_rows, 0)
    global_ids = first_row + jnp.arange(local_rows, dtype=jnp.int32)
    matches = listing[None, :, 0] == global_ids[:, None]
    is_moved = jnp.any(matches, axis=1)
    old_owner = jnp.sum(jnp.where(matches, listing[None, :, 1], 0), axis=1)
    distance = jnp.remainder(device - old_owner, devices)
    slot_of = jnp.where(distance <= HOP, HOP + distance - 1, HOP - (devices - distance))
    targets = jnp.remainder(device + jnp.array(offsets, jnp.int32), devices)
    holding = (listing[None, :, 1] == device) & (listing[None, :, 2] == targets[:, None])
    held_request = jnp.sum(jnp.where(holding, listing[None, :, 0], 0), axis=1)
    request_hit = jnp.arange(tables.shape[0], dtype=jnp.int32)[None, :] == held_request[:, None]
    sent_ids = jnp.sum(jnp.where(request_hit[:, :, None], tables[None, :, :MIGP], 0), axis=1)
    page_hit = (
        sent_ids[:, :, None] == jnp.arange(pool_pages, dtype=jnp.int32)[None, None, :]
    ).astype(jnp.bfloat16)
    pages_sent = jnp.einsum(
        "smp,pwc->smwc", page_hit, pool, preferred_element_type=jnp.float32
    ).astype(jnp.bfloat16)
    arrivals = [shifted(pages_sent[number], REQ, offsets[number]) for number in range(slots)]
    arrived = jnp.concatenate(arrivals, axis=0)
    page_column = jnp.minimum(jnp.arange(MAXP, dtype=jnp.int32), MIGP - 1)
    moved_pages = pool_pages + slot_of[:, None] * MIGP + page_column[None, :]
    used_table = jnp.where(is_moved[:, None], moved_pages, own_table)
    page_rows = pool.shape[1]
    living = (
        jnp.arange(MAXP, dtype=jnp.int32)[:, None] * page_rows
        + jnp.arange(page_rows, dtype=jnp.int32)[None, :]
    )[None] < own_lengths[:, None, None]
    living = living.astype(jnp.float32)
    all_pages = jnp.arange(pool_pages + arrived.shape[0], dtype=jnp.int32)
    hits = (used_table[:, :, None] == all_pages[None, None, :]).astype(jnp.float32)
    counts = jnp.einsum("rsp,rsw->rpw", hits, living).reshape(local_rows, -1)
    pool_counts = counts[:, : pool_pages * page_rows]
    arrived_counts = counts[:, pool_pages * page_rows :]
    head_match = jnp.arange(KVH)[:, None] == jnp.arange(KVH)[None, :]
    blocked = jnp.where(
        head_match[None, :, None, :, None], queries[:, :, :, None, :], jnp.zeros((), queries.dtype)
    ).reshape(local_rows, KVH, group, key_width)
    pool_scores, pool_values = dense_scores(blocked, pool, pool_counts)
    arrived_scores, arrived_values = dense_scores(blocked, arrived, arrived_counts)
    spread = jnp.zeros((local_rows, KVH, group, key_width), jnp.float32)
    tops = jnp.maximum(
        jnp.maximum(jnp.max(pool_scores, axis=-1), jnp.max(arrived_scores, axis=-1)), own_score
    )
    own_weight = jnp.exp(own_score - tops)
    sums = own_weight
    accs = own_weight.astype(jnp.bfloat16).astype(jnp.float32)[..., None] * new_values.astype(
        jnp.float32
    )[:, :, None, :]
    for scores, values, count in (
        (pool_scores, pool_values, pool_counts),
        (arrived_scores, arrived_values, arrived_counts),
    ):
        weights = jnp.exp(scores - tops[..., None])
        sums = sums + jnp.sum(weights * count[:, None, None, :], axis=-1)
        rounded = weights.astype(jnp.bfloat16).astype(jnp.float32) * count[:, None, None, :]
        high = rounded.astype(jnp.bfloat16)
        low = (rounded - high.astype(jnp.float32)).astype(jnp.bfloat16)
        for piece in (high, low):
            spread = spread + jnp.einsum(
                "rkgt,tc->rkgc", piece, values, preferred_element_type=jnp.float32
            )
    spread = spread.reshape(local_rows, KVH, group, KVH, HD)
    accs = accs + jnp.sum(
        jnp.where(head_match[None, :, None, :, None], spread, 0.0), axis=3
    )
    attended = (accs / sums[..., None]).reshape(local_rows, query_width).astype(jnp.bfloat16)
    partner_attended = from_partner(attended, "guide", 0)
    both_attended = jnp.where(
        side == 0, jnp.stack([attended, partner_attended]), jnp.stack([partner_attended, attended])
    )
    head_half = w_out.shape[0]
    attended_part = lax.dynamic_slice_in_dim(both_attended, side * head_half, head_half, 2)
    selected = attended_part
    out_parts = jnp.einsum("grc,cd->grd", selected, w_out, preferred_element_type=jnp.float32)
    own_out = jnp.where(side == 0, out_parts[0], out_parts[1])
    other_out = jnp.where(side == 0, out_parts[1], out_parts[0]).astype(jnp.bfloat16)
    state_after = states_in + (
        own_out + from_partner(other_out, "guide", 0).astype(jnp.float32)
    )
    final = rms_scale(state_after, final_gain).astype(jnp.bfloat16)
    pair = ("guide", "x_lo")
    from_side = lax.ppermute(final, pair, [(0, 1), (3, 2)])
    from_diagonal = lax.ppermute(final, pair, [(2, 1), (1, 2)])
    from_guide = lax.ppermute(final, pair, [(2, 0), (1, 3)])
    home = lax.axis_index("x_lo") == side
    same_group = jnp.where(home, final, from_side)
    other_group = jnp.where(home, from_guide, from_diagonal)
    cond = jnp.where(side == 0, same_group, other_group).astype(jnp.float32)
    uncond = jnp.where(side == 0, other_group, same_group).astype(jnp.float32)
    combined = (uncond + guidance * (cond - uncond)).astype(jnp.bfloat16)
    gathered = lax.all_gather(combined, "y", axis=0, tiled=False)
    gathered = lax.all_gather(gathered, "z", axis=1, tiled=False)
    core = lax.axis_index("core")
    twin = lax.ppermute(gathered, "core", [(0, 1), (1, 0)])
    mine_logits = jnp.einsum("yzrd,dv->yzrv", gathered, w_vocab, preferred_element_type=jnp.float32)
    twin_logits = jnp.einsum("yzrd,dv->yzrv", twin, w_vocab, preferred_element_type=jnp.float32)
    logits = jnp.stack(
        [
            jnp.where(core == 0, mine_logits, twin_logits),
            jnp.where(core == 0, twin_logits, mine_logits),
        ],
        axis=2,
    )
    return logits.reshape(-1, logits.shape[-1])


def solution(mesh):
    split = Mesh(mesh.devices.reshape((mesh.devices.shape[0],) + REQ_SPLIT), ("guide",) + REQ)
    in_specs = (
        P("guide", REQ, None),
        P(),
        P("guide", None),
        P("guide", None),
        P(),
        P(None, REQ),
        P("guide", REQ, None, None),
        P("guide", None),
        P("guide", None, None),
        P("guide", None, None),
    )
    out_specs = P("guide", REQ)
    return jax.shard_map(body, mesh=split, in_specs=in_specs, out_specs=out_specs, check_vma=False)
```

```python
import math

import jax
import jax.numpy as jnp
from jax import lax
from jax.sharding import Mesh
from jax.sharding import PartitionSpec as P

QH = 20
KVH = 5
HD = 64
MAXP = 8
MIGP = 2
HOP = 2
REQ = ("x_lo", "y", "z", "core")
REQ_SPLIT = (2, 4, 8, 2)


epsilon = 1e-06
guidance = 3.0


def from_partner(block, axis, bit):
    count = lax.axis_size(axis)
    route = []
    for low in range(count):
        high = low | 1 << bit
        if high != low and high < count:
            route += [(low, high), (high, low)]
    return lax.ppermute(block, axis, route)


def shifted(value, axis, steps):
    count = lax.axis_size(axis)
    pairs = [(source, (source + steps) % count) for source in range(count)]
    return lax.ppermute(value, axis, pairs)


def rms_scale(values, gain):
    return values * lax.rsqrt(jnp.mean(values * values, axis=-1, keepdims=True) + epsilon) * gain


def masked_scores(queries, page_rows, lengths):
    count = page_rows.shape[0]
    span = page_rows.shape[1]
    half_width = page_rows.shape[2] // 2
    key_rows = page_rows[:, :, :half_width].reshape(count, span, KVH, HD)
    value_rows = page_rows[:, :, half_width:].reshape(count, span, KVH, HD)
    scores = jnp.einsum(
        "rkgd,rskd->rkgs", queries, key_rows, preferred_element_type=jnp.float32
    ) * (1.0 / math.sqrt(HD))
    living = jnp.arange(span, dtype=jnp.int32)[None, :] < lengths[:, None]
    scores = jnp.where(living[:, None, None, :], scores, -jnp.inf)
    return (scores, value_rows)


def attend_all(queries, page_rows, lengths, own_score, value_new):
    scores, value_rows = masked_scores(queries, page_rows, lengths)
    highest = jnp.maximum(jnp.max(scores, axis=-1), own_score)
    weights = jnp.exp(scores - highest[..., None])
    own_weight = jnp.exp(own_score - highest)
    denominator = jnp.sum(weights, axis=-1) + own_weight
    weighted = jnp.einsum(
        "rkgs,rskd->rkgd",
        weights.astype(jnp.bfloat16),
        value_rows,
        preferred_element_type=jnp.float32,
    )
    own_rounded = own_weight.astype(jnp.bfloat16).astype(jnp.float32)
    weighted = weighted + own_rounded[..., None] * value_new.astype(jnp.float32)[:, :, None, :]
    return (highest, denominator, weighted)


def gather_pages(pool, tables):
    picked = pool[tables]
    return picked.reshape(tables.shape[0], tables.shape[1] * pool.shape[1], pool.shape[2])


def dense_scores(queries, page_rows, counts):
    count = page_rows.shape[0] * page_rows.shape[1]
    half_width = page_rows.shape[2] // 2
    flat = page_rows.reshape(count, page_rows.shape[2])
    key_rows = flat[:, :half_width].reshape(count, KVH, HD)
    value_rows = flat[:, half_width:].reshape(count, KVH, HD)
    scores = jnp.einsum(
        "rkgd,tkd->rkgt", queries, key_rows, preferred_element_type=jnp.float32
    ) * (1.0 / math.sqrt(HD))
    scores = jnp.where(counts[:, None, None, :] > 0, scores, -jnp.inf)
    return (scores, value_rows)


def body(
    hidden_in,
    attn_gain,
    w_qkv,
    w_out,
    final_gain,
    w_vocab,
    kv_pool,
    cache_len,
    page_table,
    migrations,
):
    device = lax.axis_index(REQ)
    devices = lax.axis_size(REQ)
    side = lax.axis_index("guide")
    local_rows = hidden_in.shape[1]
    group = QH // KVH
    query_width = QH * HD
    key_width = KVH * HD
    scaling = 1.0 / math.sqrt(HD)
    slots = 2 * HOP
    offsets = [number - HOP if number < HOP else number - HOP + 1 for number in range(slots)]
    states_in = hidden_in[0].astype(jnp.float32)
    normed = rms_scale(states_in, attn_gain).astype(jnp.bfloat16)
    partner_normed = from_partner(normed, "guide", 0)
    both_normed = jnp.where(
        side == 0, jnp.stack([normed, partner_normed]), jnp.stack([partner_normed, normed])
    )
    inner_half = w_qkv.shape[0]
    normed_part = lax.dynamic_slice_in_dim(both_normed, side * inner_half, inner_half, 2)
    selected = normed_part
    qkv_parts = jnp.einsum("grd,df->grf", selected, w_qkv, preferred_element_type=jnp.float32)
    own_qkv = jnp.where(side == 0, qkv_parts[0], qkv_parts[1])
    other_qkv = jnp.where(side == 0, qkv_parts[1], qkv_parts[0])
    joined = (own_qkv + from_partner(other_qkv, "guide", 0)).astype(jnp.bfloat16)
    queries = joined[:, :query_width].reshape(local_rows, KVH, group, HD)
    new_keys = joined[:, query_width : query_width + key_width].reshape(local_rows, KVH, HD)
    new_values = joined[:, query_width + key_width :].reshape(local_rows, KVH, HD)
    own_score = (
        jnp.einsum("rkgd,rkd->rkg", queries, new_keys, preferred_element_type=jnp.float32) * scaling
    )
    tables = page_table[0]
    lengths_all = cache_len[0]
    listing = migrations[0]
    pool = kv_pool[0]
    pool_pages = pool.shape[0]
    first_row = device * local_rows
    own_table = lax.dynamic_slice_in_dim(tables, first_row, local_rows, 0)
    own_lengths = lax.dynamic_slice_in_dim(lengths_all, first_row, local_rows, 0)
    global_ids = first_row + jnp.arange(local_rows, dtype=jnp.int32)
    matches = listing[None, :, 0] == global_ids[:, None]
    is_moved = jnp.any(matches, axis=1)
    old_owner = jnp.sum(jnp.where(matches, listing[None, :, 1], 0), axis=1)
    distance = jnp.remainder(device - old_owner, devices)
    slot_of = jnp.where(distance <= HOP, HOP + distance - 1, HOP - (devices - distance))
    targets = jnp.remainder(device + jnp.array(offsets, jnp.int32), devices)
    holding = (listing[None, :, 1] == device) & (listing[None, :, 2] == targets[:, None])
    held_request = jnp.sum(jnp.where(holding, listing[None, :, 0], 0), axis=1)
    request_hit = jnp.arange(tables.shape[0], dtype=jnp.int32)[None, :] == held_request[:, None]
    sent_ids = jnp.sum(jnp.where(request_hit[:, :, None], tables[None, :, :MIGP], 0), axis=1)
    page_hit = (
        sent_ids[:, :, None] == jnp.arange(pool_pages, dtype=jnp.int32)[None, None, :]
    ).astype(jnp.bfloat16)
    pages_sent = jnp.einsum(
        "smp,pwc->smwc", page_hit, pool, preferred_element_type=jnp.float32
    ).astype(jnp.bfloat16)
    arrivals = [shifted(pages_sent[number], REQ, offsets[number]) for number in range(slots)]
    arrived = jnp.concatenate(arrivals, axis=0)
    page_column = jnp.minimum(jnp.arange(MAXP, dtype=jnp.int32), MIGP - 1)
    moved_pages = pool_pages + slot_of[:, None] * MIGP + page_column[None, :]
    used_table = jnp.where(is_moved[:, None], moved_pages, own_table)
    page_rows = pool.shape[1]
    living = (
        jnp.arange(MAXP, dtype=jnp.int32)[:, None] * page_rows
        + jnp.arange(page_rows, dtype=jnp.int32)[None, :]
    )[None] < own_lengths[:, None, None]
    living = living.astype(jnp.float32)
    all_pages = jnp.arange(pool_pages + arrived.shape[0], dtype=jnp.int32)
    hits = (used_table[:, :, None] == all_pages[None, None, :]).astype(jnp.float32)
    counts = jnp.einsum("rsp,rsw->rpw", hits, living).reshape(local_rows, -1)
    pool_counts = counts[:, : pool_pages * page_rows]
    arrived_counts = counts[:, pool_pages * page_rows :]
    pool_scores, pool_values = dense_scores(queries, pool, pool_counts)
    arrived_scores, arrived_values = dense_scores(queries, arrived, arrived_counts)
    tops = jnp.maximum(
        jnp.maximum(jnp.max(pool_scores, axis=-1), jnp.max(arrived_scores, axis=-1)), own_score
    )
    own_weight = jnp.exp(own_score - tops)
    sums = own_weight
    accs = own_weight.astype(jnp.bfloat16).astype(jnp.float32)[..., None] * new_values.astype(
        jnp.float32
    )[:, :, None, :]
    for scores, values, count in (
        (pool_scores, pool_values, pool_counts),
        (arrived_scores, arrived_values, arrived_counts),
    ):
        weights = jnp.exp(scores - tops[..., None])
        sums = sums + jnp.sum(weights * count[:, None, None, :], axis=-1)
        rounded = weights.astype(jnp.bfloat16).astype(jnp.float32) * count[:, None, None, :]
        accs = accs + jnp.einsum(
            "rkgt,tkd->rkgd",
            rounded,
            values.astype(jnp.float32),
            precision=lax.Precision.HIGHEST,
            preferred_element_type=jnp.float32,
        )
    attended = (accs / sums[..., None]).reshape(local_rows, query_width).astype(jnp.bfloat16)
    partner_attended = from_partner(attended, "guide", 0)
    both_attended = jnp.where(
        side == 0, jnp.stack([attended, partner_attended]), jnp.stack([partner_attended, attended])
    )
    head_half = w_out.shape[0]
    attended_part = lax.dynamic_slice_in_dim(both_attended, side * head_half, head_half, 2)
    selected = attended_part
    out_parts = jnp.einsum("grc,cd->grd", selected, w_out, preferred_element_type=jnp.float32)
    own_out = jnp.where(side == 0, out_parts[0], out_parts[1])
    other_out = jnp.where(side == 0, out_parts[1], out_parts[0]).astype(jnp.bfloat16)
    state_after = states_in + (
        own_out + from_partner(other_out, "guide", 0).astype(jnp.float32)
    )
    final = rms_scale(state_after, final_gain).astype(jnp.bfloat16)
    pair = ("guide", "x_lo")
    from_side = lax.ppermute(final, pair, [(0, 1), (3, 2)])
    from_diagonal = lax.ppermute(final, pair, [(2, 1), (1, 2)])
    from_guide = lax.ppermute(final, pair, [(2, 0), (1, 3)])
    home = lax.axis_index("x_lo") == side
    same_group = jnp.where(home, final, from_side)
    other_group = jnp.where(home, from_guide, from_diagonal)
    cond = jnp.where(side == 0, same_group, other_group).astype(jnp.float32)
    uncond = jnp.where(side == 0, other_group, same_group).astype(jnp.float32)
    combined = (uncond + guidance * (cond - uncond)).astype(jnp.bfloat16)
    y_index = lax.axis_index("y")
    y_count = lax.axis_size("y")
    by_distance = [combined] + [
        shifted(combined, "y", distance) for distance in range(1, y_count)
    ]
    in_order = []
    for position in range(y_count):
        distance = jnp.remainder(position - y_index, y_count)
        pick = by_distance[0]
        for step in range(1, y_count):
            pick = jnp.where(distance == y_count - step, by_distance[step], pick)
        in_order.append(pick)
    gathered = jnp.stack(in_order)
    gathered = lax.all_gather(gathered, "z", axis=1, tiled=False)
    core = lax.axis_index("core")
    cores = lax.axis_size("core")
    twin = lax.ppermute(gathered, "core", [(0, 1), (1, 0)])
    mine_logits = jnp.einsum("yzrd,dv->yzrv", gathered, w_vocab, preferred_element_type=jnp.float32)
    twin_logits = jnp.einsum("yzrd,dv->yzrv", twin, w_vocab, preferred_element_type=jnp.float32)
    logits = jnp.zeros(
        mine_logits.shape[:2] + (cores,) + mine_logits.shape[2:], jnp.float32
    )
    logits = lax.dynamic_update_slice_in_dim(logits, mine_logits[:, :, None], core, 2)
    logits = lax.dynamic_update_slice_in_dim(logits, twin_logits[:, :, None], 1 - core, 2)
    return logits.reshape(-1, logits.shape[-1])


def solution(mesh):
    split = Mesh(mesh.devices.reshape((mesh.devices.shape[0],) + REQ_SPLIT), ("guide",) + REQ)
    in_specs = (
        P("guide", REQ, None),
        P(),
        P("guide", None),
        P("guide", None),
        P(),
        P(None, REQ),
        P("guide", REQ, None, None),
        P("guide", None),
        P("guide", None, None),
        P("guide", None, None),
    )
    out_specs = P("guide", REQ)
    return jax.shard_map(body, mesh=split, in_specs=in_specs, out_specs=out_specs, check_vma=False)
```

```python
import math

import jax
import jax.numpy as jnp
from jax import lax
from jax.sharding import Mesh
from jax.sharding import PartitionSpec as P

QH = 20
KVH = 5
HD = 64
MAXP = 8
MIGP = 2
HOP = 2
REQ = ("x_lo", "y", "z", "core")
REQ_SPLIT = (2, 4, 8, 2)


epsilon = 1e-06
guidance = 3.0


def from_partner(block, axis, bit):
    count = lax.axis_size(axis)
    route = []
    for low in range(count):
        high = low | 1 << bit
        if high != low and high < count:
            route += [(low, high), (high, low)]
    return lax.ppermute(block, axis, route)


def shifted(value, axis, steps):
    count = lax.axis_size(axis)
    pairs = [(source, (source + steps) % count) for source in range(count)]
    return lax.ppermute(value, axis, pairs)


def rms_scale(values, gain):
    return values * lax.rsqrt(jnp.mean(values * values, axis=-1, keepdims=True) + epsilon) * gain


def masked_scores(queries, page_rows, lengths):
    count = page_rows.shape[0]
    span = page_rows.shape[1]
    half_width = page_rows.shape[2] // 2
    key_rows = page_rows[:, :, :half_width].reshape(count, span, KVH, HD)
    value_rows = page_rows[:, :, half_width:].reshape(count, span, KVH, HD)
    scores = jnp.einsum(
        "rkgd,rskd->rkgs", queries, key_rows, preferred_element_type=jnp.float32
    ) * (1.0 / math.sqrt(HD))
    living = jnp.arange(span, dtype=jnp.int32)[None, :] < lengths[:, None]
    scores = jnp.where(living[:, None, None, :], scores, -jnp.inf)
    return (scores, value_rows)


def attend_all(queries, page_rows, lengths, own_score, value_new):
    scores, value_rows = masked_scores(queries, page_rows, lengths)
    highest = jnp.maximum(jnp.max(scores, axis=-1), own_score)
    weights = jnp.exp(scores - highest[..., None])
    own_weight = jnp.exp(own_score - highest)
    denominator = jnp.sum(weights, axis=-1) + own_weight
    weighted = jnp.einsum(
        "rkgs,rskd->rkgd",
        weights.astype(jnp.bfloat16),
        value_rows,
        preferred_element_type=jnp.float32,
    )
    own_rounded = own_weight.astype(jnp.bfloat16).astype(jnp.float32)
    weighted = weighted + own_rounded[..., None] * value_new.astype(jnp.float32)[:, :, None, :]
    return (highest, denominator, weighted)


def gather_pages(pool, tables):
    picked = pool[tables]
    return picked.reshape(tables.shape[0], tables.shape[1] * pool.shape[1], pool.shape[2])


def dense_scores(queries, page_rows, counts):
    count = page_rows.shape[0] * page_rows.shape[1]
    half_width = page_rows.shape[2] // 2
    flat = page_rows.reshape(count, page_rows.shape[2])
    key_rows = flat[:, :half_width].reshape(count, KVH, HD)
    value_rows = flat[:, half_width:].reshape(count, KVH, HD)
    scores = jnp.einsum(
        "rkgd,tkd->rkgt", queries, key_rows, preferred_element_type=jnp.float32
    ) * (1.0 / math.sqrt(HD))
    scores = jnp.where(counts[:, None, None, :] > 0, scores, -jnp.inf)
    return (scores, value_rows)


def body(
    hidden_in,
    attn_gain,
    w_qkv,
    w_out,
    final_gain,
    w_vocab,
    kv_pool,
    cache_len,
    page_table,
    migrations,
):
    device = lax.axis_index(REQ)
    devices = lax.axis_size(REQ)
    side = lax.axis_index("guide")
    local_rows = hidden_in.shape[1]
    group = QH // KVH
    query_width = QH * HD
    key_width = KVH * HD
    scaling = 1.0 / math.sqrt(HD)
    slots = 2 * HOP
    offsets = [number - HOP if number < HOP else number - HOP + 1 for number in range(slots)]
    states_in = hidden_in[0].astype(jnp.float32)
    normed = rms_scale(states_in, attn_gain).astype(jnp.bfloat16)
    partner_normed = from_partner(normed, "guide", 0)
    both_normed = jnp.where(
        side == 0, jnp.stack([normed, partner_normed]), jnp.stack([partner_normed, normed])
    )
    inner_half = w_qkv.shape[0]
    normed_part = lax.dynamic_slice_in_dim(both_normed, side * inner_half, inner_half, 2)
    selected = normed_part
    qkv_parts = jnp.einsum("grd,df->grf", selected, w_qkv, preferred_element_type=jnp.float32)
    own_qkv = jnp.where(side == 0, qkv_parts[0], qkv_parts[1])
    other_qkv = jnp.where(side == 0, qkv_parts[1], qkv_parts[0])
    joined = (own_qkv + from_partner(other_qkv, "guide", 0)).astype(jnp.bfloat16)
    queries = joined[:, :query_width].reshape(local_rows, KVH, group, HD)
    new_keys = joined[:, query_width : query_width + key_width].reshape(local_rows, KVH, HD)
    new_values = joined[:, query_width + key_width :].reshape(local_rows, KVH, HD)
    own_score = (
        jnp.einsum("rkgd,rkd->rkg", queries, new_keys, preferred_element_type=jnp.float32) * scaling
    )
    tables = page_table[0]
    lengths_all = cache_len[0]
    listing = migrations[0]
    pool = kv_pool[0]
    pool_pages = pool.shape[0]
    first_row = device * local_rows
    own_table = lax.dynamic_slice_in_dim(tables, first_row, local_rows, 0)
    own_lengths = lax.dynamic_slice_in_dim(lengths_all, first_row, local_rows, 0)
    global_ids = first_row + jnp.arange(local_rows, dtype=jnp.int32)
    matches = listing[None, :, 0] == global_ids[:, None]
    is_moved = jnp.any(matches, axis=1)
    old_owner = jnp.sum(jnp.where(matches, listing[None, :, 1], 0), axis=1)
    distance = jnp.remainder(device - old_owner, devices)
    slot_of = jnp.where(distance <= HOP, HOP + distance - 1, HOP - (devices - distance))
    targets = jnp.remainder(device + jnp.array(offsets, jnp.int32), devices)
    holding = (listing[None, :, 1] == device) & (listing[None, :, 2] == targets[:, None])
    held_request = jnp.sum(jnp.where(holding, listing[None, :, 0], 0), axis=1)
    request_hit = jnp.arange(tables.shape[0], dtype=jnp.int32)[None, :] == held_request[:, None]
    sent_ids = jnp.sum(jnp.where(request_hit[:, :, None], tables[None, :, :MIGP], 0), axis=1)
    page_hit = (
        sent_ids[:, :, None] == jnp.arange(pool_pages, dtype=jnp.int32)[None, None, :]
    ).astype(jnp.bfloat16)
    pages_sent = jnp.einsum(
        "smp,pwc->smwc", page_hit, pool, preferred_element_type=jnp.float32
    ).astype(jnp.bfloat16)
    partner_normed, pages_sent = lax.optimization_barrier((partner_normed, pages_sent))
    arrivals = [shifted(pages_sent[number], REQ, offsets[number]) for number in range(slots)]
    arrived = jnp.concatenate(arrivals, axis=0)
    page_column = jnp.minimum(jnp.arange(MAXP, dtype=jnp.int32), MIGP - 1)
    moved_pages = pool_pages + slot_of[:, None] * MIGP + page_column[None, :]
    used_table = jnp.where(is_moved[:, None], moved_pages, own_table)
    page_rows = pool.shape[1]
    living = (
        jnp.arange(MAXP, dtype=jnp.int32)[:, None] * page_rows
        + jnp.arange(page_rows, dtype=jnp.int32)[None, :]
    )[None] < own_lengths[:, None, None]
    living = living.astype(jnp.float32)
    all_pages = jnp.arange(pool_pages + arrived.shape[0], dtype=jnp.int32)
    hits = (used_table[:, :, None] == all_pages[None, None, :]).astype(jnp.float32)
    counts = jnp.einsum("rsp,rsw->rpw", hits, living).reshape(local_rows, -1)
    pool_counts = counts[:, : pool_pages * page_rows]
    arrived_counts = counts[:, pool_pages * page_rows :]
    pool_scores, pool_values = dense_scores(queries, pool, pool_counts)
    arrived_scores, arrived_values = dense_scores(queries, arrived, arrived_counts)
    tops = jnp.maximum(
        jnp.maximum(jnp.max(pool_scores, axis=-1), jnp.max(arrived_scores, axis=-1)), own_score
    )
    own_weight = jnp.exp(own_score - tops)
    sums = own_weight
    accs = own_weight.astype(jnp.bfloat16).astype(jnp.float32)[..., None] * new_values.astype(
        jnp.float32
    )[:, :, None, :]
    for scores, values, count in (
        (pool_scores, pool_values, pool_counts),
        (arrived_scores, arrived_values, arrived_counts),
    ):
        weights = jnp.exp(scores - tops[..., None])
        sums = sums + jnp.sum(weights * count[:, None, None, :], axis=-1)
        rounded = weights.astype(jnp.bfloat16).astype(jnp.float32) * count[:, None, None, :]
        accs = accs + jnp.einsum(
            "rkgt,tkd->rkgd",
            rounded,
            values.astype(jnp.float32),
            precision=lax.Precision.HIGHEST,
            preferred_element_type=jnp.float32,
        )
    attended = (accs / sums[..., None]).reshape(local_rows, query_width).astype(jnp.bfloat16)
    partner_attended = from_partner(attended, "guide", 0)
    both_attended = jnp.where(
        side == 0, jnp.stack([attended, partner_attended]), jnp.stack([partner_attended, attended])
    )
    head_half = w_out.shape[0]
    attended_part = lax.dynamic_slice_in_dim(both_attended, side * head_half, head_half, 2)
    selected = attended_part
    out_parts = jnp.einsum("grc,cd->grd", selected, w_out, preferred_element_type=jnp.float32)
    own_out = jnp.where(side == 0, out_parts[0], out_parts[1])
    other_out = jnp.where(side == 0, out_parts[1], out_parts[0]).astype(jnp.bfloat16)
    state_after = states_in + (
        own_out + from_partner(other_out, "guide", 0).astype(jnp.float32)
    )
    final = rms_scale(state_after, final_gain).astype(jnp.bfloat16)
    pair = ("guide", "x_lo")
    from_side = lax.ppermute(final, pair, [(0, 1), (3, 2)])
    from_diagonal = lax.ppermute(final, pair, [(2, 1), (1, 2)])
    from_guide = lax.ppermute(final, pair, [(2, 0), (1, 3)])
    home = lax.axis_index("x_lo") == side
    same_group = jnp.where(home, final, from_side)
    other_group = jnp.where(home, from_guide, from_diagonal)
    cond = jnp.where(side == 0, same_group, other_group).astype(jnp.float32)
    uncond = jnp.where(side == 0, other_group, same_group).astype(jnp.float32)
    combined = (uncond + guidance * (cond - uncond)).astype(jnp.bfloat16)
    y_index = lax.axis_index("y")
    y_count = lax.axis_size("y")
    by_distance = [combined] + [
        shifted(combined, "y", distance) for distance in range(1, y_count)
    ]
    in_order = []
    for position in range(y_count):
        distance = jnp.remainder(position - y_index, y_count)
        pick = by_distance[0]
        for step in range(1, y_count):
            pick = jnp.where(distance == y_count - step, by_distance[step], pick)
        in_order.append(pick)
    gathered = jnp.stack(in_order)
    gathered = lax.all_gather(gathered, "z", axis=1, tiled=False)
    core = lax.axis_index("core")
    cores = lax.axis_size("core")
    twin = lax.ppermute(gathered, "core", [(0, 1), (1, 0)])
    mine_logits = jnp.einsum("yzrd,dv->yzrv", gathered, w_vocab, preferred_element_type=jnp.float32)
    twin_logits = jnp.einsum("yzrd,dv->yzrv", twin, w_vocab, preferred_element_type=jnp.float32)
    logits = jnp.zeros(
        mine_logits.shape[:2] + (cores,) + mine_logits.shape[2:], jnp.float32
    )
    logits = lax.dynamic_update_slice_in_dim(logits, mine_logits[:, :, None], core, 2)
    logits = lax.dynamic_update_slice_in_dim(logits, twin_logits[:, :, None], 1 - core, 2)
    return logits.reshape(-1, logits.shape[-1])


def solution(mesh):
    split = Mesh(mesh.devices.reshape((mesh.devices.shape[0],) + REQ_SPLIT), ("guide",) + REQ)
    in_specs = (
        P("guide", REQ, None),
        P(),
        P("guide", None),
        P("guide", None),
        P(),
        P(None, REQ),
        P("guide", REQ, None, None),
        P("guide", None),
        P("guide", None, None),
        P("guide", None, None),
    )
    out_specs = P("guide", REQ)
    return jax.shard_map(body, mesh=split, in_specs=in_specs, out_specs=out_specs, check_vma=False)
```

```python
import math

import jax
import jax.numpy as jnp
from jax import lax
from jax.sharding import Mesh
from jax.sharding import PartitionSpec as P

QH = 20
KVH = 5
HD = 64
MAXP = 8
MIGP = 2
HOP = 2
REQ = ("x_lo", "y", "z", "core")
REQ_SPLIT = (2, 4, 8, 2)


epsilon = 1e-06
guidance = 3.0


def from_partner(block, axis, bit):
    count = lax.axis_size(axis)
    route = []
    for low in range(count):
        high = low | 1 << bit
        if high != low and high < count:
            route += [(low, high), (high, low)]
    return lax.ppermute(block, axis, route)


def shifted(value, axis, steps):
    count = lax.axis_size(axis)
    pairs = [(source, (source + steps) % count) for source in range(count)]
    return lax.ppermute(value, axis, pairs)


def rms_scale(values, gain):
    return values * lax.rsqrt(jnp.mean(values * values, axis=-1, keepdims=True) + epsilon) * gain


def masked_scores(queries, page_rows, lengths):
    count = page_rows.shape[0]
    span = page_rows.shape[1]
    half_width = page_rows.shape[2] // 2
    key_rows = page_rows[:, :, :half_width].reshape(count, span, KVH, HD)
    value_rows = page_rows[:, :, half_width:].reshape(count, span, KVH, HD)
    scores = jnp.einsum(
        "rkgd,rskd->rkgs", queries, key_rows, preferred_element_type=jnp.float32
    ) * (1.0 / math.sqrt(HD))
    living = jnp.arange(span, dtype=jnp.int32)[None, :] < lengths[:, None]
    scores = jnp.where(living[:, None, None, :], scores, -jnp.inf)
    return (scores, value_rows)


def attend_all(queries, page_rows, lengths, own_score, value_new):
    scores, value_rows = masked_scores(queries, page_rows, lengths)
    highest = jnp.maximum(jnp.max(scores, axis=-1), own_score)
    weights = jnp.exp(scores - highest[..., None])
    own_weight = jnp.exp(own_score - highest)
    denominator = jnp.sum(weights, axis=-1) + own_weight
    weighted = jnp.einsum(
        "rkgs,rskd->rkgd",
        weights.astype(jnp.bfloat16),
        value_rows,
        preferred_element_type=jnp.float32,
    )
    own_rounded = own_weight.astype(jnp.bfloat16).astype(jnp.float32)
    weighted = weighted + own_rounded[..., None] * value_new.astype(jnp.float32)[:, :, None, :]
    return (highest, denominator, weighted)


def gather_pages(pool, tables):
    picked = pool[tables]
    return picked.reshape(tables.shape[0], tables.shape[1] * pool.shape[1], pool.shape[2])


def dense_scores(queries, page_rows, counts):
    count = page_rows.shape[0] * page_rows.shape[1]
    half_width = page_rows.shape[2] // 2
    flat = page_rows.reshape(count, page_rows.shape[2])
    key_rows = flat[:, :half_width].reshape(count, KVH, HD)
    value_rows = flat[:, half_width:].reshape(count, KVH, HD)
    scores = jnp.einsum(
        "rkgd,tkd->rkgt", queries, key_rows, preferred_element_type=jnp.float32
    ) * (1.0 / math.sqrt(HD))
    scores = jnp.where(counts[:, None, None, :] > 0, scores, -jnp.inf)
    return (scores, value_rows)


def body(
    hidden_in,
    attn_gain,
    w_qkv,
    w_out,
    final_gain,
    w_vocab,
    kv_pool,
    cache_len,
    page_table,
    migrations,
):
    device = lax.axis_index(REQ)
    devices = lax.axis_size(REQ)
    side = lax.axis_index("guide")
    local_rows = hidden_in.shape[1]
    group = QH // KVH
    query_width = QH * HD
    key_width = KVH * HD
    scaling = 1.0 / math.sqrt(HD)
    slots = 2 * HOP
    offsets = [number - HOP if number < HOP else number - HOP + 1 for number in range(slots)]
    states_in = hidden_in[0].astype(jnp.float32)
    normed = rms_scale(states_in, attn_gain).astype(jnp.bfloat16)
    partner_normed = from_partner(normed, "guide", 0)
    both_normed = jnp.where(
        side == 0, jnp.stack([normed, partner_normed]), jnp.stack([partner_normed, normed])
    )
    inner_half = w_qkv.shape[0]
    normed_part = lax.dynamic_slice_in_dim(both_normed, side * inner_half, inner_half, 2)
    selected = normed_part
    qkv_parts = jnp.einsum("grd,df->grf", selected, w_qkv, preferred_element_type=jnp.float32)
    own_qkv = jnp.where(side == 0, qkv_parts[0], qkv_parts[1])
    other_qkv = jnp.where(side == 0, qkv_parts[1], qkv_parts[0])
    joined = (own_qkv + from_partner(other_qkv, "guide", 0)).astype(jnp.bfloat16)
    queries = joined[:, :query_width].reshape(local_rows, KVH, group, HD)
    new_keys = joined[:, query_width : query_width + key_width].reshape(local_rows, KVH, HD)
    new_values = joined[:, query_width + key_width :].reshape(local_rows, KVH, HD)
    own_score = (
        jnp.einsum("rkgd,rkd->rkg", queries, new_keys, preferred_element_type=jnp.float32) * scaling
    )
    tables = page_table[0]
    lengths_all = cache_len[0]
    listing = migrations[0]
    pool = kv_pool[0]
    pool_pages = pool.shape[0]
    first_row = device * local_rows
    own_table = lax.dynamic_slice_in_dim(tables, first_row, local_rows, 0)
    own_lengths = lax.dynamic_slice_in_dim(lengths_all, first_row, local_rows, 0)
    global_ids = first_row + jnp.arange(local_rows, dtype=jnp.int32)
    matches = listing[None, :, 0] == global_ids[:, None]
    is_moved = jnp.any(matches, axis=1)
    old_owner = jnp.sum(jnp.where(matches, listing[None, :, 1], 0), axis=1)
    distance = jnp.remainder(device - old_owner, devices)
    slot_of = jnp.where(distance <= HOP, HOP + distance - 1, HOP - (devices - distance))
    targets = jnp.remainder(device + jnp.array(offsets, jnp.int32), devices)
    holding = (listing[None, :, 1] == device) & (listing[None, :, 2] == targets[:, None])
    held_request = jnp.sum(jnp.where(holding, listing[None, :, 0], 0), axis=1)
    request_hit = jnp.arange(tables.shape[0], dtype=jnp.int32)[None, :] == held_request[:, None]
    sent_ids = jnp.sum(jnp.where(request_hit[:, :, None], tables[None, :, :MIGP], 0), axis=1)
    page_hit = (
        sent_ids[:, :, None] == jnp.arange(pool_pages, dtype=jnp.int32)[None, None, :]
    ).astype(jnp.bfloat16)
    pages_sent = jnp.einsum(
        "smp,pwc->smwc", page_hit, pool, preferred_element_type=jnp.float32
    ).astype(jnp.bfloat16)
    partner_normed, pages_sent = lax.optimization_barrier((partner_normed, pages_sent))
    arrivals = [shifted(pages_sent[number], REQ, offsets[number]) for number in range(slots)]
    arrived = jnp.concatenate(arrivals, axis=0)
    page_column = jnp.minimum(jnp.arange(MAXP, dtype=jnp.int32), MIGP - 1)
    moved_pages = pool_pages + slot_of[:, None] * MIGP + page_column[None, :]
    used_table = jnp.where(is_moved[:, None], moved_pages, own_table)
    page_rows = pool.shape[1]
    living = (
        jnp.arange(MAXP, dtype=jnp.int32)[:, None] * page_rows
        + jnp.arange(page_rows, dtype=jnp.int32)[None, :]
    )[None] < own_lengths[:, None, None]
    living = living.astype(jnp.float32)
    all_pages = jnp.arange(pool_pages + arrived.shape[0], dtype=jnp.int32)
    hits = (used_table[:, :, None] == all_pages[None, None, :]).astype(jnp.float32)
    counts = jnp.einsum("rsp,rsw->rpw", hits, living).reshape(local_rows, -1)
    pool_counts = counts[:, : pool_pages * page_rows]
    arrived_counts = counts[:, pool_pages * page_rows :]
    pool_scores, pool_values = dense_scores(queries, pool, pool_counts)
    arrived_scores, arrived_values = dense_scores(queries, arrived, arrived_counts)
    tops = jnp.maximum(
        jnp.maximum(jnp.max(pool_scores, axis=-1), jnp.max(arrived_scores, axis=-1)), own_score
    )
    own_weight = jnp.exp(own_score - tops)
    sums = own_weight
    accs = own_weight.astype(jnp.bfloat16).astype(jnp.float32)[..., None] * new_values.astype(
        jnp.float32
    )[:, :, None, :]
    for scores, values, count in (
        (pool_scores, pool_values, pool_counts),
        (arrived_scores, arrived_values, arrived_counts),
    ):
        weights = jnp.exp(scores - tops[..., None])
        sums = sums + jnp.sum(weights * count[:, None, None, :], axis=-1)
        rounded = weights.astype(jnp.bfloat16).astype(jnp.float32) * count[:, None, None, :]
        accs = accs + jnp.einsum(
            "rkgt,tkd->rkgd",
            rounded,
            values.astype(jnp.float32),
            precision=lax.Precision.HIGHEST,
            preferred_element_type=jnp.float32,
        )
    attended = (accs / sums[..., None]).reshape(local_rows, query_width).astype(jnp.bfloat16)
    partner_attended = from_partner(attended, "guide", 0)
    both_attended = jnp.where(
        side == 0, jnp.stack([attended, partner_attended]), jnp.stack([partner_attended, attended])
    )
    head_half = w_out.shape[0]
    attended_part = lax.dynamic_slice_in_dim(both_attended, side * head_half, head_half, 2)
    selected = attended_part
    out_parts = jnp.einsum("grc,cd->grd", selected, w_out, preferred_element_type=jnp.float32)
    own_out = jnp.where(side == 0, out_parts[0], out_parts[1])
    other_out = jnp.where(side == 0, out_parts[1], out_parts[0]).astype(jnp.bfloat16)
    payload = jnp.stack([states_in + own_out, other_out.astype(jnp.float32)])
    pair = ("guide", "x_lo")
    from_side = lax.ppermute(payload, pair, [(0, 1), (3, 2)])
    from_diagonal = lax.ppermute(payload, pair, [(2, 1), (1, 2)])
    from_guide = lax.ppermute(payload, pair, [(2, 0), (1, 3)])
    home = lax.axis_index("x_lo") == side
    same_source = jnp.where(home, payload, from_side)
    other_source = jnp.where(home, from_guide, from_diagonal)
    same_group = rms_scale(same_source[0] + other_source[1], final_gain).astype(jnp.bfloat16)
    other_group = rms_scale(other_source[0] + same_source[1], final_gain).astype(jnp.bfloat16)
    cond = jnp.where(side == 0, same_group, other_group).astype(jnp.float32)
    uncond = jnp.where(side == 0, other_group, same_group).astype(jnp.float32)
    combined = (uncond + guidance * (cond - uncond)).astype(jnp.bfloat16)
    y_index = lax.axis_index("y")
    y_count = lax.axis_size("y")
    by_distance = [combined] + [
        shifted(combined, "y", distance) for distance in range(1, y_count)
    ]
    in_order = []
    for position in range(y_count):
        distance = jnp.remainder(position - y_index, y_count)
        pick = by_distance[0]
        for step in range(1, y_count):
            pick = jnp.where(distance == y_count - step, by_distance[step], pick)
        in_order.append(pick)
    gathered = jnp.stack(in_order)
    gathered = lax.all_gather(gathered, "z", axis=1, tiled=False)
    core = lax.axis_index("core")
    cores = lax.axis_size("core")
    twin = lax.ppermute(gathered, "core", [(0, 1), (1, 0)])
    mine_logits = jnp.einsum("yzrd,dv->yzrv", gathered, w_vocab, preferred_element_type=jnp.float32)
    twin_logits = jnp.einsum("yzrd,dv->yzrv", twin, w_vocab, preferred_element_type=jnp.float32)
    logits = jnp.zeros(
        mine_logits.shape[:2] + (cores,) + mine_logits.shape[2:], jnp.float32
    )
    logits = lax.dynamic_update_slice_in_dim(logits, mine_logits[:, :, None], core, 2)
    logits = lax.dynamic_update_slice_in_dim(logits, twin_logits[:, :, None], 1 - core, 2)
    return logits.reshape(-1, logits.shape[-1])


def solution(mesh):
    split = Mesh(mesh.devices.reshape((mesh.devices.shape[0],) + REQ_SPLIT), ("guide",) + REQ)
    in_specs = (
        P("guide", REQ, None),
        P(),
        P("guide", None),
        P("guide", None),
        P(),
        P(None, REQ),
        P("guide", REQ, None, None),
        P("guide", None),
        P("guide", None, None),
        P("guide", None, None),
    )
    out_specs = P("guide", REQ)
    return jax.shard_map(body, mesh=split, in_specs=in_specs, out_specs=out_specs, check_vma=False)
```

```python
import math

import jax
import jax.numpy as jnp
from jax import lax
from jax.sharding import Mesh
from jax.sharding import PartitionSpec as P

QH = 20
KVH = 5
HD = 64
MAXP = 8
MIGP = 2
HOP = 2
REQ = ("x_lo", "y", "z", "core")
REQ_SPLIT = (2, 4, 8, 2)


epsilon = 1e-06
guidance = 3.0


def from_partner(block, axis, bit):
    count = lax.axis_size(axis)
    route = []
    for low in range(count):
        high = low | 1 << bit
        if high != low and high < count:
            route += [(low, high), (high, low)]
    return lax.ppermute(block, axis, route)


def shifted(value, axis, steps):
    count = lax.axis_size(axis)
    pairs = [(source, (source + steps) % count) for source in range(count)]
    return lax.ppermute(value, axis, pairs)


def rms_scale(values, gain):
    return values * lax.rsqrt(jnp.mean(values * values, axis=-1, keepdims=True) + epsilon) * gain


def masked_scores(queries, page_rows, lengths):
    count = page_rows.shape[0]
    span = page_rows.shape[1]
    half_width = page_rows.shape[2] // 2
    key_rows = page_rows[:, :, :half_width].reshape(count, span, KVH, HD)
    value_rows = page_rows[:, :, half_width:].reshape(count, span, KVH, HD)
    scores = jnp.einsum(
        "rkgd,rskd->rkgs", queries, key_rows, preferred_element_type=jnp.float32
    ) * (1.0 / math.sqrt(HD))
    living = jnp.arange(span, dtype=jnp.int32)[None, :] < lengths[:, None]
    scores = jnp.where(living[:, None, None, :], scores, -jnp.inf)
    return (scores, value_rows)


def attend_all(queries, page_rows, lengths, own_score, value_new):
    scores, value_rows = masked_scores(queries, page_rows, lengths)
    highest = jnp.maximum(jnp.max(scores, axis=-1), own_score)
    weights = jnp.exp(scores - highest[..., None])
    own_weight = jnp.exp(own_score - highest)
    denominator = jnp.sum(weights, axis=-1) + own_weight
    weighted = jnp.einsum(
        "rkgs,rskd->rkgd",
        weights.astype(jnp.bfloat16),
        value_rows,
        preferred_element_type=jnp.float32,
    )
    own_rounded = own_weight.astype(jnp.bfloat16).astype(jnp.float32)
    weighted = weighted + own_rounded[..., None] * value_new.astype(jnp.float32)[:, :, None, :]
    return (highest, denominator, weighted)


def gather_pages(pool, tables):
    picked = pool[tables]
    return picked.reshape(tables.shape[0], tables.shape[1] * pool.shape[1], pool.shape[2])


def dense_scores(queries, page_rows, counts):
    count = page_rows.shape[0] * page_rows.shape[1]
    half_width = page_rows.shape[2] // 2
    flat = page_rows.reshape(count, page_rows.shape[2])
    key_rows = flat[:, :half_width].reshape(count, KVH, HD)
    value_rows = flat[:, half_width:].reshape(count, KVH, HD)
    scores = jnp.einsum(
        "rkgd,tkd->rkgt", queries, key_rows, preferred_element_type=jnp.float32
    ) * (1.0 / math.sqrt(HD))
    scores = jnp.where(counts[:, None, None, :] > 0, scores, -jnp.inf)
    return (scores, value_rows)


def body(
    hidden_in,
    attn_gain,
    w_qkv,
    w_out,
    final_gain,
    w_vocab,
    kv_pool,
    cache_len,
    page_table,
    migrations,
):
    device = lax.axis_index(REQ)
    devices = lax.axis_size(REQ)
    side = lax.axis_index("guide")
    local_rows = hidden_in.shape[1]
    group = QH // KVH
    query_width = QH * HD
    key_width = KVH * HD
    scaling = 1.0 / math.sqrt(HD)
    slots = 2 * HOP
    offsets = [number - HOP if number < HOP else number - HOP + 1 for number in range(slots)]
    states_in = hidden_in[0].astype(jnp.float32)
    normed = rms_scale(states_in, attn_gain).astype(jnp.bfloat16)
    partner_normed = from_partner(normed, "guide", 0)
    both_normed = jnp.where(
        side == 0, jnp.stack([normed, partner_normed]), jnp.stack([partner_normed, normed])
    )
    inner_half = w_qkv.shape[0]
    normed_part = lax.dynamic_slice_in_dim(both_normed, side * inner_half, inner_half, 2)
    selected = normed_part
    qkv_parts = jnp.einsum("grd,df->grf", selected, w_qkv, preferred_element_type=jnp.float32)
    own_qkv = jnp.where(side == 0, qkv_parts[0], qkv_parts[1])
    other_qkv = jnp.where(side == 0, qkv_parts[1], qkv_parts[0])
    joined = (own_qkv + from_partner(other_qkv, "guide", 0)).astype(jnp.bfloat16)
    queries = joined[:, :query_width].reshape(local_rows, KVH, group, HD)
    new_keys = joined[:, query_width : query_width + key_width].reshape(local_rows, KVH, HD)
    new_values = joined[:, query_width + key_width :].reshape(local_rows, KVH, HD)
    own_score = (
        jnp.einsum("rkgd,rkd->rkg", queries, new_keys, preferred_element_type=jnp.float32) * scaling
    )
    tables = page_table[0]
    lengths_all = cache_len[0]
    listing = migrations[0]
    pool = kv_pool[0]
    pool_pages = pool.shape[0]
    first_row = device * local_rows
    own_table = lax.dynamic_slice_in_dim(tables, first_row, local_rows, 0)
    own_lengths = lax.dynamic_slice_in_dim(lengths_all, first_row, local_rows, 0)
    global_ids = first_row + jnp.arange(local_rows, dtype=jnp.int32)
    matches = listing[None, :, 0] == global_ids[:, None]
    is_moved = jnp.any(matches, axis=1)
    old_owner = jnp.sum(jnp.where(matches, listing[None, :, 1], 0), axis=1)
    distance = jnp.remainder(device - old_owner, devices)
    slot_of = jnp.where(distance <= HOP, HOP + distance - 1, HOP - (devices - distance))
    targets = jnp.remainder(device + jnp.array(offsets, jnp.int32), devices)
    holding = (listing[None, :, 1] == device) & (listing[None, :, 2] == targets[:, None])
    held_request = jnp.sum(jnp.where(holding, listing[None, :, 0], 0), axis=1)
    request_hit = jnp.arange(tables.shape[0], dtype=jnp.int32)[None, :] == held_request[:, None]
    sent_ids = jnp.sum(jnp.where(request_hit[:, :, None], tables[None, :, :MIGP], 0), axis=1)
    page_hit = (
        sent_ids[:, :, None] == jnp.arange(pool_pages, dtype=jnp.int32)[None, None, :]
    ).astype(jnp.bfloat16)
    pages_sent = jnp.einsum(
        "smp,pwc->smwc", page_hit, pool, preferred_element_type=jnp.float32
    ).astype(jnp.bfloat16)
    partner_normed, pages_sent = lax.optimization_barrier((partner_normed, pages_sent))
    arrivals = [shifted(pages_sent[number], REQ, offsets[number]) for number in range(slots)]
    arrived = jnp.concatenate(arrivals, axis=0)
    page_column = jnp.minimum(jnp.arange(MAXP, dtype=jnp.int32), MIGP - 1)
    moved_pages = pool_pages + slot_of[:, None] * MIGP + page_column[None, :]
    used_table = jnp.where(is_moved[:, None], moved_pages, own_table)
    page_rows = pool.shape[1]
    living = (
        jnp.arange(MAXP, dtype=jnp.int32)[:, None] * page_rows
        + jnp.arange(page_rows, dtype=jnp.int32)[None, :]
    )[None] < own_lengths[:, None, None]
    living = living.astype(jnp.float32)
    all_pages = jnp.arange(pool_pages + arrived.shape[0], dtype=jnp.int32)
    hits = (used_table[:, :, None] == all_pages[None, None, :]).astype(jnp.float32)
    counts = jnp.einsum("rsp,rsw->rpw", hits, living).reshape(local_rows, -1)
    pool_counts = counts[:, : pool_pages * page_rows]
    arrived_counts = counts[:, pool_pages * page_rows :]
    pool_scores, pool_values = dense_scores(queries, pool, pool_counts)
    arrived_scores, arrived_values = dense_scores(queries, arrived, arrived_counts)
    tops = jnp.maximum(
        jnp.maximum(jnp.max(pool_scores, axis=-1), jnp.max(arrived_scores, axis=-1)), own_score
    )
    own_weight = jnp.exp(own_score - tops)
    sums = own_weight
    accs = own_weight.astype(jnp.bfloat16).astype(jnp.float32)[..., None] * new_values.astype(
        jnp.float32
    )[:, :, None, :]
    for scores, values, count in (
        (pool_scores, pool_values, pool_counts),
        (arrived_scores, arrived_values, arrived_counts),
    ):
        weights = jnp.exp(scores - tops[..., None])
        sums = sums + jnp.sum(weights * count[:, None, None, :], axis=-1)
        rounded = weights.astype(jnp.bfloat16).astype(jnp.float32) * count[:, None, None, :]
        accs = accs + jnp.einsum(
            "rkgt,tkd->rkgd",
            rounded,
            values.astype(jnp.float32),
            precision=lax.Precision.HIGHEST,
            preferred_element_type=jnp.float32,
        )
    attended = (accs / sums[..., None]).reshape(local_rows, query_width).astype(jnp.bfloat16)
    partner_attended = from_partner(attended, "guide", 0)
    both_attended = jnp.where(
        side == 0, jnp.stack([attended, partner_attended]), jnp.stack([partner_attended, attended])
    )
    head_half = w_out.shape[0]
    attended_part = lax.dynamic_slice_in_dim(both_attended, side * head_half, head_half, 2)
    selected = attended_part
    out_parts = jnp.einsum("grc,cd->grd", selected, w_out, preferred_element_type=jnp.float32)
    own_out = jnp.where(side == 0, out_parts[0], out_parts[1])
    other_out = jnp.where(side == 0, out_parts[1], out_parts[0]).astype(jnp.bfloat16)
    payload = jnp.stack([states_in + own_out, other_out.astype(jnp.float32)])
    pair = ("guide", "x_lo")
    from_side = lax.ppermute(payload, pair, [(0, 1), (3, 2)])
    from_diagonal = lax.ppermute(payload, pair, [(2, 1), (1, 2)])
    from_guide = lax.ppermute(payload, pair, [(2, 0), (1, 3)])
    home = lax.axis_index("x_lo") == side
    same_source = jnp.where(home, payload, from_side)
    other_source = jnp.where(home, from_guide, from_diagonal)
    same_group = rms_scale(same_source[0] + other_source[1], final_gain).astype(jnp.bfloat16)
    other_group = rms_scale(other_source[0] + same_source[1], final_gain).astype(jnp.bfloat16)
    cond = jnp.where(side == 0, same_group, other_group).astype(jnp.float32)
    uncond = jnp.where(side == 0, other_group, same_group).astype(jnp.float32)
    combined = (uncond + guidance * (cond - uncond)).astype(jnp.bfloat16)
    y_index = lax.axis_index("y")
    y_count = lax.axis_size("y")
    by_distance = [combined] + [
        shifted(combined, "y", distance) for distance in range(1, y_count)
    ]
    in_order = []
    for position in range(y_count):
        distance = jnp.remainder(position - y_index, y_count)
        pick = by_distance[0]
        for step in range(1, y_count):
            pick = jnp.where(distance == y_count - step, by_distance[step], pick)
        in_order.append(pick)
    gathered = jnp.stack(in_order)
    gathered = lax.all_gather(gathered, "z", axis=1, tiled=False)
    core = lax.axis_index("core")
    cores = lax.axis_size("core")
    pieces = 2
    piece_rows = gathered.shape[0] // pieces
    twins = [
        lax.ppermute(gathered[piece * piece_rows : (piece + 1) * piece_rows], "core", [(0, 1), (1, 0)])
        for piece in range(pieces)
    ]
    mine_logits = jnp.einsum("yzrd,dv->yzrv", gathered, w_vocab, preferred_element_type=jnp.float32)
    logits = jnp.zeros(
        mine_logits.shape[:2] + (cores,) + mine_logits.shape[2:], jnp.float32
    )
    logits = lax.dynamic_update_slice_in_dim(logits, mine_logits[:, :, None], core, 2)
    for piece, twin in enumerate(twins):
        twin_logits = jnp.einsum("yzrd,dv->yzrv", twin, w_vocab, preferred_element_type=jnp.float32)
        logits = lax.dynamic_update_slice(
            logits, twin_logits[:, :, None], (piece * piece_rows, 0, 1 - core, 0, 0)
        )
    return logits.reshape(-1, logits.shape[-1])


def solution(mesh):
    split = Mesh(mesh.devices.reshape((mesh.devices.shape[0],) + REQ_SPLIT), ("guide",) + REQ)
    in_specs = (
        P("guide", REQ, None),
        P(),
        P("guide", None),
        P("guide", None),
        P(),
        P(None, REQ),
        P("guide", REQ, None, None),
        P("guide", None),
        P("guide", None, None),
        P("guide", None, None),
    )
    out_specs = P("guide", REQ)
    return jax.shard_map(body, mesh=split, in_specs=in_specs, out_specs=out_specs, check_vma=False)
```

```python
import math

import jax
import jax.numpy as jnp
from jax import lax
from jax.sharding import Mesh
from jax.sharding import PartitionSpec as P

QH = 20
KVH = 5
HD = 64
MAXP = 8
MIGP = 2
HOP = 2
REQ = ("x_lo", "y", "z", "core")
REQ_SPLIT = (2, 4, 8, 2)


epsilon = 1e-06
guidance = 3.0


def from_partner(block, axis, bit):
    count = lax.axis_size(axis)
    route = []
    for low in range(count):
        high = low | 1 << bit
        if high != low and high < count:
            route += [(low, high), (high, low)]
    return lax.ppermute(block, axis, route)


def shifted(value, axis, steps):
    count = lax.axis_size(axis)
    pairs = [(source, (source + steps) % count) for source in range(count)]
    return lax.ppermute(value, axis, pairs)


def rms_scale(values, gain):
    return values * lax.rsqrt(jnp.mean(values * values, axis=-1, keepdims=True) + epsilon) * gain


def masked_scores(queries, page_rows, lengths):
    count = page_rows.shape[0]
    span = page_rows.shape[1]
    half_width = page_rows.shape[2] // 2
    key_rows = page_rows[:, :, :half_width].reshape(count, span, KVH, HD)
    value_rows = page_rows[:, :, half_width:].reshape(count, span, KVH, HD)
    scores = jnp.einsum(
        "rkgd,rskd->rkgs", queries, key_rows, preferred_element_type=jnp.float32
    ) * (1.0 / math.sqrt(HD))
    living = jnp.arange(span, dtype=jnp.int32)[None, :] < lengths[:, None]
    scores = jnp.where(living[:, None, None, :], scores, -jnp.inf)
    return (scores, value_rows)


def attend_all(queries, page_rows, lengths, own_score, value_new):
    scores, value_rows = masked_scores(queries, page_rows, lengths)
    highest = jnp.maximum(jnp.max(scores, axis=-1), own_score)
    weights = jnp.exp(scores - highest[..., None])
    own_weight = jnp.exp(own_score - highest)
    denominator = jnp.sum(weights, axis=-1) + own_weight
    weighted = jnp.einsum(
        "rkgs,rskd->rkgd",
        weights.astype(jnp.bfloat16),
        value_rows,
        preferred_element_type=jnp.float32,
    )
    own_rounded = own_weight.astype(jnp.bfloat16).astype(jnp.float32)
    weighted = weighted + own_rounded[..., None] * value_new.astype(jnp.float32)[:, :, None, :]
    return (highest, denominator, weighted)


def gather_pages(pool, tables):
    picked = pool[tables]
    return picked.reshape(tables.shape[0], tables.shape[1] * pool.shape[1], pool.shape[2])


def dense_scores(queries, page_rows, counts):
    count = page_rows.shape[0] * page_rows.shape[1]
    half_width = page_rows.shape[2] // 2
    flat = page_rows.reshape(count, page_rows.shape[2])
    key_rows = flat[:, :half_width].reshape(count, KVH, HD)
    value_rows = flat[:, half_width:].reshape(count, KVH, HD)
    scores = jnp.einsum(
        "rkgd,tkd->rkgt", queries, key_rows, preferred_element_type=jnp.float32
    ) * (1.0 / math.sqrt(HD))
    scores = jnp.where(counts[:, None, None, :] > 0, scores, -jnp.inf)
    return (scores, value_rows)


def body(
    hidden_in,
    attn_gain,
    w_qkv,
    w_out,
    final_gain,
    w_vocab,
    kv_pool,
    cache_len,
    page_table,
    migrations,
):
    device = lax.axis_index(REQ)
    devices = lax.axis_size(REQ)
    side = lax.axis_index("guide")
    local_rows = hidden_in.shape[1]
    group = QH // KVH
    query_width = QH * HD
    key_width = KVH * HD
    scaling = 1.0 / math.sqrt(HD)
    slots = 2 * HOP
    offsets = [number - HOP if number < HOP else number - HOP + 1 for number in range(slots)]
    states_in = hidden_in[0].astype(jnp.float32)
    normed = rms_scale(states_in, attn_gain).astype(jnp.bfloat16)
    inner_half = w_qkv.shape[0]
    own_columns = lax.dynamic_slice_in_dim(normed, side * inner_half, inner_half, 1)
    partner_normed = from_partner(
        lax.dynamic_slice_in_dim(normed, (1 - side) * inner_half, inner_half, 1), "guide", 0
    )
    selected = jnp.where(
        side == 0,
        jnp.stack([own_columns, partner_normed]),
        jnp.stack([partner_normed, own_columns]),
    )
    qkv_parts = jnp.einsum("grd,df->grf", selected, w_qkv, preferred_element_type=jnp.float32)
    own_qkv = jnp.where(side == 0, qkv_parts[0], qkv_parts[1])
    other_qkv = jnp.where(side == 0, qkv_parts[1], qkv_parts[0])
    joined = (own_qkv + from_partner(other_qkv, "guide", 0)).astype(jnp.bfloat16)
    queries = joined[:, :query_width].reshape(local_rows, KVH, group, HD)
    new_keys = joined[:, query_width : query_width + key_width].reshape(local_rows, KVH, HD)
    new_values = joined[:, query_width + key_width :].reshape(local_rows, KVH, HD)
    own_score = (
        jnp.einsum("rkgd,rkd->rkg", queries, new_keys, preferred_element_type=jnp.float32) * scaling
    )
    tables = page_table[0]
    lengths_all = cache_len[0]
    listing = migrations[0]
    pool = kv_pool[0]
    pool_pages = pool.shape[0]
    first_row = device * local_rows
    own_table = lax.dynamic_slice_in_dim(tables, first_row, local_rows, 0)
    own_lengths = lax.dynamic_slice_in_dim(lengths_all, first_row, local_rows, 0)
    global_ids = first_row + jnp.arange(local_rows, dtype=jnp.int32)
    matches = listing[None, :, 0] == global_ids[:, None]
    is_moved = jnp.any(matches, axis=1)
    old_owner = jnp.sum(jnp.where(matches, listing[None, :, 1], 0), axis=1)
    distance = jnp.remainder(device - old_owner, devices)
    slot_of = jnp.where(distance <= HOP, HOP + distance - 1, HOP - (devices - distance))
    targets = jnp.remainder(device + jnp.array(offsets, jnp.int32), devices)
    holding = (listing[None, :, 1] == device) & (listing[None, :, 2] == targets[:, None])
    held_request = jnp.sum(jnp.where(holding, listing[None, :, 0], 0), axis=1)
    request_hit = jnp.arange(tables.shape[0], dtype=jnp.int32)[None, :] == held_request[:, None]
    sent_ids = jnp.sum(jnp.where(request_hit[:, :, None], tables[None, :, :MIGP], 0), axis=1)
    page_hit = (
        sent_ids[:, :, None] == jnp.arange(pool_pages, dtype=jnp.int32)[None, None, :]
    ).astype(jnp.bfloat16)
    pages_sent = jnp.einsum(
        "smp,pwc->smwc", page_hit, pool, preferred_element_type=jnp.float32
    ).astype(jnp.bfloat16)
    partner_normed, pages_sent = lax.optimization_barrier((partner_normed, pages_sent))
    arrivals = [shifted(pages_sent[number], REQ, offsets[number]) for number in range(slots)]
    arrived = jnp.concatenate(arrivals, axis=0)
    page_column = jnp.minimum(jnp.arange(MAXP, dtype=jnp.int32), MIGP - 1)
    moved_pages = pool_pages + slot_of[:, None] * MIGP + page_column[None, :]
    used_table = jnp.where(is_moved[:, None], moved_pages, own_table)
    page_rows = pool.shape[1]
    living = (
        jnp.arange(MAXP, dtype=jnp.int32)[:, None] * page_rows
        + jnp.arange(page_rows, dtype=jnp.int32)[None, :]
    )[None] < own_lengths[:, None, None]
    living = living.astype(jnp.float32)
    all_pages = jnp.arange(pool_pages + arrived.shape[0], dtype=jnp.int32)
    hits = (used_table[:, :, None] == all_pages[None, None, :]).astype(jnp.float32)
    counts = jnp.einsum("rsp,rsw->rpw", hits, living).reshape(local_rows, -1)
    pool_counts = counts[:, : pool_pages * page_rows]
    arrived_counts = counts[:, pool_pages * page_rows :]
    pool_scores, pool_values = dense_scores(queries, pool, pool_counts)
    arrived_scores, arrived_values = dense_scores(queries, arrived, arrived_counts)
    tops = jnp.maximum(
        jnp.maximum(jnp.max(pool_scores, axis=-1), jnp.max(arrived_scores, axis=-1)), own_score
    )
    own_weight = jnp.exp(own_score - tops)
    sums = own_weight
    accs = own_weight.astype(jnp.bfloat16).astype(jnp.float32)[..., None] * new_values.astype(
        jnp.float32
    )[:, :, None, :]
    for scores, values, count in (
        (pool_scores, pool_values, pool_counts),
        (arrived_scores, arrived_values, arrived_counts),
    ):
        weights = jnp.exp(scores - tops[..., None])
        sums = sums + jnp.sum(weights * count[:, None, None, :], axis=-1)
        rounded = weights.astype(jnp.bfloat16).astype(jnp.float32) * count[:, None, None, :]
        accs = accs + jnp.einsum(
            "rkgt,tkd->rkgd",
            rounded,
            values.astype(jnp.float32),
            precision=lax.Precision.HIGHEST,
            preferred_element_type=jnp.float32,
        )
    attended = (accs / sums[..., None]).reshape(local_rows, query_width).astype(jnp.bfloat16)
    head_half = w_out.shape[0]
    own_heads = lax.dynamic_slice_in_dim(attended, side * head_half, head_half, 1)
    partner_heads = from_partner(
        lax.dynamic_slice_in_dim(attended, (1 - side) * head_half, head_half, 1), "guide", 0
    )
    selected = jnp.where(
        side == 0, jnp.stack([own_heads, partner_heads]), jnp.stack([partner_heads, own_heads])
    )
    out_parts = jnp.einsum("grc,cd->grd", selected, w_out, preferred_element_type=jnp.float32)
    own_out = jnp.where(side == 0, out_parts[0], out_parts[1])
    other_out = jnp.where(side == 0, out_parts[1], out_parts[0]).astype(jnp.bfloat16)
    payload = jnp.stack([states_in + own_out, other_out.astype(jnp.float32)])
    pair = ("guide", "x_lo")
    from_side = lax.ppermute(payload, pair, [(0, 1), (3, 2)])
    from_diagonal = lax.ppermute(payload, pair, [(2, 1), (1, 2)])
    from_guide = lax.ppermute(payload, pair, [(2, 0), (1, 3)])
    home = lax.axis_index("x_lo") == side
    same_source = jnp.where(home, payload, from_side)
    other_source = jnp.where(home, from_guide, from_diagonal)
    same_group = rms_scale(same_source[0] + other_source[1], final_gain).astype(jnp.bfloat16)
    other_group = rms_scale(other_source[0] + same_source[1], final_gain).astype(jnp.bfloat16)
    cond = jnp.where(side == 0, same_group, other_group).astype(jnp.float32)
    uncond = jnp.where(side == 0, other_group, same_group).astype(jnp.float32)
    combined = (uncond + guidance * (cond - uncond)).astype(jnp.bfloat16)
    y_index = lax.axis_index("y")
    y_count = lax.axis_size("y")
    by_distance = [combined] + [
        shifted(combined, "y", distance) for distance in range(1, y_count)
    ]
    in_order = []
    for position in range(y_count):
        distance = jnp.remainder(position - y_index, y_count)
        pick = by_distance[0]
        for step in range(1, y_count):
            pick = jnp.where(distance == y_count - step, by_distance[step], pick)
        in_order.append(pick)
    gathered = jnp.stack(in_order)
    gathered = lax.all_gather(gathered, "z", axis=1, tiled=False)
    core = lax.axis_index("core")
    cores = lax.axis_size("core")
    twin = lax.ppermute(gathered, "core", [(0, 1), (1, 0)])
    mine_logits = jnp.einsum("yzrd,dv->yzrv", gathered, w_vocab, preferred_element_type=jnp.float32)
    twin_logits = jnp.einsum("yzrd,dv->yzrv", twin, w_vocab, preferred_element_type=jnp.float32)
    logits = jnp.zeros(
        mine_logits.shape[:2] + (cores,) + mine_logits.shape[2:], jnp.float32
    )
    logits = lax.dynamic_update_slice_in_dim(logits, mine_logits[:, :, None], core, 2)
    logits = lax.dynamic_update_slice_in_dim(logits, twin_logits[:, :, None], 1 - core, 2)
    return logits.reshape(-1, logits.shape[-1])


def solution(mesh):
    split = Mesh(mesh.devices.reshape((mesh.devices.shape[0],) + REQ_SPLIT), ("guide",) + REQ)
    in_specs = (
        P("guide", REQ, None),
        P(),
        P("guide", None),
        P("guide", None),
        P(),
        P(None, REQ),
        P("guide", REQ, None, None),
        P("guide", None),
        P("guide", None, None),
        P("guide", None, None),
    )
    out_specs = P("guide", REQ)
    return jax.shard_map(body, mesh=split, in_specs=in_specs, out_specs=out_specs, check_vma=False)
```

```python
import math

import jax
import jax.numpy as jnp
from jax import lax
from jax.sharding import Mesh
from jax.sharding import PartitionSpec as P

QH = 20
KVH = 5
HD = 64
MAXP = 8
MIGP = 2
HOP = 2
REQ = ("x_lo", "y", "z", "core")
REQ_SPLIT = (2, 4, 8, 2)


epsilon = 1e-06
guidance = 3.0


def from_partner(block, axis, bit):
    count = lax.axis_size(axis)
    route = []
    for low in range(count):
        high = low | 1 << bit
        if high != low and high < count:
            route += [(low, high), (high, low)]
    return lax.ppermute(block, axis, route)


def shifted(value, axis, steps):
    count = lax.axis_size(axis)
    pairs = [(source, (source + steps) % count) for source in range(count)]
    return lax.ppermute(value, axis, pairs)


def rms_scale(values, gain):
    return values * lax.rsqrt(jnp.mean(values * values, axis=-1, keepdims=True) + epsilon) * gain


def masked_scores(queries, page_rows, lengths):
    count = page_rows.shape[0]
    span = page_rows.shape[1]
    half_width = page_rows.shape[2] // 2
    key_rows = page_rows[:, :, :half_width].reshape(count, span, KVH, HD)
    value_rows = page_rows[:, :, half_width:].reshape(count, span, KVH, HD)
    scores = jnp.einsum(
        "rkgd,rskd->rkgs", queries, key_rows, preferred_element_type=jnp.float32
    ) * (1.0 / math.sqrt(HD))
    living = jnp.arange(span, dtype=jnp.int32)[None, :] < lengths[:, None]
    scores = jnp.where(living[:, None, None, :], scores, -jnp.inf)
    return (scores, value_rows)


def attend_all(queries, page_rows, lengths, own_score, value_new):
    scores, value_rows = masked_scores(queries, page_rows, lengths)
    highest = jnp.maximum(jnp.max(scores, axis=-1), own_score)
    weights = jnp.exp(scores - highest[..., None])
    own_weight = jnp.exp(own_score - highest)
    denominator = jnp.sum(weights, axis=-1) + own_weight
    weighted = jnp.einsum(
        "rkgs,rskd->rkgd",
        weights.astype(jnp.bfloat16),
        value_rows,
        preferred_element_type=jnp.float32,
    )
    own_rounded = own_weight.astype(jnp.bfloat16).astype(jnp.float32)
    weighted = weighted + own_rounded[..., None] * value_new.astype(jnp.float32)[:, :, None, :]
    return (highest, denominator, weighted)


def gather_pages(pool, tables):
    picked = pool[tables]
    return picked.reshape(tables.shape[0], tables.shape[1] * pool.shape[1], pool.shape[2])


def dense_scores(queries, page_rows, counts):
    count = page_rows.shape[0] * page_rows.shape[1]
    half_width = page_rows.shape[2] // 2
    flat = page_rows.reshape(count, page_rows.shape[2])
    key_rows = flat[:, :half_width].reshape(count, KVH, HD)
    value_rows = flat[:, half_width:].reshape(count, KVH, HD)
    scores = jnp.einsum(
        "rkgd,tkd->rkgt", queries, key_rows, preferred_element_type=jnp.float32
    ) * (1.0 / math.sqrt(HD))
    scores = jnp.where(counts[:, None, None, :] > 0, scores, -jnp.inf)
    return (scores, value_rows)


def body(
    hidden_in,
    attn_gain,
    w_qkv,
    w_out,
    final_gain,
    w_vocab,
    kv_pool,
    cache_len,
    page_table,
    migrations,
):
    device = lax.axis_index(REQ)
    devices = lax.axis_size(REQ)
    side = lax.axis_index("guide")
    local_rows = hidden_in.shape[1]
    group = QH // KVH
    query_width = QH * HD
    key_width = KVH * HD
    scaling = 1.0 / math.sqrt(HD)
    slots = 2 * HOP
    offsets = [number - HOP if number < HOP else number - HOP + 1 for number in range(slots)]
    states_in = hidden_in[0].astype(jnp.float32)
    normed = rms_scale(states_in, attn_gain).astype(jnp.bfloat16)
    inner_half = w_qkv.shape[0]
    own_columns = lax.dynamic_slice_in_dim(normed, side * inner_half, inner_half, 1)
    partner_normed = from_partner(
        lax.dynamic_slice_in_dim(normed, (1 - side) * inner_half, inner_half, 1), "guide", 0
    )
    selected = jnp.where(
        side == 0,
        jnp.stack([own_columns, partner_normed]),
        jnp.stack([partner_normed, own_columns]),
    )
    qkv_parts = jnp.einsum("grd,df->grf", selected, w_qkv, preferred_element_type=jnp.float32)
    own_qkv = jnp.where(side == 0, qkv_parts[0], qkv_parts[1])
    other_qkv = jnp.where(side == 0, qkv_parts[1], qkv_parts[0])
    joined = (own_qkv + from_partner(other_qkv, "guide", 0)).astype(jnp.bfloat16)
    queries = joined[:, :query_width].reshape(local_rows, KVH, group, HD)
    new_keys = joined[:, query_width : query_width + key_width].reshape(local_rows, KVH, HD)
    new_values = joined[:, query_width + key_width :].reshape(local_rows, KVH, HD)
    own_score = (
        jnp.einsum("rkgd,rkd->rkg", queries, new_keys, preferred_element_type=jnp.float32) * scaling
    )
    tables = page_table[0]
    lengths_all = cache_len[0]
    listing = migrations[0]
    pool = kv_pool[0]
    pool_pages = pool.shape[0]
    first_row = device * local_rows
    own_table = lax.dynamic_slice_in_dim(tables, first_row, local_rows, 0)
    own_lengths = lax.dynamic_slice_in_dim(lengths_all, first_row, local_rows, 0)
    global_ids = first_row + jnp.arange(local_rows, dtype=jnp.int32)
    matches = listing[None, :, 0] == global_ids[:, None]
    is_moved = jnp.any(matches, axis=1)
    old_owner = jnp.sum(jnp.where(matches, listing[None, :, 1], 0), axis=1)
    distance = jnp.remainder(device - old_owner, devices)
    slot_of = jnp.where(distance <= HOP, HOP + distance - 1, HOP - (devices - distance))
    targets = jnp.remainder(device + jnp.array(offsets, jnp.int32), devices)
    holding = (listing[None, :, 1] == device) & (listing[None, :, 2] == targets[:, None])
    held_request = jnp.sum(jnp.where(holding, listing[None, :, 0], 0), axis=1)
    request_hit = jnp.arange(tables.shape[0], dtype=jnp.int32)[None, :] == held_request[:, None]
    sent_ids = jnp.sum(jnp.where(request_hit[:, :, None], tables[None, :, :MIGP], 0), axis=1)
    page_hit = (
        sent_ids[:, :, None] == jnp.arange(pool_pages, dtype=jnp.int32)[None, None, :]
    ).astype(jnp.bfloat16)
    pages_sent = jnp.einsum(
        "smp,pwc->smwc", page_hit, pool, preferred_element_type=jnp.float32
    ).astype(jnp.bfloat16)
    partner_normed, pages_sent = lax.optimization_barrier((partner_normed, pages_sent))
    arrivals = [shifted(pages_sent[number], REQ, offsets[number]) for number in range(slots)]
    arrived = jnp.concatenate(arrivals, axis=0)
    page_column = jnp.minimum(jnp.arange(MAXP, dtype=jnp.int32), MIGP - 1)
    moved_pages = pool_pages + slot_of[:, None] * MIGP + page_column[None, :]
    used_table = jnp.where(is_moved[:, None], moved_pages, own_table)
    page_rows = pool.shape[1]
    living = (
        jnp.arange(MAXP, dtype=jnp.int32)[:, None] * page_rows
        + jnp.arange(page_rows, dtype=jnp.int32)[None, :]
    )[None] < own_lengths[:, None, None]
    living = living.astype(jnp.float32)
    all_pages = jnp.arange(pool_pages + arrived.shape[0], dtype=jnp.int32)
    hits = (used_table[:, :, None] == all_pages[None, None, :]).astype(jnp.float32)
    counts = jnp.einsum("rsp,rsw->rpw", hits, living).reshape(local_rows, -1)
    pool_counts = counts[:, : pool_pages * page_rows]
    arrived_counts = counts[:, pool_pages * page_rows :]
    pool_scores, pool_values = dense_scores(queries, pool, pool_counts)
    arrived_scores, arrived_values = dense_scores(queries, arrived, arrived_counts)
    tops = jnp.maximum(
        jnp.maximum(jnp.max(pool_scores, axis=-1), jnp.max(arrived_scores, axis=-1)), own_score
    )
    own_weight = jnp.exp(own_score - tops)
    sums = own_weight
    accs = own_weight.astype(jnp.bfloat16).astype(jnp.float32)[..., None] * new_values.astype(
        jnp.float32
    )[:, :, None, :]
    for scores, values, count in (
        (pool_scores, pool_values, pool_counts),
        (arrived_scores, arrived_values, arrived_counts),
    ):
        weights = jnp.exp(scores - tops[..., None])
        sums = sums + jnp.sum(weights * count[:, None, None, :], axis=-1)
        rounded = weights.astype(jnp.bfloat16).astype(jnp.float32) * count[:, None, None, :]
        accs = accs + jnp.einsum(
            "rkgt,tkd->rkgd",
            rounded,
            values.astype(jnp.float32),
            precision=lax.Precision.HIGHEST,
            preferred_element_type=jnp.float32,
        )
    attended = (accs / sums[..., None]).reshape(local_rows, query_width).astype(jnp.bfloat16)
    head_half = w_out.shape[0]
    own_heads = lax.dynamic_slice_in_dim(attended, side * head_half, head_half, 1)
    partner_heads = from_partner(
        lax.dynamic_slice_in_dim(attended, (1 - side) * head_half, head_half, 1), "guide", 0
    )
    selected = jnp.where(
        side == 0, jnp.stack([own_heads, partner_heads]), jnp.stack([partner_heads, own_heads])
    )
    out_parts = jnp.einsum("grc,cd->grd", selected, w_out, preferred_element_type=jnp.float32)
    own_out = jnp.where(side == 0, out_parts[0], out_parts[1])
    other_out = jnp.where(side == 0, out_parts[1], out_parts[0]).astype(jnp.bfloat16)
    state_part = states_in + own_out
    pair = ("guide", "x_lo")
    routes = ([(0, 1), (3, 2)], [(2, 1), (1, 2)], [(2, 0), (1, 3)])
    side_state, diagonal_state, guide_state = [lax.ppermute(state_part, pair, r) for r in routes]
    side_out, diagonal_out, guide_out = [lax.ppermute(other_out, pair, r) for r in routes]
    home = lax.axis_index("x_lo") == side
    same_state = jnp.where(home, state_part, side_state)
    same_out = jnp.where(home, other_out, side_out).astype(jnp.float32)
    other_state = jnp.where(home, guide_state, diagonal_state)
    other_part = jnp.where(home, guide_out, diagonal_out).astype(jnp.float32)
    same_group = rms_scale(same_state + other_part, final_gain).astype(jnp.bfloat16)
    other_group = rms_scale(other_state + same_out, final_gain).astype(jnp.bfloat16)
    cond = jnp.where(side == 0, same_group, other_group).astype(jnp.float32)
    uncond = jnp.where(side == 0, other_group, same_group).astype(jnp.float32)
    combined = (uncond + guidance * (cond - uncond)).astype(jnp.bfloat16)
    y_index = lax.axis_index("y")
    y_count = lax.axis_size("y")
    by_distance = [combined] + [
        shifted(combined, "y", distance) for distance in range(1, y_count)
    ]
    in_order = []
    for position in range(y_count):
        distance = jnp.remainder(position - y_index, y_count)
        pick = by_distance[0]
        for step in range(1, y_count):
            pick = jnp.where(distance == y_count - step, by_distance[step], pick)
        in_order.append(pick)
    gathered = jnp.stack(in_order)
    gathered = lax.all_gather(gathered, "z", axis=1, tiled=False)
    core = lax.axis_index("core")
    cores = lax.axis_size("core")
    twin = lax.ppermute(gathered, "core", [(0, 1), (1, 0)])
    mine_logits = jnp.einsum("yzrd,dv->yzrv", gathered, w_vocab, preferred_element_type=jnp.float32)
    twin_logits = jnp.einsum("yzrd,dv->yzrv", twin, w_vocab, preferred_element_type=jnp.float32)
    logits = jnp.zeros(
        mine_logits.shape[:2] + (cores,) + mine_logits.shape[2:], jnp.float32
    )
    logits = lax.dynamic_update_slice_in_dim(logits, mine_logits[:, :, None], core, 2)
    logits = lax.dynamic_update_slice_in_dim(logits, twin_logits[:, :, None], 1 - core, 2)
    return logits.reshape(-1, logits.shape[-1])


def solution(mesh):
    split = Mesh(mesh.devices.reshape((mesh.devices.shape[0],) + REQ_SPLIT), ("guide",) + REQ)
    in_specs = (
        P("guide", REQ, None),
        P(),
        P("guide", None),
        P("guide", None),
        P(),
        P(None, REQ),
        P("guide", REQ, None, None),
        P("guide", None),
        P("guide", None, None),
        P("guide", None, None),
    )
    out_specs = P("guide", REQ)
    return jax.shard_map(body, mesh=split, in_specs=in_specs, out_specs=out_specs, check_vma=False)
```

```python
import math

import jax
import jax.numpy as jnp
from jax import lax
from jax.sharding import Mesh
from jax.sharding import PartitionSpec as P

QH = 20
KVH = 5
HD = 64
MAXP = 8
MIGP = 2
HOP = 2
REQ = ("x_lo", "y", "z", "core")
REQ_SPLIT = (2, 4, 8, 2)


epsilon = 1e-06
guidance = 3.0


def from_partner(block, axis, bit):
    count = lax.axis_size(axis)
    route = []
    for low in range(count):
        high = low | 1 << bit
        if high != low and high < count:
            route += [(low, high), (high, low)]
    return lax.ppermute(block, axis, route)


def shifted(value, axis, steps):
    count = lax.axis_size(axis)
    pairs = [(source, (source + steps) % count) for source in range(count)]
    return lax.ppermute(value, axis, pairs)


def rms_scale(values, gain):
    return values * lax.rsqrt(jnp.mean(values * values, axis=-1, keepdims=True) + epsilon) * gain


def masked_scores(queries, page_rows, lengths):
    count = page_rows.shape[0]
    span = page_rows.shape[1]
    half_width = page_rows.shape[2] // 2
    key_rows = page_rows[:, :, :half_width].reshape(count, span, KVH, HD)
    value_rows = page_rows[:, :, half_width:].reshape(count, span, KVH, HD)
    scores = jnp.einsum(
        "rkgd,rskd->rkgs", queries, key_rows, preferred_element_type=jnp.float32
    ) * (1.0 / math.sqrt(HD))
    living = jnp.arange(span, dtype=jnp.int32)[None, :] < lengths[:, None]
    scores = jnp.where(living[:, None, None, :], scores, -jnp.inf)
    return (scores, value_rows)


def attend_all(queries, page_rows, lengths, own_score, value_new):
    scores, value_rows = masked_scores(queries, page_rows, lengths)
    highest = jnp.maximum(jnp.max(scores, axis=-1), own_score)
    weights = jnp.exp(scores - highest[..., None])
    own_weight = jnp.exp(own_score - highest)
    denominator = jnp.sum(weights, axis=-1) + own_weight
    weighted = jnp.einsum(
        "rkgs,rskd->rkgd",
        weights.astype(jnp.bfloat16),
        value_rows,
        preferred_element_type=jnp.float32,
    )
    own_rounded = own_weight.astype(jnp.bfloat16).astype(jnp.float32)
    weighted = weighted + own_rounded[..., None] * value_new.astype(jnp.float32)[:, :, None, :]
    return (highest, denominator, weighted)


def gather_pages(pool, tables):
    picked = pool[tables]
    return picked.reshape(tables.shape[0], tables.shape[1] * pool.shape[1], pool.shape[2])


def dense_scores(queries, page_rows, counts):
    count = page_rows.shape[0] * page_rows.shape[1]
    half_width = page_rows.shape[2] // 2
    flat = page_rows.reshape(count, page_rows.shape[2])
    key_rows = flat[:, :half_width].reshape(count, KVH, HD)
    value_rows = flat[:, half_width:].reshape(count, KVH, HD)
    scores = jnp.einsum(
        "rkgd,tkd->rkgt", queries, key_rows, preferred_element_type=jnp.float32
    ) * (1.0 / math.sqrt(HD))
    scores = jnp.where(counts[:, None, None, :] > 0, scores, -jnp.inf)
    return (scores, value_rows)


def body(
    hidden_in,
    attn_gain,
    w_qkv,
    w_out,
    final_gain,
    w_vocab,
    kv_pool,
    cache_len,
    page_table,
    migrations,
):
    device = lax.axis_index(REQ)
    devices = lax.axis_size(REQ)
    side = lax.axis_index("guide")
    local_rows = hidden_in.shape[1]
    group = QH // KVH
    query_width = QH * HD
    key_width = KVH * HD
    scaling = 1.0 / math.sqrt(HD)
    slots = 2 * HOP
    offsets = [number - HOP if number < HOP else number - HOP + 1 for number in range(slots)]
    states_in = hidden_in[0].astype(jnp.float32)
    normed = rms_scale(states_in, attn_gain).astype(jnp.bfloat16)
    inner_half = w_qkv.shape[0]
    own_columns = lax.dynamic_slice_in_dim(normed, side * inner_half, inner_half, 1)
    partner_normed = from_partner(
        lax.dynamic_slice_in_dim(normed, (1 - side) * inner_half, inner_half, 1), "guide", 0
    )
    selected = jnp.where(
        side == 0,
        jnp.stack([own_columns, partner_normed]),
        jnp.stack([partner_normed, own_columns]),
    )
    qkv_parts = jnp.einsum("grd,df->grf", selected, w_qkv, preferred_element_type=jnp.float32)
    own_qkv = jnp.where(side == 0, qkv_parts[0], qkv_parts[1])
    other_qkv = jnp.where(side == 0, qkv_parts[1], qkv_parts[0])
    joined = (own_qkv + from_partner(other_qkv, "guide", 0)).astype(jnp.bfloat16)
    queries = joined[:, :query_width].reshape(local_rows, KVH, group, HD)
    new_keys = joined[:, query_width : query_width + key_width].reshape(local_rows, KVH, HD)
    new_values = joined[:, query_width + key_width :].reshape(local_rows, KVH, HD)
    own_score = (
        jnp.einsum("rkgd,rkd->rkg", queries, new_keys, preferred_element_type=jnp.float32) * scaling
    )
    tables = page_table[0]
    lengths_all = cache_len[0]
    listing = migrations[0]
    pool = kv_pool[0]
    pool_pages = pool.shape[0]
    first_row = device * local_rows
    own_table = lax.dynamic_slice_in_dim(tables, first_row, local_rows, 0)
    own_lengths = lax.dynamic_slice_in_dim(lengths_all, first_row, local_rows, 0)
    global_ids = first_row + jnp.arange(local_rows, dtype=jnp.int32)
    matches = listing[None, :, 0] == global_ids[:, None]
    is_moved = jnp.any(matches, axis=1)
    old_owner = jnp.sum(jnp.where(matches, listing[None, :, 1], 0), axis=1)
    distance = jnp.remainder(device - old_owner, devices)
    slot_of = jnp.where(distance <= HOP, HOP + distance - 1, HOP - (devices - distance))
    targets = jnp.remainder(device + jnp.array(offsets, jnp.int32), devices)
    holding = (listing[None, :, 1] == device) & (listing[None, :, 2] == targets[:, None])
    held_request = jnp.sum(jnp.where(holding, listing[None, :, 0], 0), axis=1)
    request_hit = jnp.arange(tables.shape[0], dtype=jnp.int32)[None, :] == held_request[:, None]
    sent_ids = jnp.sum(jnp.where(request_hit[:, :, None], tables[None, :, :MIGP], 0), axis=1)
    page_hit = (
        sent_ids[:, :, None] == jnp.arange(pool_pages, dtype=jnp.int32)[None, None, :]
    ).astype(jnp.bfloat16)
    pages_sent = jnp.einsum(
        "smp,pwc->smwc", page_hit, pool, preferred_element_type=jnp.float32
    ).astype(jnp.bfloat16)
    partner_normed, pages_sent = lax.optimization_barrier((partner_normed, pages_sent))
    arrivals = [shifted(pages_sent[number], REQ, offsets[number]) for number in range(slots)]
    arrived = jnp.concatenate(arrivals, axis=0)
    page_column = jnp.minimum(jnp.arange(MAXP, dtype=jnp.int32), MIGP - 1)
    moved_pages = pool_pages + slot_of[:, None] * MIGP + page_column[None, :]
    used_table = jnp.where(is_moved[:, None], moved_pages, own_table)
    page_rows = pool.shape[1]
    living = (
        jnp.arange(MAXP, dtype=jnp.int32)[:, None] * page_rows
        + jnp.arange(page_rows, dtype=jnp.int32)[None, :]
    )[None] < own_lengths[:, None, None]
    living = living.astype(jnp.float32)
    all_pages = jnp.arange(pool_pages + arrived.shape[0], dtype=jnp.int32)
    hits = (used_table[:, :, None] == all_pages[None, None, :]).astype(jnp.float32)
    counts = jnp.einsum("rsp,rsw->rpw", hits, living).reshape(local_rows, -1)
    pool_counts = counts[:, : pool_pages * page_rows]
    arrived_counts = counts[:, pool_pages * page_rows :]
    pool_scores, pool_values = dense_scores(queries, pool, pool_counts)
    arrived_scores, arrived_values = dense_scores(queries, arrived, arrived_counts)
    tops = jnp.maximum(
        jnp.maximum(jnp.max(pool_scores, axis=-1), jnp.max(arrived_scores, axis=-1)), own_score
    )
    own_weight = jnp.exp(own_score - tops)
    sums = own_weight
    accs = own_weight.astype(jnp.bfloat16).astype(jnp.float32)[..., None] * new_values.astype(
        jnp.float32
    )[:, :, None, :]
    for scores, values, count in (
        (pool_scores, pool_values, pool_counts),
        (arrived_scores, arrived_values, arrived_counts),
    ):
        weights = jnp.exp(scores - tops[..., None])
        sums = sums + jnp.sum(weights * count[:, None, None, :], axis=-1)
        rounded = weights.astype(jnp.bfloat16).astype(jnp.float32) * count[:, None, None, :]
        accs = accs + jnp.einsum(
            "rkgt,tkd->rkgd",
            rounded,
            values.astype(jnp.float32),
            precision=lax.Precision.HIGHEST,
            preferred_element_type=jnp.float32,
        )
    attended = (accs / sums[..., None]).reshape(local_rows, query_width).astype(jnp.bfloat16)
    head_half = w_out.shape[0]
    own_heads = lax.dynamic_slice_in_dim(attended, side * head_half, head_half, 1)
    partner_heads = from_partner(
        lax.dynamic_slice_in_dim(attended, (1 - side) * head_half, head_half, 1), "guide", 0
    )
    selected = jnp.where(
        side == 0, jnp.stack([own_heads, partner_heads]), jnp.stack([partner_heads, own_heads])
    )
    out_parts = jnp.einsum("grc,cd->grd", selected, w_out, preferred_element_type=jnp.float32)
    own_out = jnp.where(side == 0, out_parts[0], out_parts[1])
    other_out = jnp.where(side == 0, out_parts[1], out_parts[0]).astype(jnp.bfloat16)
    payload = jnp.stack([states_in + own_out, other_out.astype(jnp.float32)])
    pair = ("guide", "x_lo")
    from_side = lax.ppermute(payload, pair, [(0, 1), (3, 2)])
    from_diagonal = lax.ppermute(payload, pair, [(2, 1), (1, 2)])
    from_guide = lax.ppermute(payload, pair, [(2, 0), (1, 3)])
    home = lax.axis_index("x_lo") == side
    same_source = jnp.where(home, payload, from_side)
    other_source = jnp.where(home, from_guide, from_diagonal)
    same_group = rms_scale(same_source[0] + other_source[1], final_gain).astype(jnp.bfloat16)
    other_group = rms_scale(other_source[0] + same_source[1], final_gain).astype(jnp.bfloat16)
    cond = jnp.where(side == 0, same_group, other_group).astype(jnp.float32)
    uncond = jnp.where(side == 0, other_group, same_group).astype(jnp.float32)
    combined = (uncond + guidance * (cond - uncond)).astype(jnp.bfloat16)
    y_index = lax.axis_index("y")
    y_count = lax.axis_size("y")
    by_distance = [combined] + [
        shifted(combined, "y", distance) for distance in range(1, y_count)
    ]
    in_order = []
    for position in range(y_count):
        distance = jnp.remainder(position - y_index, y_count)
        pick = by_distance[0]
        for step in range(1, y_count):
            pick = jnp.where(distance == y_count - step, by_distance[step], pick)
        in_order.append(pick)
    gathered = jnp.stack(in_order)
    gathered = lax.all_gather(gathered, "z", axis=0, tiled=False)
    core = lax.axis_index("core")
    cores = lax.axis_size("core")
    twin = lax.ppermute(gathered, "core", [(0, 1), (1, 0)])
    mine_logits = jnp.einsum("zyrd,dv->yzrv", gathered, w_vocab, preferred_element_type=jnp.float32)
    twin_logits = jnp.einsum("zyrd,dv->yzrv", twin, w_vocab, preferred_element_type=jnp.float32)
    logits = jnp.zeros(
        mine_logits.shape[:2] + (cores,) + mine_logits.shape[2:], jnp.float32
    )
    logits = lax.dynamic_update_slice_in_dim(logits, mine_logits[:, :, None], core, 2)
    logits = lax.dynamic_update_slice_in_dim(logits, twin_logits[:, :, None], 1 - core, 2)
    return logits.reshape(-1, logits.shape[-1])


def solution(mesh):
    split = Mesh(mesh.devices.reshape((mesh.devices.shape[0],) + REQ_SPLIT), ("guide",) + REQ)
    in_specs = (
        P("guide", REQ, None),
        P(),
        P("guide", None),
        P("guide", None),
        P(),
        P(None, REQ),
        P("guide", REQ, None, None),
        P("guide", None),
        P("guide", None, None),
        P("guide", None, None),
    )
    out_specs = P("guide", REQ)
    return jax.shard_map(body, mesh=split, in_specs=in_specs, out_specs=out_specs, check_vma=False)
```
